32 devices in a mesh: shot: 4 (over y, core), mesh: 8 (over z, x).
Axes of the slice: x: 2, y: 2, z: 4, core: 2. Of those that a mesh axis runs over, the one named last changes fastest.
Arguments:
- adjoint_state: float32 [4, 13, 35, 1024], P('shot', None, None, 'mesh'), may hold values from -6 to 6
- forward_states: float32 [4, 2, 13, 35, 1024], P('shot', None, None, None, 'mesh'), may hold values from -6 to 6
- material: float32 [6, 35, 1024], P(None, None, 'mesh'), may hold values from 0.5 to 2
- coupling: float32 [3, 6, 13, 13], replicated, may hold values from -0.375 to 0.375
- metric: float32 [3, 3, 1024], P(None, None, 'mesh'), may hold values from -4 to 4
- face_normals: float32 [3, 4, 1024], P(None, None, 'mesh'), may hold values from -4 to 4
- face_scale: float32 [4, 1024], P(None, 'mesh'), may hold values from 1 to 3
- face_neighbours: int32 [4, 1024], P(None, 'mesh'), may hold values from 0 to 639, as said below
- face_orientation: int32 [4, 1024], P(None, 'mesh'), may hold values from 0 to 5
- send_faces: int32 [1024], P('mesh'), may hold values from 0 to 511, as said below
- history_steps: float32 [5, 6, 35, 1024], P(None, None, None, 'mesh')
- history_changes: float32 [5, 6, 35, 1024], P(None, None, None, 'mesh'), as said below
Outputs:
- adjoint_final: float32 [4, 13, 35, 1024], P('shot', None, None, 'mesh')
- direction: float32 [6, 35, 1024], P(None, None, ('mesh', 'shot'))
The draws below stay inside these ranges and needn't reach their ends.
Inputs may be any that keep to these rules, and one draw needn't show every extreme that they name: `face_neighbours`: local faces of a partition are numbered x * 128 + e. Each face either forms a pair with another local face (each names the other) or reads exactly one of the 128 ghost slots, and every ghost slot is read by exactly one face; on every partition the face that reads slot 512 + j is send_faces[j] and the face that reads slot 576 + j is send_faces[64 + j]. `send_faces`: the 128 entries of one partition are distinct local face numbers. `history_changes`: for every stored pair, s_i . y_i is positive.
All inputs are finite; a program needn't handle non-finite values.
Results may differ from the reference program's by a relative error of at most 0.0003.
Values sent between devices are 32-bit elements; how exact they have to be, the bound alone decides.
No kernel may reach another device: no remote copies, remote signals or barrier semaphores. Data moves between devices by JAX's collectives and lax.ppermute only.
A program may use at most 64 MiB of HBM per device.

```python
import math
import jax
import jax.numpy as jnp
import numpy as np
from jax import lax

NF = 13
NB = 35
NFN = 15
NM = 6
HIST = 5
STEPS = 2
E_DEV = 128
BFACE = 64
SHOTS = 4
ELEMS = 1024
N_MESH = 8


def face_tables(key):
    face_count = 4 * E_DEV
    border = E_DEV // 2

    def one_partition(part_key):
        shuffled = jax.random.permutation(part_key, face_count).astype(jnp.int32)
        position = jnp.arange(face_count, dtype=jnp.int32)
        partner = 2 * border + jnp.bitwise_xor(jnp.maximum(position - 2 * border, 0), 1)
        paired = shuffled[jnp.clip(partner, 0, face_count - 1)]
        ghost_slot = face_count + position
        slot_values = jnp.where(position < 2 * border, ghost_slot, paired)
        result_table = jnp.zeros((face_count,), jnp.int32).at[shuffled].set(slot_values)
        return (result_table.reshape(4, E_DEV), shuffled[:2 * border])
    part_keys = jax.random.split(key, N_MESH)
    tables, send_lists = jax.vmap(one_partition)(part_keys)
    return (tables.transpose(1, 0, 2).reshape(4, E_DEV * N_MESH), send_lists.reshape(-1))


def draw_face_neighbours(key, part):
    return face_tables(jax.random.fold_in(key, 17))[0]


def draw_send_faces(key, part):
    return face_tables(jax.random.fold_in(key, 17))[1]


def history_pair(key):
    total_elems = E_DEV * N_MESH
    array_shape = (HIST, NM, NB, total_elems)
    pair_keys = jax.random.split(key, 6)
    base_draw = jax.random.normal(pair_keys[0], array_shape, jnp.float32)
    row_scale = jnp.exp(jax.random.uniform(pair_keys[2], (HIST, NM, NB, 1), jnp.float32, 0.0, math.log(10.0)))
    column_scale = jnp.exp(jax.random.uniform(pair_keys[3], (1, 1, 1, total_elems), jnp.float32, 0.0, math.log(10.0)))
    position = jnp.arange(total_elems, dtype=jnp.float32) / (total_elems - 1)
    rising = jnp.sqrt(1.0 + 2.0 * position)
    step_draw = 0.3 * base_draw * row_scale * column_scale * rising
    curvature = jnp.exp(jax.random.uniform(pair_keys[4], (HIST, 1, 1, 1), jnp.float32, math.log(0.3), math.log(3.0)))
    ratio_draw = jax.random.uniform(pair_keys[5], array_shape, jnp.float32, 0.5, 2.0) * (1.0 + 2.0 * position)
    return (step_draw, step_draw * ratio_draw * curvature)


def draw_history_steps(key, part):
    return history_pair(jax.random.fold_in(key, 29))[0]


def draw_history_changes(key, part):
    return history_pair(jax.random.fold_in(key, 29))[1]


def touch_ends(values, stream_key, smallest, top_value):
    extent = values.shape
    place = [jax.random.randint(jax.random.fold_in(stream_key, axis), (), 0, extent[axis]) for axis in range(len(extent))]
    values = values.at[tuple(place)].set(smallest)
    longest = extent.index(max(extent))
    place[longest] = (place[longest] + 1) % extent[longest]
    return values.at[tuple(place)].set(top_value)


def shard_levels(own_key, extent, cuts, smallest, high):
    def one(dim, parts):
        steps = jax.random.uniform(jax.random.fold_in(jax.random.fold_in(own_key, 6), dim), (parts,), jnp.float32, smallest / len(cuts), high / len(cuts))
        return jnp.repeat(jnp.exp(steps), extent[dim] // parts).reshape((-1,) + (1,) * (len(extent) - dim - 1))

    level = one(*cuts[0])
    for cut in cuts[1:]:
        level = level * one(*cut)
    return level


def centred(rng, shape, spread, reach, cuts=(), kind=jnp.bfloat16):
    level = shard_levels(rng, shape, cuts, -0.22, 0.18) if cuts else 1.0
    values = jax.random.normal(rng, shape, jnp.float32) * spread * level
    return jnp.minimum(jnp.maximum(values, -reach), reach).astype(kind)


def setup_inputs(seed: int = 0) -> dict:
    key_of = jax.random.split(jax.random.key(seed), 13)
    return {
        "adjoint_state": centred(key_of[0], (SHOTS, NF, NB, ELEMS), 1.0, 6.0, ((0, 4), (3, 8)), jnp.float32),
        "forward_states": centred(key_of[1], (SHOTS, STEPS, NF, NB, ELEMS), 1.0, 6.0, ((0, 4), (4, 8)), jnp.float32),
        "material": jnp.clip(jnp.exp(math.log(2.0) - 1.3862944 * jax.random.uniform(key_of[2], (NM, NB, ELEMS), jnp.float32) ** shard_levels(key_of[2], (NM, NB, ELEMS), ((2, 8),), -0.2, 0.2)), 0.5, 2.0),
        "coupling": centred(key_of[3], (3, NM, NF, NF), (3 * NM * NF) ** -0.5, 0.375, (), jnp.float32),
        "metric": centred(key_of[4], (3, 3, ELEMS), 1.0, 4.0, ((2, 8),), jnp.float32),
        "face_normals": centred(key_of[5], (3, 4, ELEMS), 1.0, 4.0, ((2, 8),), jnp.float32),
        "face_scale": jnp.clip(jnp.exp(math.log(3.0) - 1.0986123 * jax.random.uniform(key_of[6], (4, ELEMS), jnp.float32) ** shard_levels(key_of[6], (4, ELEMS), ((1, 8),), -0.2, 0.2)), 1.0, 3.0),
        "face_neighbours": draw_face_neighbours(jax.random.fold_in(key_of[12], 71), 0),
        "face_orientation": touch_ends(jax.random.randint(key_of[8], (4, ELEMS), 0, 6), jax.random.fold_in(key_of[8], 1), 0, 5).astype(jnp.int32),
        "send_faces": draw_send_faces(jax.random.fold_in(key_of[12], 71), 0),
        "history_steps": draw_history_steps(jax.random.fold_in(key_of[12], 71), 0),
        "history_changes": draw_history_changes(jax.random.fold_in(key_of[12], 71), 0),
    }


HIGH = lax.Precision.HIGHEST
STEP_SIZE = 0.02


def invert_matrix(matrix):
    order_count = matrix.shape[0]
    working = np.concatenate([matrix * 1.0, np.eye(order_count)], axis=1)
    for column in range(order_count):
        pivot_row = column + int(np.argmax(np.abs(working[column:, column])))
        working[[column, pivot_row]] = working[[pivot_row, column]]
        working[column] = working[column] / working[column, column]
        for target in range(order_count):
            if target != column:
                working[target] = working[target] - working[target, column] * working[column]
    return working[:, order_count:]


def basis_tables():
    points = [(across, along, upward) for upward in range(5) for along in range(5 - upward) for across in range(5 - upward - along)]
    exponents = np.array(points) * 1.0
    coords = exponents / 4.0
    vander = np.prod(coords[:, None, :] ** exponents[None, :, :], axis=2)
    inverse = invert_matrix(vander)
    derivs = []
    for direction_axis in range(3):
        lowered = np.maximum(exponents - np.eye(3)[direction_axis], 0.0)
        slopes = exponents[None, :, direction_axis] * np.prod(coords[:, None, :] ** lowered[None, :, :], axis=2)
        derivs.append(slopes @ inverse)
    moments = np.array([[math.factorial(first[0] + second[0]) * math.factorial(first[1] + second[1]) * math.factorial(first[2] + second[2]) / math.factorial(sum(first) + sum(second) + 3) for second in points] for first in points])
    mass_matrix = inverse.T @ moments @ inverse
    lattice = [(across, along) for along in range(5) for across in range(5 - along)]
    lattice_powers = np.array(lattice) * 1.0
    face_vander = np.prod((lattice_powers / 4.0)[:, None, :] ** lattice_powers[None, :, :], axis=2)
    face_inverse = invert_matrix(face_vander)
    face_moments = np.array([[math.factorial(first[0] + second[0]) * math.factorial(first[1] + second[1]) / math.factorial(sum(first) + sum(second) + 2) for second in lattice] for first in lattice])
    face_mass = face_inverse.T @ face_moments @ face_inverse
    numbers = {point: number for number, point in enumerate(points)}
    face_points = [
        [(across, along, 0) for across, along in lattice],
        [(across, 0, along) for across, along in lattice],
        [(0, across, along) for across, along in lattice],
        [(across, along, 4 - across - along) for across, along in lattice]]
    face_nodes = np.array([[numbers[point] for point in listing] for listing in face_points], np.int32)
    mass_inverse = invert_matrix(mass_matrix)
    lift_tables = []
    for face_number in range(4):
        selector = np.eye(35)[face_nodes[face_number]]
        lift_tables.append(mass_inverse @ selector.T @ face_mass)
    orderings = [(0, 1, 2), (1, 2, 0), (2, 0, 1), (1, 0, 2), (0, 2, 1), (2, 1, 0)]
    lattice_numbers = {point: number for number, point in enumerate(lattice)}
    triples = [(across, along, 4 - across - along) for across, along in lattice]
    turn_nodes = np.array([[lattice_numbers[(triple[ordering[0]], triple[ordering[1]])] for triple in triples] for ordering in orderings], np.int32)
    return (jnp.asarray(np.stack(derivs), jnp.float32), jnp.asarray(np.stack(lift_tables), jnp.float32), face_nodes, turn_nodes)


def volume_term(adjoint, material, coupling, metric, derivs):
    reference_grads = jnp.einsum("rab,fbe->rfae", derivs, adjoint, precision=HIGH)
    spatial = jnp.einsum("rde,rfae->dfae", metric, reference_grads, precision=HIGH)
    mixing = jnp.einsum("dpfg,dfae->pgae", coupling, spatial, precision=HIGH)
    return jnp.sum(material[:, None] * mixing, axis=0)


def kernel_term(adjoint, forward, coupling, metric, derivs):
    reference_grads = jnp.einsum("rab,fbe->rfae", derivs, forward, precision=HIGH)
    spatial = jnp.einsum("rde,rfae->dfae", metric, reference_grads, precision=HIGH)
    mixing = jnp.einsum("dpfg,dgae->pfae", coupling, spatial, precision=HIGH)
    return jnp.sum(mixing * adjoint[None], axis=1)


def surface_term(jump_trace, face_material, face_normals, face_scale, coupling, lift_tables):
    weighted = face_normals[:, None, None] * jump_trace[None]
    mixing = jnp.einsum("dpfg,dfnxe->pgnxe", coupling, weighted, precision=HIGH)
    face_flux = 0.5 * jnp.sum(face_material[:, None] * mixing, axis=0) + 0.5 * jump_trace
    return jnp.einsum("xan,fnxe->fae", lift_tables, face_flux * face_scale[None, None], precision=HIGH)


def two_loop(total_grad, history_steps, history_changes):
    curvature = [jnp.sum(history_steps[slot] * history_changes[slot]) for slot in range(HIST)]
    alphas = [None] * HIST
    work = total_grad
    for slot in reversed(range(HIST)):
        alphas[slot] = jnp.sum(history_steps[slot] * work) / curvature[slot]
        work = work - alphas[slot] * history_changes[slot]
    scaling = curvature[HIST - 1] / jnp.sum(history_changes[HIST - 1] * history_changes[HIST - 1])
    work = scaling * work
    for slot in range(HIST):
        beta_now = jnp.sum(history_changes[slot] * work) / curvature[slot]
        work = work + (alphas[slot] - beta_now) * history_steps[slot]
    return -work


def reference(adjoint_state, forward_states, material, coupling, metric, face_normals, face_scale, face_neighbours, face_orientation, send_faces, history_steps, history_changes):
    derivs, lift_tables, face_nodes, turn_nodes = basis_tables()
    face_material = material[:, face_nodes.T, :]
    neighbours = face_neighbours.reshape(4, N_MESH, E_DEV).transpose(1, 0, 2).reshape(N_MESH, 4 * E_DEV)
    orient = face_orientation.reshape(4, N_MESH, E_DEV).transpose(1, 0, 2).reshape(N_MESH, 4 * E_DEV)
    sends = send_faces.reshape(N_MESH, 2 * BFACE)

    def outer_traces(inner_trace):
        partitioned = inner_trace.reshape(NF, NFN, 4, N_MESH, E_DEV).transpose(3, 0, 1, 2, 4).reshape(N_MESH, NF, NFN, 4 * E_DEV)
        sent_traces = jax.vmap(lambda traces, listing: traces[:, :, listing])(partitioned, sends)
        empty = jnp.zeros((1, NF, NFN, BFACE), jnp.float32)
        from_below = jnp.concatenate([empty, sent_traces[:-1, :, :, BFACE:]], axis=0)
        from_above = jnp.concatenate([sent_traces[1:, :, :, :BFACE], empty], axis=0)
        extended = jnp.concatenate([partitioned, from_below, from_above], axis=3)
        gathered = jax.vmap(lambda traces, listing: traces[:, :, listing])(extended, neighbours)
        turned = gathered
        for option in range(6):
            turned = jnp.where((orient == option)[:, None, None, :], gathered[:, :, turn_nodes[option], :], turned)
        return turned.reshape(N_MESH, NF, NFN, 4, E_DEV).transpose(1, 2, 3, 0, 4).reshape(NF, NFN, 4, ELEMS)

    def one_shot(operands):
        adjoint, forwards = operands
        gradient = jnp.zeros((NM, NB, ELEMS), jnp.float32)
        for step_index in range(STEPS):
            inner_trace = adjoint[:, face_nodes.T, :]
            jump_trace = outer_traces(inner_trace) - inner_trace
            change = volume_term(adjoint, material, coupling, metric, derivs) + surface_term(jump_trace, face_material, face_normals, face_scale, coupling, lift_tables)
            adjoint = adjoint + STEP_SIZE * change
            gradient = gradient + STEP_SIZE * kernel_term(adjoint, forwards[step_index], coupling, metric, derivs)
        return adjoint, gradient

    finals, gradients = lax.map(one_shot, (adjoint_state, forward_states))
    total_grad = jnp.sum(gradients, axis=0)
    return finals, two_loop(total_grad, history_steps, history_changes)
```

```python
import math

import jax
import jax.numpy as jnp
import numpy as np
from jax import lax
from jax.sharding import PartitionSpec as P

HIGH = lax.Precision.HIGHEST
STEP_SIZE = 0.02


def padded(x, sides, width):
    for axis, dim in sides:
        devices, length = (lax.axis_size(axis), x.shape[dim])
        up = [(i, (i + 1) % devices) for i in range(devices - 1)]
        down = [(j, i) for i, j in up]
        last = lax.slice_in_dim(x, length - width, length, axis=dim)
        first = lax.slice_in_dim(x, 0, width, axis=dim)
        before = lax.ppermute(last, axis, up)
        after = lax.ppermute(first, axis, down)
        x = jnp.concatenate([before, x, after], axis=dim)
    return x


def invert_matrix(matrix):
    order_count = matrix.shape[0]
    working = np.concatenate([matrix * 1.0, np.eye(order_count)], axis=1)
    for column in range(order_count):
        pivot_row = column + int(np.argmax(np.abs(working[column:, column])))
        working[[column, pivot_row]] = working[[pivot_row, column]]
        working[column] = working[column] / working[column, column]
        for target in range(order_count):
            if target != column:
                working[target] = working[target] - working[target, column] * working[column]
    return working[:, order_count:]


def basis_tables():
    points = [
        (across, along, upward)
        for upward in range(5)
        for along in range(5 - upward)
        for across in range(5 - upward - along)
    ]
    exponents = np.array(points) * 1.0
    coords = exponents / 4.0
    vander = np.prod(coords[:, None, :] ** exponents[None, :, :], axis=2)
    inverse = invert_matrix(vander)
    derivs = []
    for direction_axis in range(3):
        lowered = np.maximum(exponents - np.eye(3)[direction_axis], 0.0)
        slopes = exponents[None, :, direction_axis] * np.prod(
            coords[:, None, :] ** lowered[None, :, :], axis=2
        )
        derivs.append(slopes @ inverse)
    moments = np.array(
        [
            [
                math.factorial(first[0] + second[0])
                * math.factorial(first[1] + second[1])
                * math.factorial(first[2] + second[2])
                / math.factorial(sum(first) + sum(second) + 3)
                for second in points
            ]
            for first in points
        ]
    )
    mass_matrix = inverse.T @ moments @ inverse
    lattice = [(across, along) for along in range(5) for across in range(5 - along)]
    lattice_powers = np.array(lattice) * 1.0
    face_vander = np.prod((lattice_powers / 4.0)[:, None, :] ** lattice_powers[None, :, :], axis=2)
    face_inverse = invert_matrix(face_vander)
    face_moments = np.array(
        [
            [
                math.factorial(first[0] + second[0])
                * math.factorial(first[1] + second[1])
                / math.factorial(sum(first) + sum(second) + 2)
                for second in lattice
            ]
            for first in lattice
        ]
    )
    face_mass = face_inverse.T @ face_moments @ face_inverse
    numbers = {point: number for number, point in enumerate(points)}
    face_points = [
        [(across, along, 0) for across, along in lattice],
        [(across, 0, along) for across, along in lattice],
        [(0, across, along) for across, along in lattice],
        [(across, along, 4 - across - along) for across, along in lattice],
    ]
    face_nodes = np.array(
        [[numbers[point] for point in listing] for listing in face_points], np.int32
    )
    mass_inverse = invert_matrix(mass_matrix)
    lift_tables = []
    for face_number in range(4):
        selector = np.eye(35)[face_nodes[face_number]]
        lift_tables.append(mass_inverse @ selector.T @ face_mass)
    orderings = [(0, 1, 2), (1, 2, 0), (2, 0, 1), (1, 0, 2), (0, 2, 1), (2, 1, 0)]
    lattice_numbers = {point: number for number, point in enumerate(lattice)}
    triples = [(across, along, 4 - across - along) for across, along in lattice]
    turn_nodes = np.array(
        [
            [lattice_numbers[triple[ordering[0]], triple[ordering[1]]] for triple in triples]
            for ordering in orderings
        ],
        np.int32,
    )
    return (
        jnp.asarray(np.stack(derivs), jnp.float32),
        jnp.asarray(np.stack(lift_tables), jnp.float32),
        face_nodes,
        turn_nodes,
    )


def spatial_of(field, metric, derivs):
    reference_grads = jnp.einsum("rab,fbe->rfae", derivs, field, precision=HIGH)
    rows = []
    for direction_axis in range(3):
        total = metric[0, direction_axis] * reference_grads[0]
        total = total + metric[1, direction_axis] * reference_grads[1]
        total = total + metric[2, direction_axis] * reference_grads[2]
        rows.append(total)
    return jnp.stack(rows)


def volume_term(adjoint, material, coupling, metric, derivs):
    spatial = spatial_of(adjoint, metric, derivs)
    mixing = jnp.einsum("dpfg,dfae->pgae", coupling, spatial, precision=HIGH)
    return jnp.sum(material[:, None] * mixing, axis=0)


def kernel_term(adjoint, forward, coupling, metric, derivs):
    spatial = spatial_of(forward, metric, derivs)
    mixing = jnp.einsum("dpfg,dgae->pfae", coupling, spatial, precision=HIGH)
    return jnp.sum(mixing * adjoint[None], axis=1)


def surface_term(jump_trace, face_material, face_normals, face_scale, coupling, lift_tables):
    weighted = face_normals[:, None, None] * jump_trace[None]
    mixing = jnp.einsum("dpfg,dfnxe->pgnxe", coupling, weighted, precision=HIGH)
    face_flux = 0.5 * jnp.sum(face_material[:, None] * mixing, axis=0) + 0.5 * jump_trace
    return jnp.einsum(
        "xan,fnxe->fae", lift_tables, face_flux * face_scale[None, None], precision=HIGH
    )


def search_direction(grad_share, local_grad, step_rows, change_rows, own_share, combine_sums):
    pairs = step_rows.shape[0]
    step_share = own_share(step_rows)
    change_share = own_share(change_rows)
    step_grad = jnp.sum(step_rows * local_grad[None], axis=(1, 2, 3))
    change_grad = jnp.sum(change_rows * local_grad[None], axis=(1, 2, 3))
    step_change = jnp.sum(step_share[:, None] * change_share[None, :], axis=(2, 3, 4))
    change_change = jnp.sum(change_share[:, None] * change_share[None, :], axis=(2, 3, 4))
    summed = combine_sums(
        jnp.concatenate(
            [step_grad, change_grad, step_change.reshape(-1), change_change.reshape(-1)]
        )
    )
    step_grad = summed[:pairs]
    change_grad = summed[pairs : 2 * pairs]
    step_change = summed[2 * pairs : 2 * pairs + pairs * pairs].reshape(pairs, pairs)
    change_change = summed[2 * pairs + pairs * pairs :].reshape(pairs, pairs)
    curvature = [step_change[slot, slot] for slot in range(pairs)]
    alphas = [None] * pairs
    for slot in reversed(range(pairs)):
        projected = step_grad[slot]
        for later in range(slot + 1, pairs):
            projected = projected - alphas[later] * step_change[slot, later]
        alphas[slot] = projected / curvature[slot]
    scaling = curvature[pairs - 1] / change_change[pairs - 1, pairs - 1]
    weights = [None] * pairs
    for slot in range(pairs):
        along = change_grad[slot]
        for other in range(pairs):
            along = along - alphas[other] * change_change[slot, other]
        along = scaling * along
        for earlier in range(slot):
            along = along + weights[earlier] * step_change[earlier, slot]
        beta_now = along / curvature[slot]
        weights[slot] = alphas[slot] - beta_now
    work = scaling * grad_share
    for slot in range(pairs):
        work = work - (scaling * alphas[slot]) * change_share[slot]
    for slot in range(pairs):
        work = work + weights[slot] * step_share[slot]
    return -work


def shards(
    adjoint_state,
    forward_states,
    material,
    coupling,
    metric,
    face_normals,
    face_scale,
    face_neighbours,
    face_orientation,
    send_faces,
    history_steps,
    history_changes,
):
    derivs, lift_tables, face_nodes, turn_nodes = basis_tables()
    fields = adjoint_state.shape[1]
    elements = adjoint_state.shape[3]
    node_count = material.shape[1]
    params = material.shape[0]
    face_width = face_nodes.shape[1]
    border = send_faces.shape[0] // 2
    slot_count = 4 * elements + 2 * border
    adjoint = adjoint_state[0]
    face_material = material[:, face_nodes.T, :]
    neighbours = face_neighbours.reshape(-1)
    orient = face_orientation.reshape(-1)
    node_pick = jnp.zeros((face_width, 4 * elements), jnp.int32)
    for option in range(turn_nodes.shape[0]):
        node_pick = (
            node_pick
            + (orient == option).astype(jnp.int32)[None, :]
            * jnp.asarray(turn_nodes[option], jnp.int32)[:, None]
        )
    flat_index = (node_pick * slot_count + neighbours[None, :]).reshape(-1)
    gradient = jnp.zeros((params, node_count, elements), jnp.float32)
    for step_index in range(forward_states.shape[1]):
        inner_trace = adjoint[:, face_nodes.T, :]
        flat_trace = inner_trace.reshape(fields, face_width, 4 * elements)
        sent_traces = flat_trace[:, :, send_faces]
        extended = padded(sent_traces, (("mesh", 2),), border)
        ghosts = jnp.concatenate(
            [flat_trace, extended[:, :, :border], extended[:, :, 3 * border :]], axis=2
        )
        turned = ghosts.reshape(fields, face_width * slot_count)[:, flat_index]
        jump_trace = turned.reshape(fields, face_width, 4, elements) - inner_trace
        change = volume_term(adjoint, material, coupling, metric, derivs) + surface_term(
            jump_trace, face_material, face_normals, face_scale, coupling, lift_tables
        )
        adjoint = adjoint + STEP_SIZE * change
        gradient = gradient + STEP_SIZE * kernel_term(
            adjoint, forward_states[0, step_index], coupling, metric, derivs
        )
    shot_count = lax.axis_size("shot")
    share_width = elements // shot_count
    share_start = lax.axis_index("shot") * share_width

    def own_share(rows):
        return lax.dynamic_slice_in_dim(rows, share_start, share_width, rows.ndim - 1)

    def combine_sums(values):
        return lax.psum(values, ("shot", "mesh"))

    grad_share = lax.psum_scatter(gradient, "shot", scatter_dimension=2, tiled=True)
    result = search_direction(
        grad_share, gradient, history_steps, history_changes, own_share, combine_sums
    )
    return (adjoint[None], result)


def solution(mesh):
    placed = (
        P("shot", None, None, "mesh"),
        P("shot", None, None, None, "mesh"),
        P(None, None, "mesh"),
        P(),
        P(None, None, "mesh"),
        P(None, None, "mesh"),
        P(None, "mesh"),
        P(None, "mesh"),
        P(None, "mesh"),
        P("mesh"),
        P(None, None, None, "mesh"),
        P(None, None, None, "mesh"),
    )
    return jax.shard_map(
        shards,
        mesh=mesh,
        in_specs=placed,
        out_specs=(P("shot", None, None, "mesh"), P(None, None, ("mesh", "shot"))),
        check_vma=False,
    )
```

```python
import math

import jax
import jax.numpy as jnp
import numpy as np
from jax import lax
from jax.sharding import PartitionSpec as P

HIGH = lax.Precision.HIGHEST
STEP_SIZE = 0.02


def padded(x, sides, width):
    for axis, dim in sides:
        devices, length = (lax.axis_size(axis), x.shape[dim])
        up = [(i, (i + 1) % devices) for i in range(devices - 1)]
        down = [(j, i) for i, j in up]
        last = lax.slice_in_dim(x, length - width, length, axis=dim)
        first = lax.slice_in_dim(x, 0, width, axis=dim)
        before = lax.ppermute(last, axis, up)
        after = lax.ppermute(first, axis, down)
        x = jnp.concatenate([before, x, after], axis=dim)
    return x


def invert_matrix(matrix):
    order_count = matrix.shape[0]
    working = np.concatenate([matrix * 1.0, np.eye(order_count)], axis=1)
    for column in range(order_count):
        pivot_row = column + int(np.argmax(np.abs(working[column:, column])))
        working[[column, pivot_row]] = working[[pivot_row, column]]
        working[column] = working[column] / working[column, column]
        for target in range(order_count):
            if target != column:
                working[target] = working[target] - working[target, column] * working[column]
    return working[:, order_count:]


def basis_tables():
    points = [
        (across, along, upward)
        for upward in range(5)
        for along in range(5 - upward)
        for across in range(5 - upward - along)
    ]
    exponents = np.array(points) * 1.0
    coords = exponents / 4.0
    vander = np.prod(coords[:, None, :] ** exponents[None, :, :], axis=2)
    inverse = invert_matrix(vander)
    derivs = []
    for direction_axis in range(3):
        lowered = np.maximum(exponents - np.eye(3)[direction_axis], 0.0)
        slopes = exponents[None, :, direction_axis] * np.prod(
            coords[:, None, :] ** lowered[None, :, :], axis=2
        )
        derivs.append(slopes @ inverse)
    moments = np.array(
        [
            [
                math.factorial(first[0] + second[0])
                * math.factorial(first[1] + second[1])
                * math.factorial(first[2] + second[2])
                / math.factorial(sum(first) + sum(second) + 3)
                for second in points
            ]
            for first in points
        ]
    )
    mass_matrix = inverse.T @ moments @ inverse
    lattice = [(across, along) for along in range(5) for across in range(5 - along)]
    lattice_powers = np.array(lattice) * 1.0
    face_vander = np.prod((lattice_powers / 4.0)[:, None, :] ** lattice_powers[None, :, :], axis=2)
    face_inverse = invert_matrix(face_vander)
    face_moments = np.array(
        [
            [
                math.factorial(first[0] + second[0])
                * math.factorial(first[1] + second[1])
                / math.factorial(sum(first) + sum(second) + 2)
                for second in lattice
            ]
            for first in lattice
        ]
    )
    face_mass = face_inverse.T @ face_moments @ face_inverse
    numbers = {point: number for number, point in enumerate(points)}
    face_points = [
        [(across, along, 0) for across, along in lattice],
        [(across, 0, along) for across, along in lattice],
        [(0, across, along) for across, along in lattice],
        [(across, along, 4 - across - along) for across, along in lattice],
    ]
    face_nodes = np.array(
        [[numbers[point] for point in listing] for listing in face_points], np.int32
    )
    mass_inverse = invert_matrix(mass_matrix)
    lift_tables = []
    for face_number in range(4):
        selector = np.eye(35)[face_nodes[face_number]]
        lift_tables.append(mass_inverse @ selector.T @ face_mass)
    orderings = [(0, 1, 2), (1, 2, 0), (2, 0, 1), (1, 0, 2), (0, 2, 1), (2, 1, 0)]
    lattice_numbers = {point: number for number, point in enumerate(lattice)}
    triples = [(across, along, 4 - across - along) for across, along in lattice]
    turn_nodes = np.array(
        [
            [lattice_numbers[triple[ordering[0]], triple[ordering[1]]] for triple in triples]
            for ordering in orderings
        ],
        np.int32,
    )
    return (
        jnp.asarray(np.stack(derivs), jnp.float32),
        jnp.asarray(np.stack(lift_tables), jnp.float32),
        face_nodes,
        turn_nodes,
    )


def spatial_of(field, metric, derivs):
    reference_grads = jnp.einsum("rab,fbe->rfae", derivs, field, precision=HIGH)
    rows = []
    for direction_axis in range(3):
        total = metric[0, direction_axis] * reference_grads[0]
        total = total + metric[1, direction_axis] * reference_grads[1]
        total = total + metric[2, direction_axis] * reference_grads[2]
        rows.append(total)
    return jnp.stack(rows)


def volume_term(adjoint, material, coupling, metric, derivs):
    spatial = spatial_of(adjoint, metric, derivs)
    mixing = jnp.einsum("dpfg,dfae->pgae", coupling, spatial, precision=HIGH)
    return jnp.sum(material[:, None] * mixing, axis=0)


def kernel_term(adjoint, forward, coupling, metric, derivs):
    spatial = spatial_of(forward, metric, derivs)
    mixing = jnp.einsum("dpfg,dgae->pfae", coupling, spatial, precision=HIGH)
    return jnp.sum(mixing * adjoint[None], axis=1)


def surface_term(jump_trace, face_material, face_normals, face_scale, coupling, lift_tables):
    weighted = face_normals[:, None, None] * jump_trace[None]
    mixing = jnp.einsum("dpfg,dfnxe->pgnxe", coupling, weighted, precision=HIGH)
    face_flux = 0.5 * jnp.sum(face_material[:, None] * mixing, axis=0) + 0.5 * jump_trace
    return jnp.einsum(
        "xan,fnxe->fae", lift_tables, face_flux * face_scale[None, None], precision=HIGH
    )


def search_direction(grad_share, local_grad, step_rows, change_rows, own_share, keep_gram, combine_sums):
    pairs = step_rows.shape[0]
    step_flat = step_rows.reshape(pairs, -1)
    change_flat = change_rows.reshape(pairs, -1)
    both_flat = jnp.concatenate([step_flat, change_flat], axis=0)
    with_grad = jnp.dot(both_flat, local_grad.reshape(-1), precision=HIGH)
    gram = jnp.dot(both_flat, change_flat.T, precision=HIGH) * keep_gram
    summed = combine_sums(jnp.concatenate([with_grad, gram.reshape(-1)]))
    step_grad = summed[:pairs]
    change_grad = summed[pairs : 2 * pairs]
    gram = summed[2 * pairs :].reshape(2 * pairs, pairs)
    step_change = gram[:pairs]
    change_change = gram[pairs:]
    curvature = [step_change[slot, slot] for slot in range(pairs)]
    alphas = [None] * pairs
    for slot in reversed(range(pairs)):
        projected = step_grad[slot]
        for later in range(slot + 1, pairs):
            projected = projected - alphas[later] * step_change[slot, later]
        alphas[slot] = projected / curvature[slot]
    scaling = curvature[pairs - 1] / change_change[pairs - 1, pairs - 1]
    weights = [None] * pairs
    for slot in range(pairs):
        along = change_grad[slot]
        for other in range(pairs):
            along = along - alphas[other] * change_change[slot, other]
        along = scaling * along
        for earlier in range(slot):
            along = along + weights[earlier] * step_change[earlier, slot]
        beta_now = along / curvature[slot]
        weights[slot] = alphas[slot] - beta_now
    step_share = own_share(step_rows)
    change_share = own_share(change_rows)
    work = scaling * grad_share
    for slot in range(pairs):
        work = work - (scaling * alphas[slot]) * change_share[slot]
    for slot in range(pairs):
        work = work + weights[slot] * step_share[slot]
    return -work


def shards(
    adjoint_state,
    forward_states,
    material,
    coupling,
    metric,
    face_normals,
    face_scale,
    face_neighbours,
    face_orientation,
    send_faces,
    history_steps,
    history_changes,
):
    derivs, lift_tables, face_nodes, turn_nodes = basis_tables()
    fields = adjoint_state.shape[1]
    elements = adjoint_state.shape[3]
    node_count = material.shape[1]
    params = material.shape[0]
    face_width = face_nodes.shape[1]
    border = send_faces.shape[0] // 2
    slot_count = 4 * elements + 2 * border
    adjoint = adjoint_state[0]
    face_material = material[:, face_nodes.T, :]
    neighbours = face_neighbours.reshape(-1)
    orient = face_orientation.reshape(-1)
    node_pick = jnp.zeros((face_width, 4 * elements), jnp.int32)
    for option in range(turn_nodes.shape[0]):
        node_pick = (
            node_pick
            + (orient == option).astype(jnp.int32)[None, :]
            * jnp.asarray(turn_nodes[option], jnp.int32)[:, None]
        )
    flat_index = (node_pick * slot_count + neighbours[None, :]).reshape(-1)
    gradient = jnp.zeros((params, node_count, elements), jnp.float32)
    for step_index in range(forward_states.shape[1]):
        inner_trace = adjoint[:, face_nodes.T, :]
        flat_trace = inner_trace.reshape(fields, face_width, 4 * elements)
        sent_traces = flat_trace[:, :, send_faces]
        extended = padded(sent_traces, (("mesh", 2),), border)
        ghosts = jnp.concatenate(
            [flat_trace, extended[:, :, :border], extended[:, :, 3 * border :]], axis=2
        )
        turned = ghosts.reshape(fields, face_width * slot_count)[:, flat_index]
        jump_trace = turned.reshape(fields, face_width, 4, elements) - inner_trace
        change = volume_term(adjoint, material, coupling, metric, derivs) + surface_term(
            jump_trace, face_material, face_normals, face_scale, coupling, lift_tables
        )
        adjoint = adjoint + STEP_SIZE * change
        gradient = gradient + STEP_SIZE * kernel_term(
            adjoint, forward_states[0, step_index], coupling, metric, derivs
        )
    shot_count = lax.axis_size("shot")
    share_width = elements // shot_count
    share_start = lax.axis_index("shot") * share_width

    def own_share(rows):
        return lax.dynamic_slice_in_dim(rows, share_start, share_width, rows.ndim - 1)

    device_count = shot_count * lax.axis_size("mesh")

    def combine_sums(values):
        spread = jnp.broadcast_to(values[None], (device_count,) + values.shape)
        return jnp.sum(lax.all_to_all(spread, ("shot", "mesh"), 0, 0, tiled=False), axis=0)

    pieces = gradient.reshape(params, node_count, shot_count, share_width)
    grad_share = jnp.sum(lax.all_to_all(pieces, "shot", 2, 2, tiled=False), axis=2)
    keep_gram = (lax.axis_index("shot") == 0).astype(jnp.float32)
    result = search_direction(
        grad_share, gradient, history_steps, history_changes, own_share, keep_gram, combine_sums
    )
    return (adjoint[None], result)


def solution(mesh):
    placed = (
        P("shot", None, None, "mesh"),
        P("shot", None, None, None, "mesh"),
        P(None, None, "mesh"),
        P(),
        P(None, None, "mesh"),
        P(None, None, "mesh"),
        P(None, "mesh"),
        P(None, "mesh"),
        P(None, "mesh"),
        P("mesh"),
        P(None, None, None, "mesh"),
        P(None, None, None, "mesh"),
    )
    return jax.shard_map(
        shards,
        mesh=mesh,
        in_specs=placed,
        out_specs=(P("shot", None, None, "mesh"), P(None, None, ("mesh", "shot"))),
        check_vma=False,
    )
```

```python
import math

import jax
import jax.numpy as jnp
import numpy as np
from jax import lax
from jax.sharding import PartitionSpec as P

HIGH = lax.Precision.HIGHEST
STEP_SIZE = 0.02


def padded(x, sides, width):
    for axis, dim in sides:
        devices, length = (lax.axis_size(axis), x.shape[dim])
        up = [(i, (i + 1) % devices) for i in range(devices - 1)]
        down = [(j, i) for i, j in up]
        last = lax.slice_in_dim(x, length - width, length, axis=dim)
        first = lax.slice_in_dim(x, 0, width, axis=dim)
        before = lax.ppermute(last, axis, up)
        after = lax.ppermute(first, axis, down)
        x = jnp.concatenate([before, x, after], axis=dim)
    return x


def invert_matrix(matrix):
    order_count = matrix.shape[0]
    working = np.concatenate([matrix * 1.0, np.eye(order_count)], axis=1)
    for column in range(order_count):
        pivot_row = column + int(np.argmax(np.abs(working[column:, column])))
        working[[column, pivot_row]] = working[[pivot_row, column]]
        working[column] = working[column] / working[column, column]
        for target in range(order_count):
            if target != column:
                working[target] = working[target] - working[target, column] * working[column]
    return working[:, order_count:]


def basis_tables():
    points = [
        (across, along, upward)
        for upward in range(5)
        for along in range(5 - upward)
        for across in range(5 - upward - along)
    ]
    exponents = np.array(points) * 1.0
    coords = exponents / 4.0
    vander = np.prod(coords[:, None, :] ** exponents[None, :, :], axis=2)
    inverse = invert_matrix(vander)
    derivs = []
    for direction_axis in range(3):
        lowered = np.maximum(exponents - np.eye(3)[direction_axis], 0.0)
        slopes = exponents[None, :, direction_axis] * np.prod(
            coords[:, None, :] ** lowered[None, :, :], axis=2
        )
        derivs.append(slopes @ inverse)
    moments = np.array(
        [
            [
                math.factorial(first[0] + second[0])
                * math.factorial(first[1] + second[1])
                * math.factorial(first[2] + second[2])
                / math.factorial(sum(first) + sum(second) + 3)
                for second in points
            ]
            for first in points
        ]
    )
    mass_matrix = inverse.T @ moments @ inverse
    lattice = [(across, along) for along in range(5) for across in range(5 - along)]
    lattice_powers = np.array(lattice) * 1.0
    face_vander = np.prod((lattice_powers / 4.0)[:, None, :] ** lattice_powers[None, :, :], axis=2)
    face_inverse = invert_matrix(face_vander)
    face_moments = np.array(
        [
            [
                math.factorial(first[0] + second[0])
                * math.factorial(first[1] + second[1])
                / math.factorial(sum(first) + sum(second) + 2)
                for second in lattice
            ]
            for first in lattice
        ]
    )
    face_mass = face_inverse.T @ face_moments @ face_inverse
    numbers = {point: number for number, point in enumerate(points)}
    face_points = [
        [(across, along, 0) for across, along in lattice],
        [(across, 0, along) for across, along in lattice],
        [(0, across, along) for across, along in lattice],
        [(across, along, 4 - across - along) for across, along in lattice],
    ]
    face_nodes = np.array(
        [[numbers[point] for point in listing] for listing in face_points], np.int32
    )
    mass_inverse = invert_matrix(mass_matrix)
    lift_tables = []
    for face_number in range(4):
        selector = np.eye(35)[face_nodes[face_number]]
        lift_tables.append(mass_inverse @ selector.T @ face_mass)
    orderings = [(0, 1, 2), (1, 2, 0), (2, 0, 1), (1, 0, 2), (0, 2, 1), (2, 1, 0)]
    lattice_numbers = {point: number for number, point in enumerate(lattice)}
    triples = [(across, along, 4 - across - along) for across, along in lattice]
    turn_nodes = np.array(
        [
            [lattice_numbers[triple[ordering[0]], triple[ordering[1]]] for triple in triples]
            for ordering in orderings
        ],
        np.int32,
    )
    return (
        jnp.asarray(np.stack(derivs), jnp.float32),
        jnp.asarray(np.stack(lift_tables), jnp.float32),
        face_nodes,
        turn_nodes,
    )


def spatial_of(field, metric, derivs):
    reference_grads = jnp.einsum("rab,fbe->rfae", derivs, field, precision=HIGH)
    rows = []
    for direction_axis in range(3):
        total = metric[0, direction_axis] * reference_grads[0]
        total = total + metric[1, direction_axis] * reference_grads[1]
        total = total + metric[2, direction_axis] * reference_grads[2]
        rows.append(total)
    return jnp.stack(rows)


def volume_term(adjoint, material, coupling, metric, derivs):
    spatial = spatial_of(adjoint, metric, derivs)
    mixing = jnp.einsum("dpfg,dfae->pgae", coupling, spatial, precision=HIGH)
    return jnp.sum(material[:, None] * mixing, axis=0)


def kernel_term(adjoint, forward, coupling, metric, derivs):
    spatial = spatial_of(forward, metric, derivs)
    mixing = jnp.einsum("dpfg,dgae->pfae", coupling, spatial, precision=HIGH)
    return jnp.sum(mixing * adjoint[None], axis=1)


def surface_term(jump_trace, face_material, face_normals, face_scale, coupling, lift_tables):
    weighted = face_normals[:, None, None] * jump_trace[None]
    mixing = jnp.einsum("dpfg,dfnxe->pgnxe", coupling, weighted, precision=HIGH)
    face_flux = 0.5 * jnp.sum(face_material[:, None] * mixing, axis=0) + 0.5 * jump_trace
    return jnp.einsum(
        "xan,fnxe->fae", lift_tables, face_flux * face_scale[None, None], precision=HIGH
    )


def halving_sum(values, axis, count):
    position = lax.axis_index(axis)
    work = values
    bit = count // 2
    while bit >= 1:
        width = work.shape[-1] // 2
        upper = (position & bit) != 0
        low = work[..., :width]
        high = work[..., width:]
        sent = lax.ppermute(
            jnp.where(upper, low, high), axis, [(i, i ^ bit) for i in range(count)]
        )
        work = jnp.where(upper, high, low) + sent
        bit //= 2
    return work


def search_direction(grad_share, local_grad, step_rows, change_rows, own_share, keep_gram, combine_sums):
    pairs = step_rows.shape[0]
    step_flat = step_rows.reshape(pairs, -1)
    change_flat = change_rows.reshape(pairs, -1)
    both_flat = jnp.concatenate([step_flat, change_flat], axis=0)
    with_grad = jnp.dot(both_flat, local_grad.reshape(-1), precision=HIGH)
    gram = jnp.dot(both_flat, change_flat.T, precision=HIGH) * keep_gram
    summed = combine_sums(jnp.concatenate([with_grad, gram.reshape(-1)]))
    step_grad = summed[:pairs]
    change_grad = summed[pairs : 2 * pairs]
    gram = summed[2 * pairs :].reshape(2 * pairs, pairs)
    step_change = gram[:pairs]
    change_change = gram[pairs:]
    curvature = [step_change[slot, slot] for slot in range(pairs)]
    alphas = [None] * pairs
    for slot in reversed(range(pairs)):
        projected = step_grad[slot]
        for later in range(slot + 1, pairs):
            projected = projected - alphas[later] * step_change[slot, later]
        alphas[slot] = projected / curvature[slot]
    scaling = curvature[pairs - 1] / change_change[pairs - 1, pairs - 1]
    weights = [None] * pairs
    for slot in range(pairs):
        along = change_grad[slot]
        for other in range(pairs):
            along = along - alphas[other] * change_change[slot, other]
        along = scaling * along
        for earlier in range(slot):
            along = along + weights[earlier] * step_change[earlier, slot]
        beta_now = along / curvature[slot]
        weights[slot] = alphas[slot] - beta_now
    step_share = own_share(step_rows)
    change_share = own_share(change_rows)
    work = scaling * grad_share
    for slot in range(pairs):
        work = work - (scaling * alphas[slot]) * change_share[slot]
    for slot in range(pairs):
        work = work + weights[slot] * step_share[slot]
    return -work


def shards(
    adjoint_state,
    forward_states,
    material,
    coupling,
    metric,
    face_normals,
    face_scale,
    face_neighbours,
    face_orientation,
    send_faces,
    history_steps,
    history_changes,
):
    derivs, lift_tables, face_nodes, turn_nodes = basis_tables()
    fields = adjoint_state.shape[1]
    elements = adjoint_state.shape[3]
    node_count = material.shape[1]
    params = material.shape[0]
    face_width = face_nodes.shape[1]
    border = send_faces.shape[0] // 2
    slot_count = 4 * elements + 2 * border
    adjoint = adjoint_state[0]
    face_material = material[:, face_nodes.T, :]
    neighbours = face_neighbours.reshape(-1)
    orient = face_orientation.reshape(-1)
    node_pick = jnp.zeros((face_width, 4 * elements), jnp.int32)
    for option in range(turn_nodes.shape[0]):
        node_pick = (
            node_pick
            + (orient == option).astype(jnp.int32)[None, :]
            * jnp.asarray(turn_nodes[option], jnp.int32)[:, None]
        )
    flat_index = (node_pick * slot_count + neighbours[None, :]).reshape(-1)
    gradient = jnp.zeros((params, node_count, elements), jnp.float32)
    for step_index in range(forward_states.shape[1]):
        inner_trace = adjoint[:, face_nodes.T, :]
        flat_trace = inner_trace.reshape(fields, face_width, 4 * elements)
        sent_traces = flat_trace[:, :, send_faces]
        extended = padded(sent_traces, (("mesh", 2),), border)
        ghosts = jnp.concatenate(
            [flat_trace, extended[:, :, :border], extended[:, :, 3 * border :]], axis=2
        )
        turned = ghosts.reshape(fields, face_width * slot_count)[:, flat_index]
        jump_trace = turned.reshape(fields, face_width, 4, elements) - inner_trace
        change = volume_term(adjoint, material, coupling, metric, derivs) + surface_term(
            jump_trace, face_material, face_normals, face_scale, coupling, lift_tables
        )
        adjoint = adjoint + STEP_SIZE * change
        gradient = gradient + STEP_SIZE * kernel_term(
            adjoint, forward_states[0, step_index], coupling, metric, derivs
        )
    shot_count = lax.axis_size("shot")
    share_width = elements // shot_count
    share_start = lax.axis_index("shot") * share_width

    def own_share(rows):
        return lax.dynamic_slice_in_dim(rows, share_start, share_width, rows.ndim - 1)

    device_count = shot_count * lax.axis_size("mesh")

    def combine_sums(values):
        spread = jnp.broadcast_to(values[None], (device_count,) + values.shape)
        return jnp.sum(lax.all_to_all(spread, ("shot", "mesh"), 0, 0, tiled=False), axis=0)

    grad_share = halving_sum(gradient, "shot", shot_count)
    keep_gram = (lax.axis_index("shot") == 0).astype(jnp.float32)
    result = search_direction(
        grad_share, gradient, history_steps, history_changes, own_share, keep_gram, combine_sums
    )
    return (adjoint[None], result)


def solution(mesh):
    placed = (
        P("shot", None, None, "mesh"),
        P("shot", None, None, None, "mesh"),
        P(None, None, "mesh"),
        P(),
        P(None, None, "mesh"),
        P(None, None, "mesh"),
        P(None, "mesh"),
        P(None, "mesh"),
        P(None, "mesh"),
        P("mesh"),
        P(None, None, None, "mesh"),
        P(None, None, None, "mesh"),
    )
    return jax.shard_map(
        shards,
        mesh=mesh,
        in_specs=placed,
        out_specs=(P("shot", None, None, "mesh"), P(None, None, ("mesh", "shot"))),
        check_vma=False,
    )
```

```python
import math

import jax
import jax.numpy as jnp
import numpy as np
from jax import lax
from jax.sharding import PartitionSpec as P

HIGH = lax.Precision.HIGHEST
STEP_SIZE = 0.02


def padded(x, sides, width):
    for axis, dim in sides:
        devices, length = (lax.axis_size(axis), x.shape[dim])
        up = [(i, (i + 1) % devices) for i in range(devices - 1)]
        down = [(j, i) for i, j in up]
        last = lax.slice_in_dim(x, length - width, length, axis=dim)
        first = lax.slice_in_dim(x, 0, width, axis=dim)
        before = lax.ppermute(last, axis, up)
        after = lax.ppermute(first, axis, down)
        x = jnp.concatenate([before, x, after], axis=dim)
    return x


def invert_matrix(matrix):
    order_count = matrix.shape[0]
    working = np.concatenate([matrix * 1.0, np.eye(order_count)], axis=1)
    for column in range(order_count):
        pivot_row = column + int(np.argmax(np.abs(working[column:, column])))
        working[[column, pivot_row]] = working[[pivot_row, column]]
        working[column] = working[column] / working[column, column]
        for target in range(order_count):
            if target != column:
                working[target] = working[target] - working[target, column] * working[column]
    return working[:, order_count:]


def basis_tables():
    points = [
        (across, along, upward)
        for upward in range(5)
        for along in range(5 - upward)
        for across in range(5 - upward - along)
    ]
    exponents = np.array(points) * 1.0
    coords = exponents / 4.0
    vander = np.prod(coords[:, None, :] ** exponents[None, :, :], axis=2)
    inverse = invert_matrix(vander)
    derivs = []
    for direction_axis in range(3):
        lowered = np.maximum(exponents - np.eye(3)[direction_axis], 0.0)
        slopes = exponents[None, :, direction_axis] * np.prod(
            coords[:, None, :] ** lowered[None, :, :], axis=2
        )
        derivs.append(slopes @ inverse)
    moments = np.array(
        [
            [
                math.factorial(first[0] + second[0])
                * math.factorial(first[1] + second[1])
                * math.factorial(first[2] + second[2])
                / math.factorial(sum(first) + sum(second) + 3)
                for second in points
            ]
            for first in points
        ]
    )
    mass_matrix = inverse.T @ moments @ inverse
    lattice = [(across, along) for along in range(5) for across in range(5 - along)]
    lattice_powers = np.array(lattice) * 1.0
    face_vander = np.prod((lattice_powers / 4.0)[:, None, :] ** lattice_powers[None, :, :], axis=2)
    face_inverse = invert_matrix(face_vander)
    face_moments = np.array(
        [
            [
                math.factorial(first[0] + second[0])
                * math.factorial(first[1] + second[1])
                / math.factorial(sum(first) + sum(second) + 2)
                for second in lattice
            ]
            for first in lattice
        ]
    )
    face_mass = face_inverse.T @ face_moments @ face_inverse
    numbers = {point: number for number, point in enumerate(points)}
    face_points = [
        [(across, along, 0) for across, along in lattice],
        [(across, 0, along) for across, along in lattice],
        [(0, across, along) for across, along in lattice],
        [(across, along, 4 - across - along) for across, along in lattice],
    ]
    face_nodes = np.array(
        [[numbers[point] for point in listing] for listing in face_points], np.int32
    )
    mass_inverse = invert_matrix(mass_matrix)
    lift_tables = []
    for face_number in range(4):
        selector = np.eye(35)[face_nodes[face_number]]
        lift_tables.append(mass_inverse @ selector.T @ face_mass)
    orderings = [(0, 1, 2), (1, 2, 0), (2, 0, 1), (1, 0, 2), (0, 2, 1), (2, 1, 0)]
    lattice_numbers = {point: number for number, point in enumerate(lattice)}
    triples = [(across, along, 4 - across - along) for across, along in lattice]
    turn_nodes = np.array(
        [
            [lattice_numbers[triple[ordering[0]], triple[ordering[1]]] for triple in triples]
            for ordering in orderings
        ],
        np.int32,
    )
    return (
        jnp.asarray(np.stack(derivs), jnp.float32),
        jnp.asarray(np.stack(lift_tables), jnp.float32),
        face_nodes,
        turn_nodes,
    )


def spatial_of(field, metric, derivs):
    reference_grads = jnp.einsum("rab,fbe->rfae", derivs, field, precision=HIGH)
    rows = []
    for direction_axis in range(3):
        total = metric[0, direction_axis] * reference_grads[0]
        total = total + metric[1, direction_axis] * reference_grads[1]
        total = total + metric[2, direction_axis] * reference_grads[2]
        rows.append(total)
    return jnp.stack(rows)


def volume_term(adjoint, material, coupling, metric, derivs):
    spatial = spatial_of(adjoint, metric, derivs)
    mixing = jnp.einsum("dpfg,dfae->pgae", coupling, spatial, precision=HIGH)
    return jnp.sum(material[:, None] * mixing, axis=0)


def kernel_term(adjoint, forward, coupling, metric, derivs):
    spatial = spatial_of(forward, metric, derivs)
    mixing = jnp.einsum("dpfg,dgae->pfae", coupling, spatial, precision=HIGH)
    return jnp.sum(mixing * adjoint[None], axis=1)


def surface_term(jump_trace, face_material, face_normals, face_scale, coupling, lift_tables):
    weighted = face_normals[:, None, None] * jump_trace[None]
    mixing = jnp.einsum("dpfg,dfnxe->pgnxe", coupling, weighted, precision=HIGH)
    face_flux = 0.5 * jnp.sum(face_material[:, None] * mixing, axis=0) + 0.5 * jump_trace
    return jnp.einsum(
        "xan,fnxe->fae", lift_tables, face_flux * face_scale[None, None], precision=HIGH
    )


def halving_sum(values, axis, count):
    position = lax.axis_index(axis)
    work = values
    bit = count // 2
    while bit >= 1:
        width = work.shape[-1] // 2
        upper = (position & bit) != 0
        low = work[..., :width]
        high = work[..., width:]
        sent = lax.ppermute(
            jnp.where(upper, low, high), axis, [(i, i ^ bit) for i in range(count)]
        )
        work = jnp.where(upper, high, low) + sent
        bit //= 2
    return work


def search_direction(grad_share, local_grad, step_rows, change_rows, own_share, keep_gram, combine_sums):
    pairs = step_rows.shape[0]
    step_flat = step_rows.reshape(pairs, -1)
    change_flat = change_rows.reshape(pairs, -1)
    both_flat = jnp.concatenate([step_flat, change_flat], axis=0)
    with_grad = jnp.dot(both_flat, local_grad.reshape(-1), precision=HIGH)
    gram = jnp.dot(both_flat, change_flat.T, precision=HIGH) * keep_gram
    summed = combine_sums(jnp.concatenate([with_grad, gram.reshape(-1)]))
    step_grad = summed[:pairs]
    change_grad = summed[pairs : 2 * pairs]
    gram = summed[2 * pairs :].reshape(2 * pairs, pairs)
    step_change = gram[:pairs]
    change_change = gram[pairs:]
    curvature = [step_change[slot, slot] for slot in range(pairs)]
    alphas = [None] * pairs
    for slot in reversed(range(pairs)):
        projected = step_grad[slot]
        for later in range(slot + 1, pairs):
            projected = projected - alphas[later] * step_change[slot, later]
        alphas[slot] = projected / curvature[slot]
    scaling = curvature[pairs - 1] / change_change[pairs - 1, pairs - 1]
    weights = [None] * pairs
    for slot in range(pairs):
        along = change_grad[slot]
        for other in range(pairs):
            along = along - alphas[other] * change_change[slot, other]
        along = scaling * along
        for earlier in range(slot):
            along = along + weights[earlier] * step_change[earlier, slot]
        beta_now = along / curvature[slot]
        weights[slot] = alphas[slot] - beta_now
    combined = (-scaling * alphas[0]) * change_rows[0]
    for slot in range(1, pairs):
        combined = combined - (scaling * alphas[slot]) * change_rows[slot]
    for slot in range(pairs):
        combined = combined + weights[slot] * step_rows[slot]
    work = scaling * grad_share + own_share(combined)
    return -work


def shards(
    adjoint_state,
    forward_states,
    material,
    coupling,
    metric,
    face_normals,
    face_scale,
    face_neighbours,
    face_orientation,
    send_faces,
    history_steps,
    history_changes,
):
    derivs, lift_tables, face_nodes, turn_nodes = basis_tables()
    fields = adjoint_state.shape[1]
    elements = adjoint_state.shape[3]
    node_count = material.shape[1]
    params = material.shape[0]
    face_width = face_nodes.shape[1]
    border = send_faces.shape[0] // 2
    slot_count = 4 * elements + 2 * border
    adjoint = adjoint_state[0]
    face_material = material[:, face_nodes.T, :]
    neighbours = face_neighbours.reshape(-1)
    orient = face_orientation.reshape(-1)
    node_pick = jnp.zeros((face_width, 4 * elements), jnp.int32)
    for option in range(turn_nodes.shape[0]):
        node_pick = (
            node_pick
            + (orient == option).astype(jnp.int32)[None, :]
            * jnp.asarray(turn_nodes[option], jnp.int32)[:, None]
        )
    flat_index = (node_pick * slot_count + neighbours[None, :]).reshape(-1)
    gradient = jnp.zeros((params, node_count, elements), jnp.float32)
    for step_index in range(forward_states.shape[1]):
        inner_trace = adjoint[:, face_nodes.T, :]
        flat_trace = inner_trace.reshape(fields, face_width, 4 * elements)
        sent_traces = flat_trace[:, :, send_faces]
        extended = padded(sent_traces, (("mesh", 2),), border)
        ghosts = jnp.concatenate(
            [flat_trace, extended[:, :, :border], extended[:, :, 3 * border :]], axis=2
        )
        turned = ghosts.reshape(fields, face_width * slot_count)[:, flat_index]
        jump_trace = turned.reshape(fields, face_width, 4, elements) - inner_trace
        change = volume_term(adjoint, material, coupling, metric, derivs) + surface_term(
            jump_trace, face_material, face_normals, face_scale, coupling, lift_tables
        )
        adjoint = adjoint + STEP_SIZE * change
        gradient = gradient + STEP_SIZE * kernel_term(
            adjoint, forward_states[0, step_index], coupling, metric, derivs
        )
    shot_count = lax.axis_size("shot")
    share_width = elements // shot_count
    share_start = lax.axis_index("shot") * share_width

    def own_share(rows):
        return lax.dynamic_slice_in_dim(rows, share_start, share_width, rows.ndim - 1)

    device_count = shot_count * lax.axis_size("mesh")

    def combine_sums(values):
        spread = jnp.broadcast_to(values[None], (device_count,) + values.shape)
        return jnp.sum(lax.all_to_all(spread, ("shot", "mesh"), 0, 0, tiled=False), axis=0)

    grad_share = halving_sum(gradient, "shot", shot_count)
    keep_gram = (lax.axis_index("shot") == 0).astype(jnp.float32)
    result = search_direction(
        grad_share, gradient, history_steps, history_changes, own_share, keep_gram, combine_sums
    )
    return (adjoint[None], result)


def solution(mesh):
    placed = (
        P("shot", None, None, "mesh"),
        P("shot", None, None, None, "mesh"),
        P(None, None, "mesh"),
        P(),
        P(None, None, "mesh"),
        P(None, None, "mesh"),
        P(None, "mesh"),
        P(None, "mesh"),
        P(None, "mesh"),
        P("mesh"),
        P(None, None, None, "mesh"),
        P(None, None, None, "mesh"),
    )
    return jax.shard_map(
        shards,
        mesh=mesh,
        in_specs=placed,
        out_specs=(P("shot", None, None, "mesh"), P(None, None, ("mesh", "shot"))),
        check_vma=False,
    )
```

```python
import math

import jax
import jax.numpy as jnp
import numpy as np
from jax import lax
from jax.sharding import PartitionSpec as P

HIGH = lax.Precision.HIGHEST
STEP_SIZE = 0.02


def padded(x, sides, width):
    for axis, dim in sides:
        devices, length = (lax.axis_size(axis), x.shape[dim])
        up = [(i, (i + 1) % devices) for i in range(devices - 1)]
        down = [(j, i) for i, j in up]
        last = lax.slice_in_dim(x, length - width, length, axis=dim)
        first = lax.slice_in_dim(x, 0, width, axis=dim)
        before = lax.ppermute(last, axis, up)
        after = lax.ppermute(first, axis, down)
        x = jnp.concatenate([before, x, after], axis=dim)
    return x


def invert_matrix(matrix):
    order_count = matrix.shape[0]
    working = np.concatenate([matrix * 1.0, np.eye(order_count)], axis=1)
    for column in range(order_count):
        pivot_row = column + int(np.argmax(np.abs(working[column:, column])))
        working[[column, pivot_row]] = working[[pivot_row, column]]
        working[column] = working[column] / working[column, column]
        for target in range(order_count):
            if target != column:
                working[target] = working[target] - working[target, column] * working[column]
    return working[:, order_count:]


def basis_tables():
    points = [
        (across, along, upward)
        for upward in range(5)
        for along in range(5 - upward)
        for across in range(5 - upward - along)
    ]
    exponents = np.array(points) * 1.0
    coords = exponents / 4.0
    vander = np.prod(coords[:, None, :] ** exponents[None, :, :], axis=2)
    inverse = invert_matrix(vander)
    derivs = []
    for direction_axis in range(3):
        lowered = np.maximum(exponents - np.eye(3)[direction_axis], 0.0)
        slopes = exponents[None, :, direction_axis] * np.prod(
            coords[:, None, :] ** lowered[None, :, :], axis=2
        )
        derivs.append(slopes @ inverse)
    moments = np.array(
        [
            [
                math.factorial(first[0] + second[0])
                * math.factorial(first[1] + second[1])
                * math.factorial(first[2] + second[2])
                / math.factorial(sum(first) + sum(second) + 3)
                for second in points
            ]
            for first in points
        ]
    )
    mass_matrix = inverse.T @ moments @ inverse
    lattice = [(across, along) for along in range(5) for across in range(5 - along)]
    lattice_powers = np.array(lattice) * 1.0
    face_vander = np.prod((lattice_powers / 4.0)[:, None, :] ** lattice_powers[None, :, :], axis=2)
    face_inverse = invert_matrix(face_vander)
    face_moments = np.array(
        [
            [
                math.factorial(first[0] + second[0])
                * math.factorial(first[1] + second[1])
                / math.factorial(sum(first) + sum(second) + 2)
                for second in lattice
            ]
            for first in lattice
        ]
    )
    face_mass = face_inverse.T @ face_moments @ face_inverse
    numbers = {point: number for number, point in enumerate(points)}
    face_points = [
        [(across, along, 0) for across, along in lattice],
        [(across, 0, along) for across, along in lattice],
        [(0, across, along) for across, along in lattice],
        [(across, along, 4 - across - along) for across, along in lattice],
    ]
    face_nodes = np.array(
        [[numbers[point] for point in listing] for listing in face_points], np.int32
    )
    mass_inverse = invert_matrix(mass_matrix)
    lift_tables = []
    for face_number in range(4):
        selector = np.eye(35)[face_nodes[face_number]]
        lift_tables.append(mass_inverse @ selector.T @ face_mass)
    orderings = [(0, 1, 2), (1, 2, 0), (2, 0, 1), (1, 0, 2), (0, 2, 1), (2, 1, 0)]
    lattice_numbers = {point: number for number, point in enumerate(lattice)}
    triples = [(across, along, 4 - across - along) for across, along in lattice]
    turn_nodes = np.array(
        [
            [lattice_numbers[triple[ordering[0]], triple[ordering[1]]] for triple in triples]
            for ordering in orderings
        ],
        np.int32,
    )
    return (
        jnp.asarray(np.stack(derivs), jnp.float32),
        jnp.asarray(np.stack(lift_tables), jnp.float32),
        face_nodes,
        turn_nodes,
    )


def spatial_of(field, metric, derivs):
    reference_grads = jnp.einsum("rab,fbe->rfae", derivs, field, precision=HIGH)
    rows = []
    for direction_axis in range(3):
        total = metric[0, direction_axis] * reference_grads[0]
        total = total + metric[1, direction_axis] * reference_grads[1]
        total = total + metric[2, direction_axis] * reference_grads[2]
        rows.append(total)
    return jnp.stack(rows)


def volume_term(adjoint, material, coupling, metric, derivs):
    spatial = spatial_of(adjoint, metric, derivs)
    mixing = jnp.einsum("dpfg,dfae->pgae", coupling, spatial, precision=HIGH)
    return jnp.sum(material[:, None] * mixing, axis=0)


def kernel_term(adjoint, forward, coupling, metric, derivs):
    spatial = spatial_of(forward, metric, derivs)
    mixing = jnp.einsum("dpfg,dgae->pfae", coupling, spatial, precision=HIGH)
    return jnp.sum(mixing * adjoint[None], axis=1)


def surface_term(jump_trace, face_material, face_normals, face_scale, coupling, lift_tables):
    weighted = face_normals[:, None, None] * jump_trace[None]
    mixing = jnp.einsum("dpfg,dfnxe->pgnxe", coupling, weighted, precision=HIGH)
    face_flux = 0.5 * jnp.sum(face_material[:, None] * mixing, axis=0) + 0.5 * jump_trace
    return jnp.einsum(
        "xan,fnxe->fae", lift_tables, face_flux * face_scale[None, None], precision=HIGH
    )


def halving_sum(values, axis, count):
    position = lax.axis_index(axis)
    work = values
    bit = count // 2
    while bit >= 1:
        width = work.shape[-1] // 2
        upper = (position & bit) != 0
        low = work[..., :width]
        high = work[..., width:]
        sent = lax.ppermute(
            jnp.where(upper, low, high), axis, [(i, i ^ bit) for i in range(count)]
        )
        work = jnp.where(upper, high, low) + sent
        bit //= 2
    return work


def search_direction(grad_share, step_share, change_share, gram, combine_sums):
    pairs = step_share.shape[0]
    both_share = jnp.concatenate([step_share, change_share], axis=0)
    with_grad = jnp.sum(both_share * grad_share[None], axis=(1, 2, 3))
    summed = combine_sums(jnp.concatenate([with_grad, gram.reshape(-1)]))
    step_grad = summed[:pairs]
    change_grad = summed[pairs : 2 * pairs]
    gram = summed[2 * pairs :].reshape(2 * pairs, pairs)
    step_change = gram[:pairs]
    change_change = gram[pairs:]
    curvature = [step_change[slot, slot] for slot in range(pairs)]
    alphas = [None] * pairs
    for slot in reversed(range(pairs)):
        projected = step_grad[slot]
        for later in range(slot + 1, pairs):
            projected = projected - alphas[later] * step_change[slot, later]
        alphas[slot] = projected / curvature[slot]
    scaling = curvature[pairs - 1] / change_change[pairs - 1, pairs - 1]
    weights = [None] * pairs
    for slot in range(pairs):
        along = change_grad[slot]
        for other in range(pairs):
            along = along - alphas[other] * change_change[slot, other]
        along = scaling * along
        for earlier in range(slot):
            along = along + weights[earlier] * step_change[earlier, slot]
        beta_now = along / curvature[slot]
        weights[slot] = alphas[slot] - beta_now
    work = scaling * grad_share
    for slot in range(pairs):
        work = work - (scaling * alphas[slot]) * change_share[slot]
    for slot in range(pairs):
        work = work + weights[slot] * step_share[slot]
    return -work


def shards(
    adjoint_state,
    forward_states,
    material,
    coupling,
    metric,
    face_normals,
    face_scale,
    face_neighbours,
    face_orientation,
    send_faces,
    history_steps,
    history_changes,
):
    derivs, lift_tables, face_nodes, turn_nodes = basis_tables()
    fields = adjoint_state.shape[1]
    elements = adjoint_state.shape[3]
    node_count = material.shape[1]
    params = material.shape[0]
    face_width = face_nodes.shape[1]
    border = send_faces.shape[0] // 2
    slot_count = 4 * elements + 2 * border
    adjoint = adjoint_state[0]
    face_material = material[:, face_nodes.T, :]
    neighbours = face_neighbours.reshape(-1)
    orient = face_orientation.reshape(-1)
    node_pick = jnp.zeros((face_width, 4 * elements), jnp.int32)
    for option in range(turn_nodes.shape[0]):
        node_pick = (
            node_pick
            + (orient == option).astype(jnp.int32)[None, :]
            * jnp.asarray(turn_nodes[option], jnp.int32)[:, None]
        )
    flat_index = (node_pick * slot_count + neighbours[None, :]).reshape(-1)
    shot_count = lax.axis_size("shot")
    share_width = elements // shot_count
    share_start = lax.axis_index("shot") * share_width

    def own_share(rows):
        return lax.dynamic_slice_in_dim(rows, share_start, share_width, rows.ndim - 1)

    step_share = own_share(history_steps)
    change_share = own_share(history_changes)
    both_share = jnp.concatenate([step_share, change_share], axis=0)
    gram = jnp.sum(both_share[:, None] * change_share[None, :], axis=(2, 3, 4))
    step_share, change_share, gram, adjoint = lax.optimization_barrier(
        (step_share, change_share, gram, adjoint)
    )
    gradient = jnp.zeros((params, node_count, elements), jnp.float32)
    for step_index in range(forward_states.shape[1]):
        inner_trace = adjoint[:, face_nodes.T, :]
        flat_trace = inner_trace.reshape(fields, face_width, 4 * elements)
        sent_traces = flat_trace[:, :, send_faces]
        extended = padded(sent_traces, (("mesh", 2),), border)
        ghosts = jnp.concatenate(
            [flat_trace, extended[:, :, :border], extended[:, :, 3 * border :]], axis=2
        )
        turned = ghosts.reshape(fields, face_width * slot_count)[:, flat_index]
        jump_trace = turned.reshape(fields, face_width, 4, elements) - inner_trace
        change = volume_term(adjoint, material, coupling, metric, derivs) + surface_term(
            jump_trace, face_material, face_normals, face_scale, coupling, lift_tables
        )
        adjoint = adjoint + STEP_SIZE * change
        gradient = gradient + STEP_SIZE * kernel_term(
            adjoint, forward_states[0, step_index], coupling, metric, derivs
        )
    device_count = shot_count * lax.axis_size("mesh")

    def combine_sums(values):
        spread = jnp.broadcast_to(values[None], (device_count,) + values.shape)
        return jnp.sum(lax.all_to_all(spread, ("shot", "mesh"), 0, 0, tiled=False), axis=0)

    grad_share = halving_sum(gradient, "shot", shot_count)
    result = search_direction(grad_share, step_share, change_share, gram, combine_sums)
    return (adjoint[None], result)


def solution(mesh):
    placed = (
        P("shot", None, None, "mesh"),
        P("shot", None, None, None, "mesh"),
        P(None, None, "mesh"),
        P(),
        P(None, None, "mesh"),
        P(None, None, "mesh"),
        P(None, "mesh"),
        P(None, "mesh"),
        P(None, "mesh"),
        P("mesh"),
        P(None, None, None, "mesh"),
        P(None, None, None, "mesh"),
    )
    return jax.shard_map(
        shards,
        mesh=mesh,
        in_specs=placed,
        out_specs=(P("shot", None, None, "mesh"), P(None, None, ("mesh", "shot"))),
        check_vma=False,
    )
```

```python
import math

import jax
import jax.numpy as jnp
import numpy as np
from jax import lax
from jax.sharding import PartitionSpec as P

HIGH = lax.Precision.HIGHEST
STEP_SIZE = 0.02


def padded(x, sides, width):
    for axis, dim in sides:
        devices, length = (lax.axis_size(axis), x.shape[dim])
        up = [(i, (i + 1) % devices) for i in range(devices - 1)]
        down = [(j, i) for i, j in up]
        last = lax.slice_in_dim(x, length - width, length, axis=dim)
        first = lax.slice_in_dim(x, 0, width, axis=dim)
        before = lax.ppermute(last, axis, up)
        after = lax.ppermute(first, axis, down)
        x = jnp.concatenate([before, x, after], axis=dim)
    return x


def invert_matrix(matrix):
    order_count = matrix.shape[0]
    working = np.concatenate([matrix * 1.0, np.eye(order_count)], axis=1)
    for column in range(order_count):
        pivot_row = column + int(np.argmax(np.abs(working[column:, column])))
        working[[column, pivot_row]] = working[[pivot_row, column]]
        working[column] = working[column] / working[column, column]
        for target in range(order_count):
            if target != column:
                working[target] = working[target] - working[target, column] * working[column]
    return working[:, order_count:]


def basis_tables():
    points = [
        (across, along, upward)
        for upward in range(5)
        for along in range(5 - upward)
        for across in range(5 - upward - along)
    ]
    exponents = np.array(points) * 1.0
    coords = exponents / 4.0
    vander = np.prod(coords[:, None, :] ** exponents[None, :, :], axis=2)
    inverse = invert_matrix(vander)
    derivs = []
    for direction_axis in range(3):
        lowered = np.maximum(exponents - np.eye(3)[direction_axis], 0.0)
        slopes = exponents[None, :, direction_axis] * np.prod(
            coords[:, None, :] ** lowered[None, :, :], axis=2
        )
        derivs.append(slopes @ inverse)
    moments = np.array(
        [
            [
                math.factorial(first[0] + second[0])
                * math.factorial(first[1] + second[1])
                * math.factorial(first[2] + second[2])
                / math.factorial(sum(first) + sum(second) + 3)
                for second in points
            ]
            for first in points
        ]
    )
    mass_matrix = inverse.T @ moments @ inverse
    lattice = [(across, along) for along in range(5) for across in range(5 - along)]
    lattice_powers = np.array(lattice) * 1.0
    face_vander = np.prod((lattice_powers / 4.0)[:, None, :] ** lattice_powers[None, :, :], axis=2)
    face_inverse = invert_matrix(face_vander)
    face_moments = np.array(
        [
            [
                math.factorial(first[0] + second[0])
                * math.factorial(first[1] + second[1])
                / math.factorial(sum(first) + sum(second) + 2)
                for second in lattice
            ]
            for first in lattice
        ]
    )
    face_mass = face_inverse.T @ face_moments @ face_inverse
    numbers = {point: number for number, point in enumerate(points)}
    face_points = [
        [(across, along, 0) for across, along in lattice],
        [(across, 0, along) for across, along in lattice],
        [(0, across, along) for across, along in lattice],
        [(across, along, 4 - across - along) for across, along in lattice],
    ]
    face_nodes = np.array(
        [[numbers[point] for point in listing] for listing in face_points], np.int32
    )
    mass_inverse = invert_matrix(mass_matrix)
    lift_tables = []
    for face_number in range(4):
        selector = np.eye(35)[face_nodes[face_number]]
        lift_tables.append(mass_inverse @ selector.T @ face_mass)
    orderings = [(0, 1, 2), (1, 2, 0), (2, 0, 1), (1, 0, 2), (0, 2, 1), (2, 1, 0)]
    lattice_numbers = {point: number for number, point in enumerate(lattice)}
    triples = [(across, along, 4 - across - along) for across, along in lattice]
    turn_nodes = np.array(
        [
            [lattice_numbers[triple[ordering[0]], triple[ordering[1]]] for triple in triples]
            for ordering in orderings
        ],
        np.int32,
    )
    return (
        jnp.asarray(np.stack(derivs), jnp.float32),
        jnp.asarray(np.stack(lift_tables), jnp.float32),
        face_nodes,
        turn_nodes,
    )


def spatial_of(field, metric, derivs):
    reference_grads = jnp.einsum("rab,fbe->rfae", derivs, field, precision=HIGH)
    rows = []
    for direction_axis in range(3):
        total = metric[0, direction_axis] * reference_grads[0]
        total = total + metric[1, direction_axis] * reference_grads[1]
        total = total + metric[2, direction_axis] * reference_grads[2]
        rows.append(total)
    return jnp.stack(rows)


def volume_term(adjoint, material, coupling, metric, derivs):
    spatial = spatial_of(adjoint, metric, derivs)
    mixing = jnp.einsum("dpfg,dfae->pgae", coupling, spatial, precision=HIGH)
    return jnp.sum(material[:, None] * mixing, axis=0)


def kernel_term(adjoint, forward, coupling, metric, derivs):
    spatial = spatial_of(forward, metric, derivs)
    mixing = jnp.einsum("dpfg,dgae->pfae", coupling, spatial, precision=HIGH)
    return jnp.sum(mixing * adjoint[None], axis=1)


def surface_term(jump_trace, face_material, face_normals, face_scale, coupling, lift_tables):
    weighted = face_normals[:, None, None] * jump_trace[None]
    mixing = jnp.einsum("dpfg,dfnxe->pgnxe", coupling, weighted, precision=HIGH)
    face_flux = 0.5 * jnp.sum(face_material[:, None] * mixing, axis=0) + 0.5 * jump_trace
    return jnp.einsum(
        "xan,fnxe->fae", lift_tables, face_flux * face_scale[None, None], precision=HIGH
    )


def halving_sum(values, axis, count):
    position = lax.axis_index(axis)
    work = values
    bit = count // 2
    while bit >= 1:
        width = work.shape[-1] // 2
        upper = (position & bit) != 0
        low = work[..., :width]
        high = work[..., width:]
        sent = lax.ppermute(
            jnp.where(upper, low, high), axis, [(i, i ^ bit) for i in range(count)]
        )
        work = jnp.where(upper, high, low) + sent
        bit //= 2
    return work


def search_direction(grad_share, step_share, change_share, gram, combine_sums):
    pairs = step_share.shape[0]
    both_share = jnp.concatenate([step_share, change_share], axis=0)
    with_grad = jnp.sum(both_share * grad_share[None], axis=(1, 2, 3))
    summed = combine_sums(jnp.concatenate([with_grad, gram.reshape(-1)]))
    lanes = 0.0 * step_share[0, 0, :8, :]
    summed = summed[:, None, None] + lanes[None]
    step_grad = summed[:pairs]
    change_grad = summed[pairs : 2 * pairs]
    gram = summed[2 * pairs :].reshape((2 * pairs, pairs) + summed.shape[1:])
    step_change = gram[:pairs]
    change_change = gram[pairs:]
    curvature = [step_change[slot, slot] for slot in range(pairs)]
    alphas = [None] * pairs
    for slot in reversed(range(pairs)):
        projected = step_grad[slot]
        for later in range(slot + 1, pairs):
            projected = projected - alphas[later] * step_change[slot, later]
        alphas[slot] = projected / curvature[slot]
    scaling = curvature[pairs - 1] / change_change[pairs - 1, pairs - 1]
    weights = [None] * pairs
    for slot in range(pairs):
        along = change_grad[slot]
        for other in range(pairs):
            along = along - alphas[other] * change_change[slot, other]
        along = scaling * along
        for earlier in range(slot):
            along = along + weights[earlier] * step_change[earlier, slot]
        beta_now = along / curvature[slot]
        weights[slot] = alphas[slot] - beta_now
    coefficients = jnp.stack(
        [weights[slot] for slot in range(pairs)]
        + [-scaling * alphas[slot] for slot in range(pairs)]
        + [scaling]
    )[:, 0, 0]
    rows = jnp.concatenate([both_share, grad_share[None]], axis=0)
    work = jnp.sum(coefficients[:, None, None, None] * rows, axis=0)
    return -work


def shards(
    adjoint_state,
    forward_states,
    material,
    coupling,
    metric,
    face_normals,
    face_scale,
    face_neighbours,
    face_orientation,
    send_faces,
    history_steps,
    history_changes,
):
    derivs, lift_tables, face_nodes, turn_nodes = basis_tables()
    fields = adjoint_state.shape[1]
    elements = adjoint_state.shape[3]
    node_count = material.shape[1]
    params = material.shape[0]
    face_width = face_nodes.shape[1]
    border = send_faces.shape[0] // 2
    slot_count = 4 * elements + 2 * border
    adjoint = adjoint_state[0]
    face_material = material[:, face_nodes.T, :]
    neighbours = face_neighbours.reshape(-1)
    orient = face_orientation.reshape(-1)
    node_pick = jnp.zeros((face_width, 4 * elements), jnp.int32)
    for option in range(turn_nodes.shape[0]):
        node_pick = (
            node_pick
            + (orient == option).astype(jnp.int32)[None, :]
            * jnp.asarray(turn_nodes[option], jnp.int32)[:, None]
        )
    flat_index = (node_pick * slot_count + neighbours[None, :]).reshape(-1)
    shot_count = lax.axis_size("shot")
    share_width = elements // shot_count
    share_start = lax.axis_index("shot") * share_width

    def own_share(rows):
        return lax.dynamic_slice_in_dim(rows, share_start, share_width, rows.ndim - 1)

    step_share = own_share(history_steps)
    change_share = own_share(history_changes)
    both_share = jnp.concatenate([step_share, change_share], axis=0)
    gram = jnp.sum(both_share[:, None] * change_share[None, :], axis=(2, 3, 4))
    step_share, change_share, gram, adjoint = lax.optimization_barrier(
        (step_share, change_share, gram, adjoint)
    )
    gradient = jnp.zeros((params, node_count, elements), jnp.float32)
    for step_index in range(forward_states.shape[1]):
        inner_trace = adjoint[:, face_nodes.T, :]
        flat_trace = inner_trace.reshape(fields, face_width, 4 * elements)
        sent_traces = flat_trace[:, :, send_faces]
        extended = padded(sent_traces, (("mesh", 2),), border)
        ghosts = jnp.concatenate(
            [flat_trace, extended[:, :, :border], extended[:, :, 3 * border :]], axis=2
        )
        turned = ghosts.reshape(fields, face_width * slot_count)[:, flat_index]
        jump_trace = turned.reshape(fields, face_width, 4, elements) - inner_trace
        change = volume_term(adjoint, material, coupling, metric, derivs) + surface_term(
            jump_trace, face_material, face_normals, face_scale, coupling, lift_tables
        )
        adjoint = adjoint + STEP_SIZE * change
        gradient = gradient + STEP_SIZE * kernel_term(
            adjoint, forward_states[0, step_index], coupling, metric, derivs
        )
    device_count = shot_count * lax.axis_size("mesh")

    def combine_sums(values):
        spread = jnp.broadcast_to(values[None], (device_count,) + values.shape)
        return jnp.sum(lax.all_to_all(spread, ("shot", "mesh"), 0, 0, tiled=False), axis=0)

    grad_share = halving_sum(gradient, "shot", shot_count)
    result = search_direction(grad_share, step_share, change_share, gram, combine_sums)
    return (adjoint[None], result)


def solution(mesh):
    placed = (
        P("shot", None, None, "mesh"),
        P("shot", None, None, None, "mesh"),
        P(None, None, "mesh"),
        P(),
        P(None, None, "mesh"),
        P(None, None, "mesh"),
        P(None, "mesh"),
        P(None, "mesh"),
        P(None, "mesh"),
        P("mesh"),
        P(None, None, None, "mesh"),
        P(None, None, None, "mesh"),
    )
    return jax.shard_map(
        shards,
        mesh=mesh,
        in_specs=placed,
        out_specs=(P("shot", None, None, "mesh"), P(None, None, ("mesh", "shot"))),
        check_vma=False,
    )
```

```python
import math

import jax
import jax.numpy as jnp
import numpy as np
from jax import lax
from jax.sharding import PartitionSpec as P

HIGH = lax.Precision.HIGHEST
STEP_SIZE = 0.02


def padded(x, sides, width):
    for axis, dim in sides:
        devices, length = (lax.axis_size(axis), x.shape[dim])
        up = [(i, (i + 1) % devices) for i in range(devices - 1)]
        down = [(j, i) for i, j in up]
        last = lax.slice_in_dim(x, length - width, length, axis=dim)
        first = lax.slice_in_dim(x, 0, width, axis=dim)
        before = lax.ppermute(last, axis, up)
        after = lax.ppermute(first, axis, down)
        x = jnp.concatenate([before, x, after], axis=dim)
    return x


def invert_matrix(matrix):
    order_count = matrix.shape[0]
    working = np.concatenate([matrix * 1.0, np.eye(order_count)], axis=1)
    for column in range(order_count):
        pivot_row = column + int(np.argmax(np.abs(working[column:, column])))
        working[[column, pivot_row]] = working[[pivot_row, column]]
        working[column] = working[column] / working[column, column]
        for target in range(order_count):
            if target != column:
                working[target] = working[target] - working[target, column] * working[column]
    return working[:, order_count:]


def basis_tables():
    points = [
        (across, along, upward)
        for upward in range(5)
        for along in range(5 - upward)
        for across in range(5 - upward - along)
    ]
    exponents = np.array(points) * 1.0
    coords = exponents / 4.0
    vander = np.prod(coords[:, None, :] ** exponents[None, :, :], axis=2)
    inverse = invert_matrix(vander)
    derivs = []
    for direction_axis in range(3):
        lowered = np.maximum(exponents - np.eye(3)[direction_axis], 0.0)
        slopes = exponents[None, :, direction_axis] * np.prod(
            coords[:, None, :] ** lowered[None, :, :], axis=2
        )
        derivs.append(slopes @ inverse)
    moments = np.array(
        [
            [
                math.factorial(first[0] + second[0])
                * math.factorial(first[1] + second[1])
                * math.factorial(first[2] + second[2])
                / math.factorial(sum(first) + sum(second) + 3)
                for second in points
            ]
            for first in points
        ]
    )
    mass_matrix = inverse.T @ moments @ inverse
    lattice = [(across, along) for along in range(5) for across in range(5 - along)]
    lattice_powers = np.array(lattice) * 1.0
    face_vander = np.prod((lattice_powers / 4.0)[:, None, :] ** lattice_powers[None, :, :], axis=2)
    face_inverse = invert_matrix(face_vander)
    face_moments = np.array(
        [
            [
                math.factorial(first[0] + second[0])
                * math.factorial(first[1] + second[1])
                / math.factorial(sum(first) + sum(second) + 2)
                for second in lattice
            ]
            for first in lattice
        ]
    )
    face_mass = face_inverse.T @ face_moments @ face_inverse
    numbers = {point: number for number, point in enumerate(points)}
    face_points = [
        [(across, along, 0) for across, along in lattice],
        [(across, 0, along) for across, along in lattice],
        [(0, across, along) for across, along in lattice],
        [(across, along, 4 - across - along) for across, along in lattice],
    ]
    face_nodes = np.array(
        [[numbers[point] for point in listing] for listing in face_points], np.int32
    )
    mass_inverse = invert_matrix(mass_matrix)
    lift_tables = []
    for face_number in range(4):
        selector = np.eye(35)[face_nodes[face_number]]
        lift_tables.append(mass_inverse @ selector.T @ face_mass)
    orderings = [(0, 1, 2), (1, 2, 0), (2, 0, 1), (1, 0, 2), (0, 2, 1), (2, 1, 0)]
    lattice_numbers = {point: number for number, point in enumerate(lattice)}
    triples = [(across, along, 4 - across - along) for across, along in lattice]
    turn_nodes = np.array(
        [
            [lattice_numbers[triple[ordering[0]], triple[ordering[1]]] for triple in triples]
            for ordering in orderings
        ],
        np.int32,
    )
    return (
        jnp.asarray(np.stack(derivs), jnp.float32),
        jnp.asarray(np.stack(lift_tables), jnp.float32),
        face_nodes,
        turn_nodes,
    )


def spatial_of(field, metric, derivs):
    reference_grads = jnp.einsum("rab,fbe->rfae", derivs, field, precision=HIGH)
    rows = []
    for direction_axis in range(3):
        total = metric[0, direction_axis] * reference_grads[0]
        total = total + metric[1, direction_axis] * reference_grads[1]
        total = total + metric[2, direction_axis] * reference_grads[2]
        rows.append(total)
    return jnp.stack(rows)


def volume_term(adjoint, material, coupling, metric, derivs):
    spatial = spatial_of(adjoint, metric, derivs)
    mixing = jnp.einsum("dpfg,dfae->pgae", coupling, spatial, precision=HIGH)
    return jnp.sum(material[:, None] * mixing, axis=0)


def kernel_term(adjoint, forward, coupling, metric, derivs):
    spatial = spatial_of(forward, metric, derivs)
    mixing = jnp.einsum("dpfg,dgae->pfae", coupling, spatial, precision=HIGH)
    return jnp.sum(mixing * adjoint[None], axis=1)


def surface_term(jump_trace, face_material, face_normals, face_scale, coupling, lift_tables):
    weighted = face_normals[:, None, None] * jump_trace[None]
    mixing = jnp.einsum("dpfg,dfnxe->pgnxe", coupling, weighted, precision=HIGH)
    face_flux = 0.5 * jnp.sum(face_material[:, None] * mixing, axis=0) + 0.5 * jump_trace
    return jnp.einsum(
        "xan,fnxe->fae", lift_tables, face_flux * face_scale[None, None], precision=HIGH
    )


def halving_sum(values, axis, count):
    position = lax.axis_index(axis)
    work = values
    bit = count // 2
    while bit >= 1:
        width = work.shape[-1] // 2
        upper = (position & bit) != 0
        low = work[..., :width]
        high = work[..., width:]
        sent = lax.ppermute(
            jnp.where(upper, low, high), axis, [(i, i ^ bit) for i in range(count)]
        )
        work = jnp.where(upper, high, low) + sent
        bit //= 2
    return work


def search_direction(grad_share, step_share, change_share, gram, combine_sums):
    pairs = step_share.shape[0]
    both_share = jnp.concatenate([step_share, change_share], axis=0)
    with_grad = jnp.sum(both_share * grad_share[None], axis=(1, 2, 3))
    summed = combine_sums(jnp.concatenate([with_grad, gram.reshape(-1)]))
    lanes = 0.0 * step_share[0, 0, :8, :]
    summed = summed[:, None, None] + lanes[None]
    step_grad = summed[:pairs]
    change_grad = summed[pairs : 2 * pairs]
    gram = summed[2 * pairs :].reshape((2 * pairs, pairs) + summed.shape[1:])
    step_change = gram[:pairs]
    change_change = gram[pairs:]
    curvature = [step_change[slot, slot] for slot in range(pairs)]
    alphas = [None] * pairs
    for slot in reversed(range(pairs)):
        projected = step_grad[slot]
        for later in range(slot + 1, pairs):
            projected = projected - alphas[later] * step_change[slot, later]
        alphas[slot] = projected / curvature[slot]
    scaling = curvature[pairs - 1] / change_change[pairs - 1, pairs - 1]
    weights = [None] * pairs
    for slot in range(pairs):
        along = change_grad[slot]
        for other in range(pairs):
            along = along - alphas[other] * change_change[slot, other]
        along = scaling * along
        for earlier in range(slot):
            along = along + weights[earlier] * step_change[earlier, slot]
        beta_now = along / curvature[slot]
        weights[slot] = alphas[slot] - beta_now
    coefficients = jnp.stack(
        [weights[slot] for slot in range(pairs)]
        + [-scaling * alphas[slot] for slot in range(pairs)]
        + [scaling]
    )[:, 0, 0]
    rows = jnp.concatenate([both_share, grad_share[None]], axis=0)
    work = jnp.sum(coefficients[:, None, None, None] * rows, axis=0)
    return -work


def shards(
    adjoint_state,
    forward_states,
    material,
    coupling,
    metric,
    face_normals,
    face_scale,
    face_neighbours,
    face_orientation,
    send_faces,
    history_steps,
    history_changes,
):
    derivs, lift_tables, face_nodes, turn_nodes = basis_tables()
    fields = adjoint_state.shape[1]
    elements = adjoint_state.shape[3]
    node_count = material.shape[1]
    params = material.shape[0]
    face_width = face_nodes.shape[1]
    border = send_faces.shape[0] // 2
    slot_count = 4 * elements + 2 * border
    adjoint = adjoint_state[0]
    face_material = material[:, face_nodes.T, :]
    neighbours = face_neighbours.reshape(-1)
    orient = face_orientation.reshape(-1)
    face_total = 4 * elements
    slot_pick = (
        neighbours[None, :] == jnp.arange(slot_count, dtype=jnp.int32)[:, None]
    ).astype(jnp.float32)
    local_pick = slot_pick[:face_total]
    below_pick = slot_pick[face_total : face_total + border]
    above_pick = slot_pick[face_total + border :]
    send_pick = (
        send_faces[None, :] == jnp.arange(face_total, dtype=jnp.int32)[:, None]
    ).astype(jnp.float32)
    shot_count = lax.axis_size("shot")
    share_width = elements // shot_count
    share_start = lax.axis_index("shot") * share_width

    def own_share(rows):
        return lax.dynamic_slice_in_dim(rows, share_start, share_width, rows.ndim - 1)

    step_share = own_share(history_steps)
    change_share = own_share(history_changes)
    both_share = jnp.concatenate([step_share, change_share], axis=0)
    gram = jnp.sum(both_share[:, None] * change_share[None, :], axis=(2, 3, 4))
    step_share, change_share, gram, adjoint = lax.optimization_barrier(
        (step_share, change_share, gram, adjoint)
    )
    gradient = jnp.zeros((params, node_count, elements), jnp.float32)
    for step_index in range(forward_states.shape[1]):
        inner_trace = adjoint[:, face_nodes.T, :]
        flat_trace = inner_trace.reshape(fields, face_width, 4 * elements)
        sent_traces = jnp.einsum("fns,sj->fnj", flat_trace, send_pick, precision=HIGH)
        extended = padded(sent_traces, (("mesh", 2),), border)
        gathered = jnp.einsum("fns,sj->fnj", flat_trace, local_pick, precision=HIGH)
        gathered = gathered + jnp.einsum(
            "fns,sj->fnj", extended[:, :, :border], below_pick, precision=HIGH
        )
        gathered = gathered + jnp.einsum(
            "fns,sj->fnj", extended[:, :, 3 * border :], above_pick, precision=HIGH
        )
        turned = gathered
        for option in range(turn_nodes.shape[0]):
            turned = jnp.where(
                (orient == option)[None, None, :], gathered[:, turn_nodes[option], :], turned
            )
        jump_trace = turned.reshape(fields, face_width, 4, elements) - inner_trace
        change = volume_term(adjoint, material, coupling, metric, derivs) + surface_term(
            jump_trace, face_material, face_normals, face_scale, coupling, lift_tables
        )
        adjoint = adjoint + STEP_SIZE * change
        gradient = gradient + STEP_SIZE * kernel_term(
            adjoint, forward_states[0, step_index], coupling, metric, derivs
        )
    device_count = shot_count * lax.axis_size("mesh")

    def combine_sums(values):
        spread = jnp.broadcast_to(values[None], (device_count,) + values.shape)
        return jnp.sum(lax.all_to_all(spread, ("shot", "mesh"), 0, 0, tiled=False), axis=0)

    grad_share = halving_sum(gradient, "shot", shot_count)
    result = search_direction(grad_share, step_share, change_share, gram, combine_sums)
    return (adjoint[None], result)


def solution(mesh):
    placed = (
        P("shot", None, None, "mesh"),
        P("shot", None, None, None, "mesh"),
        P(None, None, "mesh"),
        P(),
        P(None, None, "mesh"),
        P(None, None, "mesh"),
        P(None, "mesh"),
        P(None, "mesh"),
        P(None, "mesh"),
        P("mesh"),
        P(None, None, None, "mesh"),
        P(None, None, None, "mesh"),
    )
    return jax.shard_map(
        shards,
        mesh=mesh,
        in_specs=placed,
        out_specs=(P("shot", None, None, "mesh"), P(None, None, ("mesh", "shot"))),
        check_vma=False,
    )
```

```python
import math

import jax
import jax.numpy as jnp
import numpy as np
from jax import lax
from jax.sharding import PartitionSpec as P

HIGH = lax.Precision.HIGHEST
STEP_SIZE = 0.02


def padded(x, sides, width):
    for axis, dim in sides:
        devices, length = (lax.axis_size(axis), x.shape[dim])
        up = [(i, (i + 1) % devices) for i in range(devices - 1)]
        down = [(j, i) for i, j in up]
        last = lax.slice_in_dim(x, length - width, length, axis=dim)
        first = lax.slice_in_dim(x, 0, width, axis=dim)
        before = lax.ppermute(last, axis, up)
        after = lax.ppermute(first, axis, down)
        x = jnp.concatenate([before, x, after], axis=dim)
    return x


def invert_matrix(matrix):
    order_count = matrix.shape[0]
    working = np.concatenate([matrix * 1.0, np.eye(order_count)], axis=1)
    for column in range(order_count):
        pivot_row = column + int(np.argmax(np.abs(working[column:, column])))
        working[[column, pivot_row]] = working[[pivot_row, column]]
        working[column] = working[column] / working[column, column]
        for target in range(order_count):
            if target != column:
                working[target] = working[target] - working[target, column] * working[column]
    return working[:, order_count:]


def basis_tables():
    points = [
        (across, along, upward)
        for upward in range(5)
        for along in range(5 - upward)
        for across in range(5 - upward - along)
    ]
    exponents = np.array(points) * 1.0
    coords = exponents / 4.0
    vander = np.prod(coords[:, None, :] ** exponents[None, :, :], axis=2)
    inverse = invert_matrix(vander)
    derivs = []
    for direction_axis in range(3):
        lowered = np.maximum(exponents - np.eye(3)[direction_axis], 0.0)
        slopes = exponents[None, :, direction_axis] * np.prod(
            coords[:, None, :] ** lowered[None, :, :], axis=2
        )
        derivs.append(slopes @ inverse)
    moments = np.array(
        [
            [
                math.factorial(first[0] + second[0])
                * math.factorial(first[1] + second[1])
                * math.factorial(first[2] + second[2])
                / math.factorial(sum(first) + sum(second) + 3)
                for second in points
            ]
            for first in points
        ]
    )
    mass_matrix = inverse.T @ moments @ inverse
    lattice = [(across, along) for along in range(5) for across in range(5 - along)]
    lattice_powers = np.array(lattice) * 1.0
    face_vander = np.prod((lattice_powers / 4.0)[:, None, :] ** lattice_powers[None, :, :], axis=2)
    face_inverse = invert_matrix(face_vander)
    face_moments = np.array(
        [
            [
                math.factorial(first[0] + second[0])
                * math.factorial(first[1] + second[1])
                / math.factorial(sum(first) + sum(second) + 2)
                for second in lattice
            ]
            for first in lattice
        ]
    )
    face_mass = face_inverse.T @ face_moments @ face_inverse
    numbers = {point: number for number, point in enumerate(points)}
    face_points = [
        [(across, along, 0) for across, along in lattice],
        [(across, 0, along) for across, along in lattice],
        [(0, across, along) for across, along in lattice],
        [(across, along, 4 - across - along) for across, along in lattice],
    ]
    face_nodes = np.array(
        [[numbers[point] for point in listing] for listing in face_points], np.int32
    )
    mass_inverse = invert_matrix(mass_matrix)
    lift_tables = []
    for face_number in range(4):
        selector = np.eye(35)[face_nodes[face_number]]
        lift_tables.append(mass_inverse @ selector.T @ face_mass)
    orderings = [(0, 1, 2), (1, 2, 0), (2, 0, 1), (1, 0, 2), (0, 2, 1), (2, 1, 0)]
    lattice_numbers = {point: number for number, point in enumerate(lattice)}
    triples = [(across, along, 4 - across - along) for across, along in lattice]
    turn_nodes = np.array(
        [
            [lattice_numbers[triple[ordering[0]], triple[ordering[1]]] for triple in triples]
            for ordering in orderings
        ],
        np.int32,
    )
    return (
        jnp.asarray(np.stack(derivs), jnp.float32),
        jnp.asarray(np.stack(lift_tables), jnp.float32),
        face_nodes,
        turn_nodes,
    )


def spatial_of(field, metric, derivs):
    reference_grads = jnp.einsum("rab,fbe->rfae", derivs, field, precision=HIGH)
    rows = []
    for direction_axis in range(3):
        total = metric[0, direction_axis] * reference_grads[0]
        total = total + metric[1, direction_axis] * reference_grads[1]
        total = total + metric[2, direction_axis] * reference_grads[2]
        rows.append(total)
    return jnp.stack(rows)


def volume_term(adjoint, material, coupling, metric, derivs):
    spatial = spatial_of(adjoint, metric, derivs)
    mixing = jnp.einsum("dpfg,dfae->pgae", coupling, spatial, precision=HIGH)
    return jnp.sum(material[:, None] * mixing, axis=0)


def kernel_term(adjoint, forward, coupling, metric, derivs):
    spatial = spatial_of(forward, metric, derivs)
    mixing = jnp.einsum("dpfg,dgae->pfae", coupling, spatial, precision=HIGH)
    return jnp.sum(mixing * adjoint[None], axis=1)


def surface_term(jump_trace, face_material, face_normals, face_scale, coupling, lift_tables):
    weighted = face_normals[:, None, None] * jump_trace[None]
    mixing = jnp.einsum("dpfg,dfnxe->pgnxe", coupling, weighted, precision=HIGH)
    face_flux = 0.5 * jnp.sum(face_material[:, None] * mixing, axis=0) + 0.5 * jump_trace
    return jnp.einsum(
        "xan,fnxe->fae", lift_tables, face_flux * face_scale[None, None], precision=HIGH
    )


def halving_sum(values, axis, count):
    position = lax.axis_index(axis)
    work = values
    bit = count // 2
    while bit >= 1:
        width = work.shape[-1] // 2
        upper = (position & bit) != 0
        low = work[..., :width]
        high = work[..., width:]
        sent = lax.ppermute(
            jnp.where(upper, low, high), axis, [(i, i ^ bit) for i in range(count)]
        )
        work = jnp.where(upper, high, low) + sent
        bit //= 2
    return work


def search_direction(grad_share, step_share, change_share, gram, combine_sums):
    pairs = step_share.shape[0]
    both_share = jnp.concatenate([step_share, change_share], axis=0)
    with_grad = jnp.sum(both_share * grad_share[None], axis=(1, 2, 3))
    summed = combine_sums(jnp.concatenate([with_grad, gram.reshape(-1)]))
    lanes = 0.0 * step_share[0, 0, :8, :]
    summed = summed[:, None, None] + lanes[None]
    step_grad = summed[:pairs]
    change_grad = summed[pairs : 2 * pairs]
    gram = summed[2 * pairs :].reshape((2 * pairs, pairs) + summed.shape[1:])
    step_change = gram[:pairs]
    change_change = gram[pairs:]
    curvature = [step_change[slot, slot] for slot in range(pairs)]
    alphas = [None] * pairs
    for slot in reversed(range(pairs)):
        projected = step_grad[slot]
        for later in range(slot + 1, pairs):
            projected = projected - alphas[later] * step_change[slot, later]
        alphas[slot] = projected / curvature[slot]
    scaling = curvature[pairs - 1] / change_change[pairs - 1, pairs - 1]
    weights = [None] * pairs
    for slot in range(pairs):
        along = change_grad[slot]
        for other in range(pairs):
            along = along - alphas[other] * change_change[slot, other]
        along = scaling * along
        for earlier in range(slot):
            along = along + weights[earlier] * step_change[earlier, slot]
        beta_now = along / curvature[slot]
        weights[slot] = alphas[slot] - beta_now
    coefficients = jnp.stack(
        [weights[slot] for slot in range(pairs)]
        + [-scaling * alphas[slot] for slot in range(pairs)]
        + [scaling]
    )[:, 0, 0]
    rows = jnp.concatenate([both_share, grad_share[None]], axis=0)
    work = jnp.sum(coefficients[:, None, None, None] * rows, axis=0)
    return -work


def shards(
    adjoint_state,
    forward_states,
    material,
    coupling,
    metric,
    face_normals,
    face_scale,
    face_neighbours,
    face_orientation,
    send_faces,
    history_steps,
    history_changes,
):
    derivs, lift_tables, face_nodes, turn_nodes = basis_tables()
    fields = adjoint_state.shape[1]
    elements = adjoint_state.shape[3]
    node_count = material.shape[1]
    params = material.shape[0]
    face_width = face_nodes.shape[1]
    border = send_faces.shape[0] // 2
    slot_count = 4 * elements + 2 * border
    adjoint = adjoint_state[0]
    face_material = material[:, face_nodes.T, :]
    neighbours = face_neighbours.reshape(-1)
    orient = face_orientation.reshape(-1)
    face_total = 4 * elements
    slot_pick = (
        neighbours[None, :] == jnp.arange(slot_count, dtype=jnp.int32)[:, None]
    ).astype(jnp.float32)
    local_pick = slot_pick[:face_total]
    below_pick = slot_pick[face_total : face_total + border]
    above_pick = slot_pick[face_total + border :]
    node_turn = jnp.zeros((face_width, face_width, face_total), jnp.float32)
    for option in range(turn_nodes.shape[0]):
        node_turn = node_turn + (orient == option).astype(jnp.float32)[None, None, :] * jnp.asarray(
            np.eye(face_width, dtype=np.float32)[turn_nodes[option]].T
        )[:, :, None]
    send_pick = (
        send_faces[None, :] == jnp.arange(face_total, dtype=jnp.int32)[:, None]
    ).astype(jnp.float32)
    shot_count = lax.axis_size("shot")
    share_width = elements // shot_count
    share_start = lax.axis_index("shot") * share_width

    def own_share(rows):
        return lax.dynamic_slice_in_dim(rows, share_start, share_width, rows.ndim - 1)

    step_share = own_share(history_steps)
    change_share = own_share(history_changes)
    both_share = jnp.concatenate([step_share, change_share], axis=0)
    gram = jnp.sum(both_share[:, None] * change_share[None, :], axis=(2, 3, 4))
    step_share, change_share, gram, adjoint = lax.optimization_barrier(
        (step_share, change_share, gram, adjoint)
    )
    gradient = jnp.zeros((params, node_count, elements), jnp.float32)
    for step_index in range(forward_states.shape[1]):
        inner_trace = adjoint[:, face_nodes.T, :]
        flat_trace = inner_trace.reshape(fields, face_width, 4 * elements)
        sent_traces = jnp.einsum("fns,sj->fnj", flat_trace, send_pick, precision=HIGH)
        extended = padded(sent_traces, (("mesh", 2),), border)
        gathered = jnp.einsum("fns,sj->fnj", flat_trace, local_pick, precision=HIGH)
        gathered = gathered + jnp.einsum(
            "fns,sj->fnj", extended[:, :, :border], below_pick, precision=HIGH
        )
        gathered = gathered + jnp.einsum(
            "fns,sj->fnj", extended[:, :, 3 * border :], above_pick, precision=HIGH
        )
        turned = jnp.sum(gathered[:, :, None, :] * node_turn[None], axis=1)
        jump_trace = turned.reshape(fields, face_width, 4, elements) - inner_trace
        change = volume_term(adjoint, material, coupling, metric, derivs) + surface_term(
            jump_trace, face_material, face_normals, face_scale, coupling, lift_tables
        )
        adjoint = adjoint + STEP_SIZE * change
        gradient = gradient + STEP_SIZE * kernel_term(
            adjoint, forward_states[0, step_index], coupling, metric, derivs
        )
    device_count = shot_count * lax.axis_size("mesh")

    def combine_sums(values):
        spread = jnp.broadcast_to(values[None], (device_count,) + values.shape)
        return jnp.sum(lax.all_to_all(spread, ("shot", "mesh"), 0, 0, tiled=False), axis=0)

    grad_share = halving_sum(gradient, "shot", shot_count)
    result = search_direction(grad_share, step_share, change_share, gram, combine_sums)
    return (adjoint[None], result)


def solution(mesh):
    placed = (
        P("shot", None, None, "mesh"),
        P("shot", None, None, None, "mesh"),
        P(None, None, "mesh"),
        P(),
        P(None, None, "mesh"),
        P(None, None, "mesh"),
        P(None, "mesh"),
        P(None, "mesh"),
        P(None, "mesh"),
        P("mesh"),
        P(None, None, None, "mesh"),
        P(None, None, None, "mesh"),
    )
    return jax.shard_map(
        shards,
        mesh=mesh,
        in_specs=placed,
        out_specs=(P("shot", None, None, "mesh"), P(None, None, ("mesh", "shot"))),
        check_vma=False,
    )
```

```python
import math

import jax
import jax.numpy as jnp
import numpy as np
from jax import lax
from jax.sharding import PartitionSpec as P

HIGH = lax.Precision.HIGHEST
STEP_SIZE = 0.02


def padded(x, sides, width):
    for axis, dim in sides:
        devices, length = (lax.axis_size(axis), x.shape[dim])
        up = [(i, (i + 1) % devices) for i in range(devices - 1)]
        down = [(j, i) for i, j in up]
        last = lax.slice_in_dim(x, length - width, length, axis=dim)
        first = lax.slice_in_dim(x, 0, width, axis=dim)
        before = lax.ppermute(last, axis, up)
        after = lax.ppermute(first, axis, down)
        x = jnp.concatenate([before, x, after], axis=dim)
    return x


def invert_matrix(matrix):
    order_count = matrix.shape[0]
    working = np.concatenate([matrix * 1.0, np.eye(order_count)], axis=1)
    for column in range(order_count):
        pivot_row = column + int(np.argmax(np.abs(working[column:, column])))
        working[[column, pivot_row]] = working[[pivot_row, column]]
        working[column] = working[column] / working[column, column]
        for target in range(order_count):
            if target != column:
                working[target] = working[target] - working[target, column] * working[column]
    return working[:, order_count:]


def basis_tables():
    points = [
        (across, along, upward)
        for upward in range(5)
        for along in range(5 - upward)
        for across in range(5 - upward - along)
    ]
    exponents = np.array(points) * 1.0
    coords = exponents / 4.0
    vander = np.prod(coords[:, None, :] ** exponents[None, :, :], axis=2)
    inverse = invert_matrix(vander)
    derivs = []
    for direction_axis in range(3):
        lowered = np.maximum(exponents - np.eye(3)[direction_axis], 0.0)
        slopes = exponents[None, :, direction_axis] * np.prod(
            coords[:, None, :] ** lowered[None, :, :], axis=2
        )
        derivs.append(slopes @ inverse)
    moments = np.array(
        [
            [
                math.factorial(first[0] + second[0])
                * math.factorial(first[1] + second[1])
                * math.factorial(first[2] + second[2])
                / math.factorial(sum(first) + sum(second) + 3)
                for second in points
            ]
            for first in points
        ]
    )
    mass_matrix = inverse.T @ moments @ inverse
    lattice = [(across, along) for along in range(5) for across in range(5 - along)]
    lattice_powers = np.array(lattice) * 1.0
    face_vander = np.prod((lattice_powers / 4.0)[:, None, :] ** lattice_powers[None, :, :], axis=2)
    face_inverse = invert_matrix(face_vander)
    face_moments = np.array(
        [
            [
                math.factorial(first[0] + second[0])
                * math.factorial(first[1] + second[1])
                / math.factorial(sum(first) + sum(second) + 2)
                for second in lattice
            ]
            for first in lattice
        ]
    )
    face_mass = face_inverse.T @ face_moments @ face_inverse
    numbers = {point: number for number, point in enumerate(points)}
    face_points = [
        [(across, along, 0) for across, along in lattice],
        [(across, 0, along) for across, along in lattice],
        [(0, across, along) for across, along in lattice],
        [(across, along, 4 - across - along) for across, along in lattice],
    ]
    face_nodes = np.array(
        [[numbers[point] for point in listing] for listing in face_points], np.int32
    )
    mass_inverse = invert_matrix(mass_matrix)
    lift_tables = []
    for face_number in range(4):
        selector = np.eye(35)[face_nodes[face_number]]
        lift_tables.append(mass_inverse @ selector.T @ face_mass)
    orderings = [(0, 1, 2), (1, 2, 0), (2, 0, 1), (1, 0, 2), (0, 2, 1), (2, 1, 0)]
    lattice_numbers = {point: number for number, point in enumerate(lattice)}
    triples = [(across, along, 4 - across - along) for across, along in lattice]
    turn_nodes = np.array(
        [
            [lattice_numbers[triple[ordering[0]], triple[ordering[1]]] for triple in triples]
            for ordering in orderings
        ],
        np.int32,
    )
    return (
        jnp.asarray(np.stack(derivs), jnp.float32),
        jnp.asarray(np.stack(lift_tables), jnp.float32),
        face_nodes,
        turn_nodes,
    )


def spatial_of(field, metric, derivs):
    reference_grads = jnp.einsum("rab,fbe->rfae", derivs, field, precision=HIGH)
    rows = []
    for direction_axis in range(3):
        total = metric[0, direction_axis] * reference_grads[0]
        total = total + metric[1, direction_axis] * reference_grads[1]
        total = total + metric[2, direction_axis] * reference_grads[2]
        rows.append(total)
    return jnp.stack(rows)


def volume_term(adjoint, material, coupling, metric, derivs):
    spatial = spatial_of(adjoint, metric, derivs)
    mixing = jnp.einsum("dpfg,dfae->pgae", coupling, spatial, precision=HIGH)
    return jnp.sum(material[:, None] * mixing, axis=0)


def kernel_term(adjoint, forward, coupling, metric, derivs):
    spatial = spatial_of(forward, metric, derivs)
    mixing = jnp.einsum("dpfg,dgae->pfae", coupling, spatial, precision=HIGH)
    return jnp.sum(mixing * adjoint[None], axis=1)


def surface_term(jump_trace, face_material, face_normals, face_scale, coupling, lift_tables):
    weighted = face_normals[:, None, None] * jump_trace[None]
    mixing = jnp.einsum("dpfg,dfnxe->pgnxe", coupling, weighted, precision=HIGH)
    face_flux = 0.5 * jnp.sum(face_material[:, None] * mixing, axis=0) + 0.5 * jump_trace
    return jnp.einsum(
        "xan,fnxe->fae", lift_tables, face_flux * face_scale[None, None], precision=HIGH
    )


def halving_sum(values, axis, count):
    position = lax.axis_index(axis)
    work = values
    bit = count // 2
    while bit >= 1:
        width = work.shape[-1] // 2
        upper = (position & bit) != 0
        low = work[..., :width]
        high = work[..., width:]
        sent = lax.ppermute(
            jnp.where(upper, low, high), axis, [(i, i ^ bit) for i in range(count)]
        )
        work = jnp.where(upper, high, low) + sent
        bit //= 2
    return work


def search_direction(grad_share, local_grad, both_rows, step_share, change_share, gram, combine_sums):
    pairs = step_share.shape[0]
    both_share = jnp.concatenate([step_share, change_share], axis=0)
    with_grad = jnp.sum(both_rows * local_grad[None], axis=(1, 2, 3))
    summed = combine_sums(jnp.concatenate([with_grad, gram.reshape(-1)]))
    lanes = 0.0 * step_share[0, 0, :8, :]
    summed = summed[:, None, None] + lanes[None]
    step_grad = summed[:pairs]
    change_grad = summed[pairs : 2 * pairs]
    gram = summed[2 * pairs :].reshape((2 * pairs, pairs) + summed.shape[1:])
    step_change = gram[:pairs]
    change_change = gram[pairs:]
    curvature = [step_change[slot, slot] for slot in range(pairs)]
    alphas = [None] * pairs
    for slot in reversed(range(pairs)):
        projected = step_grad[slot]
        for later in range(slot + 1, pairs):
            projected = projected - alphas[later] * step_change[slot, later]
        alphas[slot] = projected / curvature[slot]
    scaling = curvature[pairs - 1] / change_change[pairs - 1, pairs - 1]
    weights = [None] * pairs
    for slot in range(pairs):
        along = change_grad[slot]
        for other in range(pairs):
            along = along - alphas[other] * change_change[slot, other]
        along = scaling * along
        for earlier in range(slot):
            along = along + weights[earlier] * step_change[earlier, slot]
        beta_now = along / curvature[slot]
        weights[slot] = alphas[slot] - beta_now
    coefficients = jnp.stack(
        [weights[slot] for slot in range(pairs)]
        + [-scaling * alphas[slot] for slot in range(pairs)]
        + [scaling]
    )[:, 0, 0]
    rows = jnp.concatenate([both_share, grad_share[None]], axis=0)
    work = jnp.sum(coefficients[:, None, None, None] * rows, axis=0)
    return -work


def shards(
    adjoint_state,
    forward_states,
    material,
    coupling,
    metric,
    face_normals,
    face_scale,
    face_neighbours,
    face_orientation,
    send_faces,
    history_steps,
    history_changes,
):
    derivs, lift_tables, face_nodes, turn_nodes = basis_tables()
    fields = adjoint_state.shape[1]
    elements = adjoint_state.shape[3]
    node_count = material.shape[1]
    params = material.shape[0]
    face_width = face_nodes.shape[1]
    border = send_faces.shape[0] // 2
    slot_count = 4 * elements + 2 * border
    adjoint = adjoint_state[0]
    face_material = material[:, face_nodes.T, :]
    neighbours = face_neighbours.reshape(-1)
    orient = face_orientation.reshape(-1)
    face_total = 4 * elements
    slot_pick = (
        neighbours[None, :] == jnp.arange(slot_count, dtype=jnp.int32)[:, None]
    ).astype(jnp.float32)
    local_pick = slot_pick[:face_total]
    below_pick = slot_pick[face_total : face_total + border]
    above_pick = slot_pick[face_total + border :]
    node_turn = jnp.zeros((face_width, face_width, face_total), jnp.float32)
    for option in range(turn_nodes.shape[0]):
        node_turn = node_turn + (orient == option).astype(jnp.float32)[None, None, :] * jnp.asarray(
            np.eye(face_width, dtype=np.float32)[turn_nodes[option]].T
        )[:, :, None]
    send_pick = (
        send_faces[None, :] == jnp.arange(face_total, dtype=jnp.int32)[:, None]
    ).astype(jnp.float32)
    shot_count = lax.axis_size("shot")
    share_width = elements // shot_count
    share_start = lax.axis_index("shot") * share_width

    def own_share(rows):
        return lax.dynamic_slice_in_dim(rows, share_start, share_width, rows.ndim - 1)

    step_share = own_share(history_steps)
    change_share = own_share(history_changes)
    both_share = jnp.concatenate([step_share, change_share], axis=0)
    gram = jnp.sum(both_share[:, None] * change_share[None, :], axis=(2, 3, 4))
    both_rows = jnp.concatenate([history_steps, history_changes], axis=0)
    both_rows, step_share, change_share, gram, adjoint = lax.optimization_barrier(
        (both_rows, step_share, change_share, gram, adjoint)
    )
    gradient = jnp.zeros((params, node_count, elements), jnp.float32)
    for step_index in range(forward_states.shape[1]):
        inner_trace = adjoint[:, face_nodes.T, :]
        flat_trace = inner_trace.reshape(fields, face_width, 4 * elements)
        sent_traces = jnp.einsum("fns,sj->fnj", flat_trace, send_pick, precision=HIGH)
        extended = padded(sent_traces, (("mesh", 2),), border)
        gathered = jnp.einsum("fns,sj->fnj", flat_trace, local_pick, precision=HIGH)
        gathered = gathered + jnp.einsum(
            "fns,sj->fnj", extended[:, :, :border], below_pick, precision=HIGH
        )
        gathered = gathered + jnp.einsum(
            "fns,sj->fnj", extended[:, :, 3 * border :], above_pick, precision=HIGH
        )
        turned = jnp.sum(gathered[:, :, None, :] * node_turn[None], axis=1)
        jump_trace = turned.reshape(fields, face_width, 4, elements) - inner_trace
        change = volume_term(adjoint, material, coupling, metric, derivs) + surface_term(
            jump_trace, face_material, face_normals, face_scale, coupling, lift_tables
        )
        adjoint = adjoint + STEP_SIZE * change
        gradient = gradient + STEP_SIZE * kernel_term(
            adjoint, forward_states[0, step_index], coupling, metric, derivs
        )
    device_count = shot_count * lax.axis_size("mesh")

    def combine_sums(values):
        spread = jnp.broadcast_to(values[None], (device_count,) + values.shape)
        return jnp.sum(lax.all_to_all(spread, ("shot", "mesh"), 0, 0, tiled=False), axis=0)

    grad_share = halving_sum(gradient, "shot", shot_count)
    result = search_direction(
        grad_share, gradient, both_rows, step_share, change_share, gram, combine_sums
    )
    return (adjoint[None], result)


def solution(mesh):
    placed = (
        P("shot", None, None, "mesh"),
        P("shot", None, None, None, "mesh"),
        P(None, None, "mesh"),
        P(),
        P(None, None, "mesh"),
        P(None, None, "mesh"),
        P(None, "mesh"),
        P(None, "mesh"),
        P(None, "mesh"),
        P("mesh"),
        P(None, None, None, "mesh"),
        P(None, None, None, "mesh"),
    )
    return jax.shard_map(
        shards,
        mesh=mesh,
        in_specs=placed,
        out_specs=(P("shot", None, None, "mesh"), P(None, None, ("mesh", "shot"))),
        check_vma=False,
    )
```

```python
import math

import jax
import jax.numpy as jnp
import numpy as np
from jax import lax
from jax.sharding import PartitionSpec as P

HIGH = lax.Precision.HIGHEST
MIX = lax.Precision.HIGH
STEP_SIZE = 0.02


def padded(x, sides, width):
    for axis, dim in sides:
        devices, length = (lax.axis_size(axis), x.shape[dim])
        up = [(i, (i + 1) % devices) for i in range(devices - 1)]
        down = [(j, i) for i, j in up]
        last = lax.slice_in_dim(x, length - width, length, axis=dim)
        first = lax.slice_in_dim(x, 0, width, axis=dim)
        before = lax.ppermute(last, axis, up)
        after = lax.ppermute(first, axis, down)
        x = jnp.concatenate([before, x, after], axis=dim)
    return x


def invert_matrix(matrix):
    order_count = matrix.shape[0]
    working = np.concatenate([matrix * 1.0, np.eye(order_count)], axis=1)
    for column in range(order_count):
        pivot_row = column + int(np.argmax(np.abs(working[column:, column])))
        working[[column, pivot_row]] = working[[pivot_row, column]]
        working[column] = working[column] / working[column, column]
        for target in range(order_count):
            if target != column:
                working[target] = working[target] - working[target, column] * working[column]
    return working[:, order_count:]


def basis_tables():
    points = [
        (across, along, upward)
        for upward in range(5)
        for along in range(5 - upward)
        for across in range(5 - upward - along)
    ]
    exponents = np.array(points) * 1.0
    coords = exponents / 4.0
    vander = np.prod(coords[:, None, :] ** exponents[None, :, :], axis=2)
    inverse = invert_matrix(vander)
    derivs = []
    for direction_axis in range(3):
        lowered = np.maximum(exponents - np.eye(3)[direction_axis], 0.0)
        slopes = exponents[None, :, direction_axis] * np.prod(
            coords[:, None, :] ** lowered[None, :, :], axis=2
        )
        derivs.append(slopes @ inverse)
    moments = np.array(
        [
            [
                math.factorial(first[0] + second[0])
                * math.factorial(first[1] + second[1])
                * math.factorial(first[2] + second[2])
                / math.factorial(sum(first) + sum(second) + 3)
                for second in points
            ]
            for first in points
        ]
    )
    mass_matrix = inverse.T @ moments @ inverse
    lattice = [(across, along) for along in range(5) for across in range(5 - along)]
    lattice_powers = np.array(lattice) * 1.0
    face_vander = np.prod((lattice_powers / 4.0)[:, None, :] ** lattice_powers[None, :, :], axis=2)
    face_inverse = invert_matrix(face_vander)
    face_moments = np.array(
        [
            [
                math.factorial(first[0] + second[0])
                * math.factorial(first[1] + second[1])
                / math.factorial(sum(first) + sum(second) + 2)
                for second in lattice
            ]
            for first in lattice
        ]
    )
    face_mass = face_inverse.T @ face_moments @ face_inverse
    numbers = {point: number for number, point in enumerate(points)}
    face_points = [
        [(across, along, 0) for across, along in lattice],
        [(across, 0, along) for across, along in lattice],
        [(0, across, along) for across, along in lattice],
        [(across, along, 4 - across - along) for across, along in lattice],
    ]
    face_nodes = np.array(
        [[numbers[point] for point in listing] for listing in face_points], np.int32
    )
    mass_inverse = invert_matrix(mass_matrix)
    lift_tables = []
    for face_number in range(4):
        selector = np.eye(35)[face_nodes[face_number]]
        lift_tables.append(mass_inverse @ selector.T @ face_mass)
    orderings = [(0, 1, 2), (1, 2, 0), (2, 0, 1), (1, 0, 2), (0, 2, 1), (2, 1, 0)]
    lattice_numbers = {point: number for number, point in enumerate(lattice)}
    triples = [(across, along, 4 - across - along) for across, along in lattice]
    turn_nodes = np.array(
        [
            [lattice_numbers[triple[ordering[0]], triple[ordering[1]]] for triple in triples]
            for ordering in orderings
        ],
        np.int32,
    )
    return (
        jnp.asarray(np.stack(derivs), jnp.float32),
        jnp.asarray(np.stack(lift_tables), jnp.float32),
        face_nodes,
        turn_nodes,
    )


def spatial_of(field, metric, derivs):
    reference_grads = jnp.einsum("rab,fbe->rfae", derivs, field, precision=MIX)
    rows = []
    for direction_axis in range(3):
        total = metric[0, direction_axis] * reference_grads[0]
        total = total + metric[1, direction_axis] * reference_grads[1]
        total = total + metric[2, direction_axis] * reference_grads[2]
        rows.append(total)
    return jnp.stack(rows)


def volume_term(adjoint, material, coupling, metric, derivs):
    spatial = spatial_of(adjoint, metric, derivs)
    mixing = jnp.einsum("dpfg,dfae->pgae", coupling, spatial, precision=MIX)
    return jnp.sum(material[:, None] * mixing, axis=0)


def kernel_term(adjoint, forward, coupling, metric, derivs):
    spatial = spatial_of(forward, metric, derivs)
    mixing = jnp.einsum("dpfg,dgae->pfae", coupling, spatial, precision=MIX)
    return jnp.sum(mixing * adjoint[None], axis=1)


def surface_term(jump_trace, face_material, face_normals, face_scale, coupling, lift_tables):
    weighted = face_normals[:, None, None] * jump_trace[None]
    mixing = jnp.einsum("dpfg,dfnxe->pgnxe", coupling, weighted, precision=MIX)
    face_flux = 0.5 * jnp.sum(face_material[:, None] * mixing, axis=0) + 0.5 * jump_trace
    return jnp.einsum(
        "xan,fnxe->fae", lift_tables, face_flux * face_scale[None, None], precision=MIX
    )


def halving_sum(values, axis, count):
    position = lax.axis_index(axis)
    work = values
    bit = count // 2
    while bit >= 1:
        width = work.shape[-1] // 2
        upper = (position & bit) != 0
        low = work[..., :width]
        high = work[..., width:]
        sent = lax.ppermute(
            jnp.where(upper, low, high), axis, [(i, i ^ bit) for i in range(count)]
        )
        work = jnp.where(upper, high, low) + sent
        bit //= 2
    return work


def search_direction(grad_share, step_share, change_share, gram, combine_sums):
    pairs = step_share.shape[0]
    both_share = jnp.concatenate([step_share, change_share], axis=0)
    with_grad = jnp.sum(both_share * grad_share[None], axis=(1, 2, 3))
    summed = combine_sums(jnp.concatenate([with_grad, gram.reshape(-1)]))
    lanes = 0.0 * step_share[0, 0, :8, :]
    summed = summed[:, None, None] + lanes[None]
    step_grad = summed[:pairs]
    change_grad = summed[pairs : 2 * pairs]
    gram = summed[2 * pairs :].reshape((2 * pairs, pairs) + summed.shape[1:])
    step_change = gram[:pairs]
    change_change = gram[pairs:]
    curvature = [step_change[slot, slot] for slot in range(pairs)]
    alphas = [None] * pairs
    for slot in reversed(range(pairs)):
        projected = step_grad[slot]
        for later in range(slot + 1, pairs):
            projected = projected - alphas[later] * step_change[slot, later]
        alphas[slot] = projected / curvature[slot]
    scaling = curvature[pairs - 1] / change_change[pairs - 1, pairs - 1]
    weights = [None] * pairs
    for slot in range(pairs):
        along = change_grad[slot]
        for other in range(pairs):
            along = along - alphas[other] * change_change[slot, other]
        along = scaling * along
        for earlier in range(slot):
            along = along + weights[earlier] * step_change[earlier, slot]
        beta_now = along / curvature[slot]
        weights[slot] = alphas[slot] - beta_now
    coefficients = jnp.stack(
        [weights[slot] for slot in range(pairs)]
        + [-scaling * alphas[slot] for slot in range(pairs)]
        + [scaling]
    )[:, 0, 0]
    rows = jnp.concatenate([both_share, grad_share[None]], axis=0)
    work = jnp.sum(coefficients[:, None, None, None] * rows, axis=0)
    return -work


def shards(
    adjoint_state,
    forward_states,
    material,
    coupling,
    metric,
    face_normals,
    face_scale,
    face_neighbours,
    face_orientation,
    send_faces,
    history_steps,
    history_changes,
):
    derivs, lift_tables, face_nodes, turn_nodes = basis_tables()
    fields = adjoint_state.shape[1]
    elements = adjoint_state.shape[3]
    node_count = material.shape[1]
    params = material.shape[0]
    face_width = face_nodes.shape[1]
    border = send_faces.shape[0] // 2
    slot_count = 4 * elements + 2 * border
    adjoint = adjoint_state[0]
    face_material = material[:, face_nodes.T, :]
    neighbours = face_neighbours.reshape(-1)
    orient = face_orientation.reshape(-1)
    face_total = 4 * elements
    slot_pick = (
        neighbours[None, :] == jnp.arange(slot_count, dtype=jnp.int32)[:, None]
    ).astype(jnp.float32)
    local_pick = slot_pick[:face_total]
    below_pick = slot_pick[face_total : face_total + border]
    above_pick = slot_pick[face_total + border :]
    node_turn = jnp.zeros((face_width, face_width, face_total), jnp.float32)
    for option in range(turn_nodes.shape[0]):
        node_turn = node_turn + (orient == option).astype(jnp.float32)[None, None, :] * jnp.asarray(
            np.eye(face_width, dtype=np.float32)[turn_nodes[option]].T
        )[:, :, None]
    send_pick = (
        send_faces[None, :] == jnp.arange(face_total, dtype=jnp.int32)[:, None]
    ).astype(jnp.float32)
    shot_count = lax.axis_size("shot")
    share_width = elements // shot_count
    share_start = lax.axis_index("shot") * share_width

    def own_share(rows):
        return lax.dynamic_slice_in_dim(rows, share_start, share_width, rows.ndim - 1)

    step_share = own_share(history_steps)
    change_share = own_share(history_changes)
    both_share = jnp.concatenate([step_share, change_share], axis=0)
    gram = jnp.sum(both_share[:, None] * change_share[None, :], axis=(2, 3, 4))
    step_share, change_share, gram, adjoint = lax.optimization_barrier(
        (step_share, change_share, gram, adjoint)
    )
    gradient = jnp.zeros((params, node_count, elements), jnp.float32)
    for step_index in range(forward_states.shape[1]):
        inner_trace = adjoint[:, face_nodes.T, :]
        flat_trace = inner_trace.reshape(fields, face_width, 4 * elements)
        sent_traces = jnp.einsum("fns,sj->fnj", flat_trace, send_pick, precision=HIGH)
        extended = padded(sent_traces, (("mesh", 2),), border)
        gathered = jnp.einsum("fns,sj->fnj", flat_trace, local_pick, precision=HIGH)
        gathered = gathered + jnp.einsum(
            "fns,sj->fnj", extended[:, :, :border], below_pick, precision=HIGH
        )
        gathered = gathered + jnp.einsum(
            "fns,sj->fnj", extended[:, :, 3 * border :], above_pick, precision=HIGH
        )
        turned = jnp.sum(gathered[:, :, None, :] * node_turn[None], axis=1)
        jump_trace = turned.reshape(fields, face_width, 4, elements) - inner_trace
        change = volume_term(adjoint, material, coupling, metric, derivs) + surface_term(
            jump_trace, face_material, face_normals, face_scale, coupling, lift_tables
        )
        adjoint = adjoint + STEP_SIZE * change
        gradient = gradient + STEP_SIZE * kernel_term(
            adjoint, forward_states[0, step_index], coupling, metric, derivs
        )
    device_count = shot_count * lax.axis_size("mesh")

    def combine_sums(values):
        spread = jnp.broadcast_to(values[None], (device_count,) + values.shape)
        return jnp.sum(lax.all_to_all(spread, ("shot", "mesh"), 0, 0, tiled=False), axis=0)

    grad_share = halving_sum(gradient, "shot", shot_count)
    result = search_direction(grad_share, step_share, change_share, gram, combine_sums)
    return (adjoint[None], result)


def solution(mesh):
    placed = (
        P("shot", None, None, "mesh"),
        P("shot", None, None, None, "mesh"),
        P(None, None, "mesh"),
        P(),
        P(None, None, "mesh"),
        P(None, None, "mesh"),
        P(None, "mesh"),
        P(None, "mesh"),
        P(None, "mesh"),
        P("mesh"),
        P(None, None, None, "mesh"),
        P(None, None, None, "mesh"),
    )
    return jax.shard_map(
        shards,
        mesh=mesh,
        in_specs=placed,
        out_specs=(P("shot", None, None, "mesh"), P(None, None, ("mesh", "shot"))),
        check_vma=False,
    )
```

```python
import math

import jax
import jax.numpy as jnp
import numpy as np
from jax import lax
from jax.sharding import PartitionSpec as P

HIGH = lax.Precision.HIGHEST
MIX = lax.Precision.HIGH
STEP_SIZE = 0.02


def padded(x, sides, width):
    for axis, dim in sides:
        devices, length = (lax.axis_size(axis), x.shape[dim])
        up = [(i, (i + 1) % devices) for i in range(devices - 1)]
        down = [(j, i) for i, j in up]
        last = lax.slice_in_dim(x, length - width, length, axis=dim)
        first = lax.slice_in_dim(x, 0, width, axis=dim)
        before = lax.ppermute(last, axis, up)
        after = lax.ppermute(first, axis, down)
        x = jnp.concatenate([before, x, after], axis=dim)
    return x


def invert_matrix(matrix):
    order_count = matrix.shape[0]
    working = np.concatenate([matrix * 1.0, np.eye(order_count)], axis=1)
    for column in range(order_count):
        pivot_row = column + int(np.argmax(np.abs(working[column:, column])))
        working[[column, pivot_row]] = working[[pivot_row, column]]
        working[column] = working[column] / working[column, column]
        for target in range(order_count):
            if target != column:
                working[target] = working[target] - working[target, column] * working[column]
    return working[:, order_count:]


def basis_tables():
    points = [
        (across, along, upward)
        for upward in range(5)
        for along in range(5 - upward)
        for across in range(5 - upward - along)
    ]
    exponents = np.array(points) * 1.0
    coords = exponents / 4.0
    vander = np.prod(coords[:, None, :] ** exponents[None, :, :], axis=2)
    inverse = invert_matrix(vander)
    derivs = []
    for direction_axis in range(3):
        lowered = np.maximum(exponents - np.eye(3)[direction_axis], 0.0)
        slopes = exponents[None, :, direction_axis] * np.prod(
            coords[:, None, :] ** lowered[None, :, :], axis=2
        )
        derivs.append(slopes @ inverse)
    moments = np.array(
        [
            [
                math.factorial(first[0] + second[0])
                * math.factorial(first[1] + second[1])
                * math.factorial(first[2] + second[2])
                / math.factorial(sum(first) + sum(second) + 3)
                for second in points
            ]
            for first in points
        ]
    )
    mass_matrix = inverse.T @ moments @ inverse
    lattice = [(across, along) for along in range(5) for across in range(5 - along)]
    lattice_powers = np.array(lattice) * 1.0
    face_vander = np.prod((lattice_powers / 4.0)[:, None, :] ** lattice_powers[None, :, :], axis=2)
    face_inverse = invert_matrix(face_vander)
    face_moments = np.array(
        [
            [
                math.factorial(first[0] + second[0])
                * math.factorial(first[1] + second[1])
                / math.factorial(sum(first) + sum(second) + 2)
                for second in lattice
            ]
            for first in lattice
        ]
    )
    face_mass = face_inverse.T @ face_moments @ face_inverse
    numbers = {point: number for number, point in enumerate(points)}
    face_points = [
        [(across, along, 0) for across, along in lattice],
        [(across, 0, along) for across, along in lattice],
        [(0, across, along) for across, along in lattice],
        [(across, along, 4 - across - along) for across, along in lattice],
    ]
    face_nodes = np.array(
        [[numbers[point] for point in listing] for listing in face_points], np.int32
    )
    mass_inverse = invert_matrix(mass_matrix)
    lift_tables = []
    for face_number in range(4):
        selector = np.eye(35)[face_nodes[face_number]]
        lift_tables.append(mass_inverse @ selector.T @ face_mass)
    orderings = [(0, 1, 2), (1, 2, 0), (2, 0, 1), (1, 0, 2), (0, 2, 1), (2, 1, 0)]
    lattice_numbers = {point: number for number, point in enumerate(lattice)}
    triples = [(across, along, 4 - across - along) for across, along in lattice]
    turn_nodes = np.array(
        [
            [lattice_numbers[triple[ordering[0]], triple[ordering[1]]] for triple in triples]
            for ordering in orderings
        ],
        np.int32,
    )
    return (
        jnp.asarray(np.stack(derivs), jnp.float32),
        jnp.asarray(np.stack(lift_tables), jnp.float32),
        face_nodes,
        turn_nodes,
    )


def spatial_of(field, metric, derivs):
    reference_grads = jnp.einsum("rab,fbe->rfae", derivs, field, precision=MIX)
    rows = []
    for direction_axis in range(3):
        total = metric[0, direction_axis] * reference_grads[0]
        total = total + metric[1, direction_axis] * reference_grads[1]
        total = total + metric[2, direction_axis] * reference_grads[2]
        rows.append(total)
    return jnp.stack(rows)


def volume_term(adjoint, material, coupling, metric, derivs):
    spatial = spatial_of(adjoint, metric, derivs)
    mixing = jnp.einsum("dpfg,dfae->pgae", coupling, spatial, precision=MIX)
    return jnp.sum(material[:, None] * mixing, axis=0)


def kernel_term(adjoint, forward, coupling, metric, derivs):
    spatial = spatial_of(forward, metric, derivs)
    mixing = jnp.einsum("dpfg,dgae->pfae", coupling, spatial, precision=MIX)
    return jnp.sum(mixing * adjoint[None], axis=1)


def surface_term(jump_trace, face_material, face_normals, face_scale, coupling, lift_tables):
    weighted = face_normals[:, None, None] * jump_trace[None]
    mixing = jnp.einsum("dpfg,dfnxe->pgnxe", coupling, weighted, precision=MIX)
    face_flux = 0.5 * jnp.sum(face_material[:, None] * mixing, axis=0) + 0.5 * jump_trace
    return jnp.einsum(
        "xan,fnxe->fae", lift_tables, face_flux * face_scale[None, None], precision=MIX
    )


def halving_sum(values, axis, count):
    position = lax.axis_index(axis)
    work = values
    bit = count // 2
    while bit >= 1:
        width = work.shape[-1] // 2
        upper = (position & bit) != 0
        low = work[..., :width]
        high = work[..., width:]
        sent = lax.ppermute(
            jnp.where(upper, low, high), axis, [(i, i ^ bit) for i in range(count)]
        )
        work = jnp.where(upper, high, low) + sent
        bit //= 2
    return work


def search_direction(grad_share, step_share, change_share, gram, combine_sums):
    pairs = step_share.shape[0]
    both_share = jnp.concatenate([step_share, change_share], axis=0)
    with_grad = jnp.sum(both_share * grad_share[None], axis=(1, 2, 3))
    summed = combine_sums(jnp.concatenate([with_grad, gram.reshape(-1)]))
    lanes = 0.0 * step_share[0, 0, :8, :]
    summed = summed[:, None, None] + lanes[None]
    step_grad = summed[:pairs]
    change_grad = summed[pairs : 2 * pairs]
    gram = summed[2 * pairs :].reshape((2 * pairs, pairs) + summed.shape[1:])
    step_change = gram[:pairs]
    change_change = gram[pairs:]
    curvature = [step_change[slot, slot] for slot in range(pairs)]
    alphas = [None] * pairs
    for slot in reversed(range(pairs)):
        projected = step_grad[slot]
        for later in range(slot + 1, pairs):
            projected = projected - alphas[later] * step_change[slot, later]
        alphas[slot] = projected / curvature[slot]
    scaling = curvature[pairs - 1] / change_change[pairs - 1, pairs - 1]
    weights = [None] * pairs
    for slot in range(pairs):
        along = change_grad[slot]
        for other in range(pairs):
            along = along - alphas[other] * change_change[slot, other]
        along = scaling * along
        for earlier in range(slot):
            along = along + weights[earlier] * step_change[earlier, slot]
        beta_now = along / curvature[slot]
        weights[slot] = alphas[slot] - beta_now
    coefficients = jnp.stack(
        [weights[slot] for slot in range(pairs)]
        + [-scaling * alphas[slot] for slot in range(pairs)]
        + [scaling]
    )[:, 0, 0]
    rows = jnp.concatenate([both_share, grad_share[None]], axis=0)
    work = jnp.sum(coefficients[:, None, None, None] * rows, axis=0)
    return -work


def shards(
    adjoint_state,
    forward_states,
    material,
    coupling,
    metric,
    face_normals,
    face_scale,
    face_neighbours,
    face_orientation,
    send_faces,
    history_steps,
    history_changes,
):
    derivs, lift_tables, face_nodes, turn_nodes = basis_tables()
    fields = adjoint_state.shape[1]
    elements = adjoint_state.shape[3]
    node_count = material.shape[1]
    params = material.shape[0]
    face_width = face_nodes.shape[1]
    border = send_faces.shape[0] // 2
    slot_count = 4 * elements + 2 * border
    adjoint = adjoint_state[0]
    node_select = jnp.asarray(np.eye(node_count, dtype=np.float32)[face_nodes.T.reshape(-1)])
    face_material = jnp.einsum(
        "ma,pae->pme", node_select, material, precision=HIGH
    ).reshape(params, face_width, 4, elements)
    neighbours = face_neighbours.reshape(-1)
    orient = face_orientation.reshape(-1)
    face_total = 4 * elements
    slot_pick = (
        neighbours[None, :] == jnp.arange(slot_count, dtype=jnp.int32)[:, None]
    ).astype(jnp.float32)
    local_pick = slot_pick[:face_total]
    below_pick = slot_pick[face_total : face_total + border]
    above_pick = slot_pick[face_total + border :]
    node_turn = jnp.zeros((face_width, face_width, face_total), jnp.float32)
    for option in range(turn_nodes.shape[0]):
        node_turn = node_turn + (orient == option).astype(jnp.float32)[None, None, :] * jnp.asarray(
            np.eye(face_width, dtype=np.float32)[turn_nodes[option]].T
        )[:, :, None]
    send_pick = (
        send_faces[None, :] == jnp.arange(face_total, dtype=jnp.int32)[:, None]
    ).astype(jnp.float32)
    shot_count = lax.axis_size("shot")
    share_width = elements // shot_count
    share_start = lax.axis_index("shot") * share_width

    def own_share(rows):
        return lax.dynamic_slice_in_dim(rows, share_start, share_width, rows.ndim - 1)

    step_share = own_share(history_steps)
    change_share = own_share(history_changes)
    both_share = jnp.concatenate([step_share, change_share], axis=0)
    gram = jnp.sum(both_share[:, None] * change_share[None, :], axis=(2, 3, 4))
    step_share, change_share, gram, adjoint = lax.optimization_barrier(
        (step_share, change_share, gram, adjoint)
    )
    gradient = jnp.zeros((params, node_count, elements), jnp.float32)
    for step_index in range(forward_states.shape[1]):
        inner_trace = jnp.einsum(
            "ma,fae->fme", node_select, adjoint, precision=HIGH
        ).reshape(fields, face_width, 4, elements)
        flat_trace = inner_trace.reshape(fields, face_width, 4 * elements)
        sent_traces = jnp.einsum("fns,sj->fnj", flat_trace, send_pick, precision=HIGH)
        extended = padded(sent_traces, (("mesh", 2),), border)
        gathered = jnp.einsum("fns,sj->fnj", flat_trace, local_pick, precision=HIGH)
        gathered = gathered + jnp.einsum(
            "fns,sj->fnj", extended[:, :, :border], below_pick, precision=HIGH
        )
        gathered = gathered + jnp.einsum(
            "fns,sj->fnj", extended[:, :, 3 * border :], above_pick, precision=HIGH
        )
        turned = jnp.sum(gathered[:, :, None, :] * node_turn[None], axis=1)
        jump_trace = turned.reshape(fields, face_width, 4, elements) - inner_trace
        change = volume_term(adjoint, material, coupling, metric, derivs) + surface_term(
            jump_trace, face_material, face_normals, face_scale, coupling, lift_tables
        )
        adjoint = adjoint + STEP_SIZE * change
        gradient = gradient + STEP_SIZE * kernel_term(
            adjoint, forward_states[0, step_index], coupling, metric, derivs
        )
    device_count = shot_count * lax.axis_size("mesh")

    def combine_sums(values):
        spread = jnp.broadcast_to(values[None], (device_count,) + values.shape)
        return jnp.sum(lax.all_to_all(spread, ("shot", "mesh"), 0, 0, tiled=False), axis=0)

    grad_share = halving_sum(gradient, "shot", shot_count)
    result = search_direction(grad_share, step_share, change_share, gram, combine_sums)
    return (adjoint[None], result)


def solution(mesh):
    placed = (
        P("shot", None, None, "mesh"),
        P("shot", None, None, None, "mesh"),
        P(None, None, "mesh"),
        P(),
        P(None, None, "mesh"),
        P(None, None, "mesh"),
        P(None, "mesh"),
        P(None, "mesh"),
        P(None, "mesh"),
        P("mesh"),
        P(None, None, None, "mesh"),
        P(None, None, None, "mesh"),
    )
    return jax.shard_map(
        shards,
        mesh=mesh,
        in_specs=placed,
        out_specs=(P("shot", None, None, "mesh"), P(None, None, ("mesh", "shot"))),
        check_vma=False,
    )
```

```python
import math

import jax
import jax.numpy as jnp
import numpy as np
from jax import lax
from jax.sharding import PartitionSpec as P

HIGH = lax.Precision.HIGHEST
MIX = lax.Precision.HIGH
STEP_SIZE = 0.02


def padded(x, sides, width):
    for axis, dim in sides:
        devices, length = (lax.axis_size(axis), x.shape[dim])
        up = [(i, (i + 1) % devices) for i in range(devices - 1)]
        down = [(j, i) for i, j in up]
        last = lax.slice_in_dim(x, length - width, length, axis=dim)
        first = lax.slice_in_dim(x, 0, width, axis=dim)
        before = lax.ppermute(last, axis, up)
        after = lax.ppermute(first, axis, down)
        x = jnp.concatenate([before, x, after], axis=dim)
    return x


def invert_matrix(matrix):
    order_count = matrix.shape[0]
    working = np.concatenate([matrix * 1.0, np.eye(order_count)], axis=1)
    for column in range(order_count):
        pivot_row = column + int(np.argmax(np.abs(working[column:, column])))
        working[[column, pivot_row]] = working[[pivot_row, column]]
        working[column] = working[column] / working[column, column]
        for target in range(order_count):
            if target != column:
                working[target] = working[target] - working[target, column] * working[column]
    return working[:, order_count:]


def basis_tables():
    points = [
        (across, along, upward)
        for upward in range(5)
        for along in range(5 - upward)
        for across in range(5 - upward - along)
    ]
    exponents = np.array(points) * 1.0
    coords = exponents / 4.0
    vander = np.prod(coords[:, None, :] ** exponents[None, :, :], axis=2)
    inverse = invert_matrix(vander)
    derivs = []
    for direction_axis in range(3):
        lowered = np.maximum(exponents - np.eye(3)[direction_axis], 0.0)
        slopes = exponents[None, :, direction_axis] * np.prod(
            coords[:, None, :] ** lowered[None, :, :], axis=2
        )
        derivs.append(slopes @ inverse)
    moments = np.array(
        [
            [
                math.factorial(first[0] + second[0])
                * math.factorial(first[1] + second[1])
                * math.factorial(first[2] + second[2])
                / math.factorial(sum(first) + sum(second) + 3)
                for second in points
            ]
            for first in points
        ]
    )
    mass_matrix = inverse.T @ moments @ inverse
    lattice = [(across, along) for along in range(5) for across in range(5 - along)]
    lattice_powers = np.array(lattice) * 1.0
    face_vander = np.prod((lattice_powers / 4.0)[:, None, :] ** lattice_powers[None, :, :], axis=2)
    face_inverse = invert_matrix(face_vander)
    face_moments = np.array(
        [
            [
                math.factorial(first[0] + second[0])
                * math.factorial(first[1] + second[1])
                / math.factorial(sum(first) + sum(second) + 2)
                for second in lattice
            ]
            for first in lattice
        ]
    )
    face_mass = face_inverse.T @ face_moments @ face_inverse
    numbers = {point: number for number, point in enumerate(points)}
    face_points = [
        [(across, along, 0) for across, along in lattice],
        [(across, 0, along) for across, along in lattice],
        [(0, across, along) for across, along in lattice],
        [(across, along, 4 - across - along) for across, along in lattice],
    ]
    face_nodes = np.array(
        [[numbers[point] for point in listing] for listing in face_points], np.int32
    )
    mass_inverse = invert_matrix(mass_matrix)
    lift_tables = []
    for face_number in range(4):
        selector = np.eye(35)[face_nodes[face_number]]
        lift_tables.append(mass_inverse @ selector.T @ face_mass)
    orderings = [(0, 1, 2), (1, 2, 0), (2, 0, 1), (1, 0, 2), (0, 2, 1), (2, 1, 0)]
    lattice_numbers = {point: number for number, point in enumerate(lattice)}
    triples = [(across, along, 4 - across - along) for across, along in lattice]
    turn_nodes = np.array(
        [
            [lattice_numbers[triple[ordering[0]], triple[ordering[1]]] for triple in triples]
            for ordering in orderings
        ],
        np.int32,
    )
    return (
        jnp.asarray(np.stack(derivs), jnp.float32),
        jnp.asarray(np.stack(lift_tables), jnp.float32),
        face_nodes,
        turn_nodes,
    )


def spatial_of(field, metric, derivs):
    reference_grads = jnp.einsum("rab,fbe->rfae", derivs, field, precision=MIX)
    rows = []
    for direction_axis in range(3):
        total = metric[0, direction_axis] * reference_grads[0]
        total = total + metric[1, direction_axis] * reference_grads[1]
        total = total + metric[2, direction_axis] * reference_grads[2]
        rows.append(total)
    return jnp.stack(rows)


def volume_term(adjoint, material, coupling, metric, derivs):
    spatial = spatial_of(adjoint, metric, derivs)
    mixing = jnp.einsum("dpfg,dfae->pgae", coupling, spatial, precision=MIX)
    return jnp.sum(material[:, None] * mixing, axis=0)


def kernel_term(adjoint, forward, coupling, metric, derivs):
    spatial = spatial_of(forward, metric, derivs)
    mixing = jnp.einsum("dpfg,dgae->pfae", coupling, spatial, precision=MIX)
    return jnp.sum(mixing * adjoint[None], axis=1)


def surface_term(jump_trace, face_material, face_normals, face_scale, coupling, lift_tables):
    weighted = face_normals[:, None, None] * jump_trace[None]
    mixing = jnp.einsum("dpfg,dfnxe->pgnxe", coupling, weighted, precision=MIX)
    face_flux = 0.5 * jnp.sum(face_material[:, None] * mixing, axis=0) + 0.5 * jump_trace
    return jnp.einsum(
        "xan,fnxe->fae", lift_tables, face_flux * face_scale[None, None], precision=MIX
    )


def halving_sum(values, axis, count):
    position = lax.axis_index(axis)
    work = values
    bit = count // 2
    while bit >= 1:
        width = work.shape[-1] // 2
        upper = (position & bit) != 0
        low = work[..., :width]
        high = work[..., width:]
        sent = lax.ppermute(
            jnp.where(upper, low, high), axis, [(i, i ^ bit) for i in range(count)]
        )
        work = jnp.where(upper, high, low) + sent
        bit //= 2
    return work


def search_direction(grad_share, step_share, change_share, gram, combine_sums):
    pairs = step_share.shape[0]
    both_share = jnp.concatenate([step_share, change_share], axis=0)
    with_grad = jnp.sum(both_share * grad_share[None], axis=(1, 2, 3))
    summed = combine_sums(jnp.concatenate([with_grad, gram.reshape(-1)]))
    lanes = 0.0 * step_share[0, 0, :8, :]
    summed = summed[:, None, None] + lanes[None]
    step_grad = summed[:pairs]
    change_grad = summed[pairs : 2 * pairs]
    gram = summed[2 * pairs :].reshape((2 * pairs, pairs) + summed.shape[1:])
    step_change = gram[:pairs]
    change_change = gram[pairs:]
    curvature = [step_change[slot, slot] for slot in range(pairs)]
    alphas = [None] * pairs
    for slot in reversed(range(pairs)):
        projected = step_grad[slot]
        for later in range(slot + 1, pairs):
            projected = projected - alphas[later] * step_change[slot, later]
        alphas[slot] = projected / curvature[slot]
    scaling = curvature[pairs - 1] / change_change[pairs - 1, pairs - 1]
    weights = [None] * pairs
    for slot in range(pairs):
        along = change_grad[slot]
        for other in range(pairs):
            along = along - alphas[other] * change_change[slot, other]
        along = scaling * along
        for earlier in range(slot):
            along = along + weights[earlier] * step_change[earlier, slot]
        beta_now = along / curvature[slot]
        weights[slot] = alphas[slot] - beta_now
    coefficients = jnp.stack(
        [weights[slot] for slot in range(pairs)]
        + [-scaling * alphas[slot] for slot in range(pairs)]
        + [scaling]
    )[:, 0, 0]
    rows = jnp.concatenate([both_share, grad_share[None]], axis=0)
    work = jnp.sum(coefficients[:, None, None, None] * rows, axis=0)
    return -work


def shards(
    adjoint_state,
    forward_states,
    material,
    coupling,
    metric,
    face_normals,
    face_scale,
    face_neighbours,
    face_orientation,
    send_faces,
    history_steps,
    history_changes,
):
    derivs, lift_tables, face_nodes, turn_nodes = basis_tables()
    fields = adjoint_state.shape[1]
    elements = adjoint_state.shape[3]
    node_count = material.shape[1]
    params = material.shape[0]
    face_width = face_nodes.shape[1]
    border = send_faces.shape[0] // 2
    slot_count = 4 * elements + 2 * border
    adjoint = adjoint_state[0]
    face_material = material[:, face_nodes.T, :]
    neighbours = face_neighbours.reshape(-1)
    orient = face_orientation.reshape(-1)
    face_total = 4 * elements
    slot_pick = (
        neighbours[None, :] == jnp.arange(slot_count, dtype=jnp.int32)[:, None]
    ).astype(jnp.float32)
    local_pick = slot_pick[:face_total]
    below_pick = slot_pick[face_total : face_total + border]
    above_pick = slot_pick[face_total + border :]
    node_turn = jnp.zeros((face_width, face_width, face_total), jnp.float32)
    for option in range(turn_nodes.shape[0]):
        node_turn = node_turn + (orient == option).astype(jnp.float32)[None, None, :] * jnp.asarray(
            np.eye(face_width, dtype=np.float32)[turn_nodes[option]].T
        )[:, :, None]
    send_pick = (
        send_faces[None, :] == jnp.arange(face_total, dtype=jnp.int32)[:, None]
    ).astype(jnp.float32)
    shot_count = lax.axis_size("shot")
    share_width = elements // shot_count
    share_start = lax.axis_index("shot") * share_width

    def own_share(rows):
        return lax.dynamic_slice_in_dim(rows, share_start, share_width, rows.ndim - 1)

    step_share = own_share(history_steps)
    change_share = own_share(history_changes)
    both_share = jnp.concatenate([step_share, change_share], axis=0)
    gram = jnp.sum(both_share[:, None] * change_share[None, :], axis=(2, 3, 4))
    step_share, change_share, gram, adjoint = lax.optimization_barrier(
        (step_share, change_share, gram, adjoint)
    )
    gradient = jnp.zeros((params, node_count, elements), jnp.float32)
    for step_index in range(forward_states.shape[1]):
        inner_trace = adjoint[:, face_nodes.T, :]
        flat_trace = inner_trace.reshape(fields, face_width, 4 * elements)
        sent_traces = jnp.einsum("fns,sj->fnj", flat_trace, send_pick, precision=MIX)
        extended = padded(sent_traces, (("mesh", 2),), border)
        gathered = jnp.einsum("fns,sj->fnj", flat_trace, local_pick, precision=MIX)
        gathered = gathered + jnp.einsum(
            "fns,sj->fnj", extended[:, :, :border], below_pick, precision=MIX
        )
        gathered = gathered + jnp.einsum(
            "fns,sj->fnj", extended[:, :, 3 * border :], above_pick, precision=MIX
        )
        turned = jnp.sum(gathered[:, :, None, :] * node_turn[None], axis=1)
        jump_trace = turned.reshape(fields, face_width, 4, elements) - inner_trace
        change = volume_term(adjoint, material, coupling, metric, derivs) + surface_term(
            jump_trace, face_material, face_normals, face_scale, coupling, lift_tables
        )
        adjoint = adjoint + STEP_SIZE * change
        gradient = gradient + STEP_SIZE * kernel_term(
            adjoint, forward_states[0, step_index], coupling, metric, derivs
        )
    device_count = shot_count * lax.axis_size("mesh")

    def combine_sums(values):
        spread = jnp.broadcast_to(values[None], (device_count,) + values.shape)
        return jnp.sum(lax.all_to_all(spread, ("shot", "mesh"), 0, 0, tiled=False), axis=0)

    grad_share = halving_sum(gradient, "shot", shot_count)
    result = search_direction(grad_share, step_share, change_share, gram, combine_sums)
    return (adjoint[None], result)


def solution(mesh):
    placed = (
        P("shot", None, None, "mesh"),
        P("shot", None, None, None, "mesh"),
        P(None, None, "mesh"),
        P(),
        P(None, None, "mesh"),
        P(None, None, "mesh"),
        P(None, "mesh"),
        P(None, "mesh"),
        P(None, "mesh"),
        P("mesh"),
        P(None, None, None, "mesh"),
        P(None, None, None, "mesh"),
    )
    return jax.shard_map(
        shards,
        mesh=mesh,
        in_specs=placed,
        out_specs=(P("shot", None, None, "mesh"), P(None, None, ("mesh", "shot"))),
        check_vma=False,
    )
```

```python
import math

import jax
import jax.numpy as jnp
import numpy as np
from jax import lax
from jax.sharding import PartitionSpec as P

HIGH = lax.Precision.HIGHEST
MIX = lax.Precision.HIGH
STEP_SIZE = 0.02


def padded(x, sides, width):
    for axis, dim in sides:
        devices, length = (lax.axis_size(axis), x.shape[dim])
        up = [(i, (i + 1) % devices) for i in range(devices - 1)]
        down = [(j, i) for i, j in up]
        last = lax.slice_in_dim(x, length - width, length, axis=dim)
        first = lax.slice_in_dim(x, 0, width, axis=dim)
        before = lax.ppermute(last, axis, up)
        after = lax.ppermute(first, axis, down)
        x = jnp.concatenate([before, x, after], axis=dim)
    return x


def invert_matrix(matrix):
    order_count = matrix.shape[0]
    working = np.concatenate([matrix * 1.0, np.eye(order_count)], axis=1)
    for column in range(order_count):
        pivot_row = column + int(np.argmax(np.abs(working[column:, column])))
        working[[column, pivot_row]] = working[[pivot_row, column]]
        working[column] = working[column] / working[column, column]
        for target in range(order_count):
            if target != column:
                working[target] = working[target] - working[target, column] * working[column]
    return working[:, order_count:]


def basis_tables():
    points = [
        (across, along, upward)
        for upward in range(5)
        for along in range(5 - upward)
        for across in range(5 - upward - along)
    ]
    exponents = np.array(points) * 1.0
    coords = exponents / 4.0
    vander = np.prod(coords[:, None, :] ** exponents[None, :, :], axis=2)
    inverse = invert_matrix(vander)
    derivs = []
    for direction_axis in range(3):
        lowered = np.maximum(exponents - np.eye(3)[direction_axis], 0.0)
        slopes = exponents[None, :, direction_axis] * np.prod(
            coords[:, None, :] ** lowered[None, :, :], axis=2
        )
        derivs.append(slopes @ inverse)
    moments = np.array(
        [
            [
                math.factorial(first[0] + second[0])
                * math.factorial(first[1] + second[1])
                * math.factorial(first[2] + second[2])
                / math.factorial(sum(first) + sum(second) + 3)
                for second in points
            ]
            for first in points
        ]
    )
    mass_matrix = inverse.T @ moments @ inverse
    lattice = [(across, along) for along in range(5) for across in range(5 - along)]
    lattice_powers = np.array(lattice) * 1.0
    face_vander = np.prod((lattice_powers / 4.0)[:, None, :] ** lattice_powers[None, :, :], axis=2)
    face_inverse = invert_matrix(face_vander)
    face_moments = np.array(
        [
            [
                math.factorial(first[0] + second[0])
                * math.factorial(first[1] + second[1])
                / math.factorial(sum(first) + sum(second) + 2)
                for second in lattice
            ]
            for first in lattice
        ]
    )
    face_mass = face_inverse.T @ face_moments @ face_inverse
    numbers = {point: number for number, point in enumerate(points)}
    face_points = [
        [(across, along, 0) for across, along in lattice],
        [(across, 0, along) for across, along in lattice],
        [(0, across, along) for across, along in lattice],
        [(across, along, 4 - across - along) for across, along in lattice],
    ]
    face_nodes = np.array(
        [[numbers[point] for point in listing] for listing in face_points], np.int32
    )
    mass_inverse = invert_matrix(mass_matrix)
    lift_tables = []
    for face_number in range(4):
        selector = np.eye(35)[face_nodes[face_number]]
        lift_tables.append(mass_inverse @ selector.T @ face_mass)
    orderings = [(0, 1, 2), (1, 2, 0), (2, 0, 1), (1, 0, 2), (0, 2, 1), (2, 1, 0)]
    lattice_numbers = {point: number for number, point in enumerate(lattice)}
    triples = [(across, along, 4 - across - along) for across, along in lattice]
    turn_nodes = np.array(
        [
            [lattice_numbers[triple[ordering[0]], triple[ordering[1]]] for triple in triples]
            for ordering in orderings
        ],
        np.int32,
    )
    return (
        jnp.asarray(np.stack(derivs), jnp.float32),
        jnp.asarray(np.stack(lift_tables), jnp.float32),
        face_nodes,
        turn_nodes,
    )


def spatial_of(field, metric, derivs):
    reference_grads = jnp.einsum("rab,fbe->rfae", derivs, field, precision=MIX)
    rows = []
    for direction_axis in range(3):
        total = metric[0, direction_axis] * reference_grads[0]
        total = total + metric[1, direction_axis] * reference_grads[1]
        total = total + metric[2, direction_axis] * reference_grads[2]
        rows.append(total)
    return jnp.stack(rows)


def volume_term(adjoint, material, coupling, metric, derivs):
    spatial = spatial_of(adjoint, metric, derivs)
    mixing = jnp.einsum("dpfg,dfae->pgae", coupling, spatial, precision=MIX)
    return jnp.sum(material[:, None] * mixing, axis=0)


def kernel_term(adjoint, forward, coupling, metric, derivs):
    spatial = spatial_of(forward, metric, derivs)
    mixing = jnp.einsum("dpfg,dgae->pfae", coupling, spatial, precision=MIX)
    return jnp.sum(mixing * adjoint[None], axis=1)


def surface_term(jump_trace, face_material, face_normals, face_scale, coupling, lift_tables):
    weighted = face_normals[:, None, None] * jump_trace[None]
    mixing = jnp.einsum("dpfg,dfnxe->pgnxe", coupling, weighted, precision=MIX)
    face_flux = 0.5 * jnp.sum(face_material[:, None] * mixing, axis=0) + 0.5 * jump_trace
    return jnp.einsum(
        "xan,fnxe->fae", lift_tables, face_flux * face_scale[None, None], precision=MIX
    )


def halving_sum(values, axis, count):
    position = lax.axis_index(axis)
    work = values
    bit = count // 2
    while bit >= 1:
        width = work.shape[-1] // 2
        upper = (position & bit) != 0
        low = work[..., :width]
        high = work[..., width:]
        sent = lax.ppermute(
            jnp.where(upper, low, high), axis, [(i, i ^ bit) for i in range(count)]
        )
        work = jnp.where(upper, high, low) + sent
        bit //= 2
    return work


def search_direction(grad_share, step_share, change_share, gram, combine_sums):
    pairs = step_share.shape[0]
    both_share = jnp.concatenate([step_share, change_share], axis=0)
    with_grad = jnp.sum(both_share * grad_share[None], axis=(1, 2, 3))
    summed = combine_sums(jnp.concatenate([with_grad, gram.reshape(-1)]))
    lanes = 0.0 * step_share[0, 0, :8, :]
    summed = summed[:, None, None] + lanes[None]
    step_grad = summed[:pairs]
    change_grad = summed[pairs : 2 * pairs]
    gram = summed[2 * pairs :].reshape((2 * pairs, pairs) + summed.shape[1:])
    step_change = gram[:pairs]
    change_change = gram[pairs:]
    curvature = [step_change[slot, slot] for slot in range(pairs)]
    alphas = [None] * pairs
    for slot in reversed(range(pairs)):
        projected = step_grad[slot]
        for later in range(slot + 1, pairs):
            projected = projected - alphas[later] * step_change[slot, later]
        alphas[slot] = projected / curvature[slot]
    scaling = curvature[pairs - 1] / change_change[pairs - 1, pairs - 1]
    weights = [None] * pairs
    for slot in range(pairs):
        along = change_grad[slot]
        for other in range(pairs):
            along = along - alphas[other] * change_change[slot, other]
        along = scaling * along
        for earlier in range(slot):
            along = along + weights[earlier] * step_change[earlier, slot]
        beta_now = along / curvature[slot]
        weights[slot] = alphas[slot] - beta_now
    coefficients = jnp.stack(
        [weights[slot] for slot in range(pairs)]
        + [-scaling * alphas[slot] for slot in range(pairs)]
        + [scaling]
    )[:, 0, 0]
    rows = jnp.concatenate([both_share, grad_share[None]], axis=0)
    work = jnp.sum(coefficients[:, None, None, None] * rows, axis=0)
    return -work


def shards(
    adjoint_state,
    forward_states,
    material,
    coupling,
    metric,
    face_normals,
    face_scale,
    face_neighbours,
    face_orientation,
    send_faces,
    history_steps,
    history_changes,
):
    derivs, lift_tables, face_nodes, turn_nodes = basis_tables()
    fields = adjoint_state.shape[1]
    elements = adjoint_state.shape[3]
    node_count = material.shape[1]
    params = material.shape[0]
    face_width = face_nodes.shape[1]
    border = send_faces.shape[0] // 2
    slot_count = 4 * elements + 2 * border
    adjoint = adjoint_state[0]
    face_material = material[:, face_nodes.T, :]
    neighbours = face_neighbours.reshape(-1)
    orient = face_orientation.reshape(-1)
    face_total = 4 * elements
    slot_pick = (
        neighbours[None, :] == jnp.arange(slot_count, dtype=jnp.int32)[:, None]
    ).astype(jnp.float32)
    local_pick = slot_pick[:face_total]
    below_pick = slot_pick[face_total : face_total + border]
    above_pick = slot_pick[face_total + border :]
    node_turn = jnp.zeros((face_width, face_width, face_total), jnp.float32)
    for option in range(turn_nodes.shape[0]):
        node_turn = node_turn + (orient == option).astype(jnp.float32)[None, None, :] * jnp.asarray(
            np.eye(face_width, dtype=np.float32)[turn_nodes[option]].T
        )[:, :, None]
    send_pick = (
        send_faces[None, :] == jnp.arange(face_total, dtype=jnp.int32)[:, None]
    ).astype(jnp.float32)
    shot_count = lax.axis_size("shot")
    share_width = elements // shot_count
    share_start = lax.axis_index("shot") * share_width

    def own_share(rows):
        return lax.dynamic_slice_in_dim(rows, share_start, share_width, rows.ndim - 1)

    lane_pick = (
        jnp.arange(elements, dtype=jnp.int32)[:, None]
        == share_start + jnp.arange(share_width, dtype=jnp.int32)[None, :]
    ).astype(jnp.float32)
    both_share = jnp.einsum(
        "ipae,ej->ipaj",
        jnp.concatenate([history_steps, history_changes], axis=0),
        lane_pick,
        precision=HIGH,
    )
    pairs = history_steps.shape[0]
    step_share = both_share[:pairs]
    change_share = both_share[pairs:]
    both_flat = both_share.reshape(2 * pairs, -1)
    gram = jnp.dot(both_flat, both_flat[pairs:].T, precision=HIGH)
    step_share, change_share, gram, adjoint = lax.optimization_barrier(
        (step_share, change_share, gram, adjoint)
    )
    gradient = jnp.zeros((params, node_count, elements), jnp.float32)
    for step_index in range(forward_states.shape[1]):
        inner_trace = adjoint[:, face_nodes.T, :]
        flat_trace = inner_trace.reshape(fields, face_width, 4 * elements)
        sent_traces = jnp.einsum("fns,sj->fnj", flat_trace, send_pick, precision=MIX)
        extended = padded(sent_traces, (("mesh", 2),), border)
        gathered = jnp.einsum("fns,sj->fnj", flat_trace, local_pick, precision=MIX)
        gathered = gathered + jnp.einsum(
            "fns,sj->fnj", extended[:, :, :border], below_pick, precision=MIX
        )
        gathered = gathered + jnp.einsum(
            "fns,sj->fnj", extended[:, :, 3 * border :], above_pick, precision=MIX
        )
        turned = jnp.sum(gathered[:, :, None, :] * node_turn[None], axis=1)
        jump_trace = turned.reshape(fields, face_width, 4, elements) - inner_trace
        change = volume_term(adjoint, material, coupling, metric, derivs) + surface_term(
            jump_trace, face_material, face_normals, face_scale, coupling, lift_tables
        )
        adjoint = adjoint + STEP_SIZE * change
        gradient = gradient + STEP_SIZE * kernel_term(
            adjoint, forward_states[0, step_index], coupling, metric, derivs
        )
    device_count = shot_count * lax.axis_size("mesh")

    def combine_sums(values):
        spread = jnp.broadcast_to(values[None], (device_count,) + values.shape)
        return jnp.sum(lax.all_to_all(spread, ("shot", "mesh"), 0, 0, tiled=False), axis=0)

    grad_share = halving_sum(gradient, "shot", shot_count)
    result = search_direction(grad_share, step_share, change_share, gram, combine_sums)
    return (adjoint[None], result)


def solution(mesh):
    placed = (
        P("shot", None, None, "mesh"),
        P("shot", None, None, None, "mesh"),
        P(None, None, "mesh"),
        P(),
        P(None, None, "mesh"),
        P(None, None, "mesh"),
        P(None, "mesh"),
        P(None, "mesh"),
        P(None, "mesh"),
        P("mesh"),
        P(None, None, None, "mesh"),
        P(None, None, None, "mesh"),
    )
    return jax.shard_map(
        shards,
        mesh=mesh,
        in_specs=placed,
        out_specs=(P("shot", None, None, "mesh"), P(None, None, ("mesh", "shot"))),
        check_vma=False,
    )
```

```python
import math

import jax
import jax.numpy as jnp
import numpy as np
from jax import lax
from jax.sharding import PartitionSpec as P

HIGH = lax.Precision.HIGHEST
MIX = lax.Precision.HIGH
STEP_SIZE = 0.02


def padded(x, sides, width):
    for axis, dim in sides:
        devices, length = (lax.axis_size(axis), x.shape[dim])
        up = [(i, (i + 1) % devices) for i in range(devices - 1)]
        down = [(j, i) for i, j in up]
        last = lax.slice_in_dim(x, length - width, length, axis=dim)
        first = lax.slice_in_dim(x, 0, width, axis=dim)
        before = lax.ppermute(last, axis, up)
        after = lax.ppermute(first, axis, down)
        x = jnp.concatenate([before, x, after], axis=dim)
    return x


def invert_matrix(matrix):
    order_count = matrix.shape[0]
    working = np.concatenate([matrix * 1.0, np.eye(order_count)], axis=1)
    for column in range(order_count):
        pivot_row = column + int(np.argmax(np.abs(working[column:, column])))
        working[[column, pivot_row]] = working[[pivot_row, column]]
        working[column] = working[column] / working[column, column]
        for target in range(order_count):
            if target != column:
                working[target] = working[target] - working[target, column] * working[column]
    return working[:, order_count:]


def basis_tables():
    points = [
        (across, along, upward)
        for upward in range(5)
        for along in range(5 - upward)
        for across in range(5 - upward - along)
    ]
    exponents = np.array(points) * 1.0
    coords = exponents / 4.0
    vander = np.prod(coords[:, None, :] ** exponents[None, :, :], axis=2)
    inverse = invert_matrix(vander)
    derivs = []
    for direction_axis in range(3):
        lowered = np.maximum(exponents - np.eye(3)[direction_axis], 0.0)
        slopes = exponents[None, :, direction_axis] * np.prod(
            coords[:, None, :] ** lowered[None, :, :], axis=2
        )
        derivs.append(slopes @ inverse)
    moments = np.array(
        [
            [
                math.factorial(first[0] + second[0])
                * math.factorial(first[1] + second[1])
                * math.factorial(first[2] + second[2])
                / math.factorial(sum(first) + sum(second) + 3)
                for second in points
            ]
            for first in points
        ]
    )
    mass_matrix = inverse.T @ moments @ inverse
    lattice = [(across, along) for along in range(5) for across in range(5 - along)]
    lattice_powers = np.array(lattice) * 1.0
    face_vander = np.prod((lattice_powers / 4.0)[:, None, :] ** lattice_powers[None, :, :], axis=2)
    face_inverse = invert_matrix(face_vander)
    face_moments = np.array(
        [
            [
                math.factorial(first[0] + second[0])
                * math.factorial(first[1] + second[1])
                / math.factorial(sum(first) + sum(second) + 2)
                for second in lattice
            ]
            for first in lattice
        ]
    )
    face_mass = face_inverse.T @ face_moments @ face_inverse
    numbers = {point: number for number, point in enumerate(points)}
    face_points = [
        [(across, along, 0) for across, along in lattice],
        [(across, 0, along) for across, along in lattice],
        [(0, across, along) for across, along in lattice],
        [(across, along, 4 - across - along) for across, along in lattice],
    ]
    face_nodes = np.array(
        [[numbers[point] for point in listing] for listing in face_points], np.int32
    )
    mass_inverse = invert_matrix(mass_matrix)
    lift_tables = []
    for face_number in range(4):
        selector = np.eye(35)[face_nodes[face_number]]
        lift_tables.append(mass_inverse @ selector.T @ face_mass)
    orderings = [(0, 1, 2), (1, 2, 0), (2, 0, 1), (1, 0, 2), (0, 2, 1), (2, 1, 0)]
    lattice_numbers = {point: number for number, point in enumerate(lattice)}
    triples = [(across, along, 4 - across - along) for across, along in lattice]
    turn_nodes = np.array(
        [
            [lattice_numbers[triple[ordering[0]], triple[ordering[1]]] for triple in triples]
            for ordering in orderings
        ],
        np.int32,
    )
    return (
        jnp.asarray(np.stack(derivs), jnp.float32),
        jnp.asarray(np.stack(lift_tables), jnp.float32),
        face_nodes,
        turn_nodes,
    )


def spatial_of(field, metric, derivs):
    reference_grads = jnp.einsum("rab,fbe->rfae", derivs, field, precision=MIX)
    rows = []
    for direction_axis in range(3):
        total = metric[0, direction_axis] * reference_grads[0]
        total = total + metric[1, direction_axis] * reference_grads[1]
        total = total + metric[2, direction_axis] * reference_grads[2]
        rows.append(total)
    return jnp.stack(rows)


def volume_term(adjoint, material, coupling, metric, derivs):
    spatial = spatial_of(adjoint, metric, derivs)
    mixing = jnp.einsum("dpfg,dfae->pgae", coupling, spatial, precision=MIX)
    return jnp.sum(material[:, None] * mixing, axis=0)


def kernel_term(adjoint, forward, coupling, metric, derivs):
    spatial = spatial_of(forward, metric, derivs)
    mixing = jnp.einsum("dpfg,dgae->pfae", coupling, spatial, precision=MIX)
    return jnp.sum(mixing * adjoint[None], axis=1)


def surface_term(jump_trace, face_material, face_normals, face_scale, coupling, lift_tables):
    weighted = face_normals[:, None, None] * jump_trace[None]
    mixing = jnp.einsum("dpfg,dfnxe->pgnxe", coupling, weighted, precision=MIX)
    face_flux = 0.5 * jnp.sum(face_material[:, None] * mixing, axis=0) + 0.5 * jump_trace
    return jnp.einsum(
        "xan,fnxe->fae", lift_tables, face_flux * face_scale[None, None], precision=MIX
    )


def halving_sum(values, axis, count):
    position = lax.axis_index(axis)
    work = values
    bit = count // 2
    while bit >= 1:
        width = work.shape[-1] // 2
        upper = (position & bit) != 0
        low = work[..., :width]
        high = work[..., width:]
        sent = lax.ppermute(
            jnp.where(upper, low, high), axis, [(i, i ^ bit) for i in range(count)]
        )
        work = jnp.where(upper, high, low) + sent
        bit //= 2
    return work


def search_direction(grad_share, step_share, change_share, gram, combine_sums):
    pairs = step_share.shape[0]
    both_share = jnp.concatenate([step_share, change_share], axis=0)
    with_grad = jnp.sum(both_share * grad_share[None], axis=(1, 2, 3))
    summed = combine_sums(jnp.concatenate([with_grad, gram.reshape(-1)]))
    lanes = 0.0 * step_share[0, 0, :8, :]
    summed = summed[:, None, None] + lanes[None]
    step_grad = summed[:pairs]
    change_grad = summed[pairs : 2 * pairs]
    gram = summed[2 * pairs :].reshape((2 * pairs, pairs) + summed.shape[1:])
    step_change = gram[:pairs]
    change_change = gram[pairs:]
    curvature = [step_change[slot, slot] for slot in range(pairs)]
    alphas = [None] * pairs
    for slot in reversed(range(pairs)):
        projected = step_grad[slot]
        for later in range(slot + 1, pairs):
            projected = projected - alphas[later] * step_change[slot, later]
        alphas[slot] = projected / curvature[slot]
    scaling = curvature[pairs - 1] / change_change[pairs - 1, pairs - 1]
    weights = [None] * pairs
    for slot in range(pairs):
        along = change_grad[slot]
        for other in range(pairs):
            along = along - alphas[other] * change_change[slot, other]
        along = scaling * along
        for earlier in range(slot):
            along = along + weights[earlier] * step_change[earlier, slot]
        beta_now = along / curvature[slot]
        weights[slot] = alphas[slot] - beta_now
    coefficients = jnp.stack(
        [weights[slot] for slot in range(pairs)]
        + [-scaling * alphas[slot] for slot in range(pairs)]
        + [scaling]
    )[:, 0, 0]
    rows = jnp.concatenate([both_share, grad_share[None]], axis=0)
    work = jnp.sum(coefficients[:, None, None, None] * rows, axis=0)
    return -work


def shards(
    adjoint_state,
    forward_states,
    material,
    coupling,
    metric,
    face_normals,
    face_scale,
    face_neighbours,
    face_orientation,
    send_faces,
    history_steps,
    history_changes,
):
    derivs, lift_tables, face_nodes, turn_nodes = basis_tables()
    fields = adjoint_state.shape[1]
    elements = adjoint_state.shape[3]
    node_count = material.shape[1]
    params = material.shape[0]
    face_width = face_nodes.shape[1]
    border = send_faces.shape[0] // 2
    slot_count = 4 * elements + 2 * border
    adjoint = adjoint_state[0]
    face_material = material[:, face_nodes.T, :]
    neighbours = face_neighbours.reshape(-1)
    orient = face_orientation.reshape(-1)
    face_total = 4 * elements
    slot_pick = (
        neighbours[None, :] == jnp.arange(slot_count, dtype=jnp.int32)[:, None]
    ).astype(jnp.float32)
    local_pick = slot_pick[:face_total]
    below_pick = slot_pick[face_total : face_total + border]
    above_pick = slot_pick[face_total + border :]
    node_turn = jnp.zeros((face_width, face_width, face_total), jnp.float32)
    for option in range(turn_nodes.shape[0]):
        node_turn = node_turn + (orient == option).astype(jnp.float32)[None, None, :] * jnp.asarray(
            np.eye(face_width, dtype=np.float32)[turn_nodes[option]].T
        )[:, :, None]
    send_pick = (
        send_faces[None, :] == jnp.arange(face_total, dtype=jnp.int32)[:, None]
    ).astype(jnp.float32)
    shot_count = lax.axis_size("shot")
    share_width = elements // shot_count
    share_start = lax.axis_index("shot") * share_width

    def own_share(rows):
        return lax.dynamic_slice_in_dim(rows, share_start, share_width, rows.ndim - 1)

    lane_pick = (
        jnp.arange(elements, dtype=jnp.int32)[:, None]
        == share_start + jnp.arange(share_width, dtype=jnp.int32)[None, :]
    ).astype(jnp.float32)
    both_share = jnp.einsum(
        "ipae,ej->ipaj",
        jnp.concatenate([history_steps, history_changes], axis=0),
        lane_pick,
        precision=MIX,
    )
    pairs = history_steps.shape[0]
    step_share = both_share[:pairs]
    change_share = both_share[pairs:]
    gram = jnp.sum(both_share[:, None] * change_share[None, :], axis=(2, 3, 4))
    step_share, change_share, gram, adjoint = lax.optimization_barrier(
        (step_share, change_share, gram, adjoint)
    )
    gradient = jnp.zeros((params, node_count, elements), jnp.float32)
    for step_index in range(forward_states.shape[1]):
        inner_trace = adjoint[:, face_nodes.T, :]
        flat_trace = inner_trace.reshape(fields, face_width, 4 * elements)
        sent_traces = jnp.einsum("fns,sj->fnj", flat_trace, send_pick, precision=MIX)
        extended = padded(sent_traces, (("mesh", 2),), border)
        gathered = jnp.einsum("fns,sj->fnj", flat_trace, local_pick, precision=MIX)
        gathered = gathered + jnp.einsum(
            "fns,sj->fnj", extended[:, :, :border], below_pick, precision=MIX
        )
        gathered = gathered + jnp.einsum(
            "fns,sj->fnj", extended[:, :, 3 * border :], above_pick, precision=MIX
        )
        turned = jnp.sum(gathered[:, :, None, :] * node_turn[None], axis=1)
        jump_trace = turned.reshape(fields, face_width, 4, elements) - inner_trace
        change = volume_term(adjoint, material, coupling, metric, derivs) + surface_term(
            jump_trace, face_material, face_normals, face_scale, coupling, lift_tables
        )
        adjoint = adjoint + STEP_SIZE * change
        gradient = gradient + STEP_SIZE * kernel_term(
            adjoint, forward_states[0, step_index], coupling, metric, derivs
        )
    device_count = shot_count * lax.axis_size("mesh")

    def combine_sums(values):
        spread = jnp.broadcast_to(values[None], (device_count,) + values.shape)
        return jnp.sum(lax.all_to_all(spread, ("shot", "mesh"), 0, 0, tiled=False), axis=0)

    grad_share = halving_sum(gradient, "shot", shot_count)
    result = search_direction(grad_share, step_share, change_share, gram, combine_sums)
    return (adjoint[None], result)


def solution(mesh):
    placed = (
        P("shot", None, None, "mesh"),
        P("shot", None, None, None, "mesh"),
        P(None, None, "mesh"),
        P(),
        P(None, None, "mesh"),
        P(None, None, "mesh"),
        P(None, "mesh"),
        P(None, "mesh"),
        P(None, "mesh"),
        P("mesh"),
        P(None, None, None, "mesh"),
        P(None, None, None, "mesh"),
    )
    return jax.shard_map(
        shards,
        mesh=mesh,
        in_specs=placed,
        out_specs=(P("shot", None, None, "mesh"), P(None, None, ("mesh", "shot"))),
        check_vma=False,
    )
```

```python
import math

import jax
import jax.numpy as jnp
import numpy as np
from jax import lax
from jax.sharding import PartitionSpec as P

HIGH = lax.Precision.HIGHEST
MIX = lax.Precision.HIGH
STEP_SIZE = 0.02


def padded(x, sides, width):
    for axis, dim in sides:
        devices, length = (lax.axis_size(axis), x.shape[dim])
        up = [(i, (i + 1) % devices) for i in range(devices - 1)]
        down = [(j, i) for i, j in up]
        last = lax.slice_in_dim(x, length - width, length, axis=dim)
        first = lax.slice_in_dim(x, 0, width, axis=dim)
        before = lax.ppermute(last, axis, up)
        after = lax.ppermute(first, axis, down)
        x = jnp.concatenate([before, x, after], axis=dim)
    return x


def invert_matrix(matrix):
    order_count = matrix.shape[0]
    working = np.concatenate([matrix * 1.0, np.eye(order_count)], axis=1)
    for column in range(order_count):
        pivot_row = column + int(np.argmax(np.abs(working[column:, column])))
        working[[column, pivot_row]] = working[[pivot_row, column]]
        working[column] = working[column] / working[column, column]
        for target in range(order_count):
            if target != column:
                working[target] = working[target] - working[target, column] * working[column]
    return working[:, order_count:]


def basis_tables():
    points = [
        (across, along, upward)
        for upward in range(5)
        for along in range(5 - upward)
        for across in range(5 - upward - along)
    ]
    exponents = np.array(points) * 1.0
    coords = exponents / 4.0
    vander = np.prod(coords[:, None, :] ** exponents[None, :, :], axis=2)
    inverse = invert_matrix(vander)
    derivs = []
    for direction_axis in range(3):
        lowered = np.maximum(exponents - np.eye(3)[direction_axis], 0.0)
        slopes = exponents[None, :, direction_axis] * np.prod(
            coords[:, None, :] ** lowered[None, :, :], axis=2
        )
        derivs.append(slopes @ inverse)
    moments = np.array(
        [
            [
                math.factorial(first[0] + second[0])
                * math.factorial(first[1] + second[1])
                * math.factorial(first[2] + second[2])
                / math.factorial(sum(first) + sum(second) + 3)
                for second in points
            ]
            for first in points
        ]
    )
    mass_matrix = inverse.T @ moments @ inverse
    lattice = [(across, along) for along in range(5) for across in range(5 - along)]
    lattice_powers = np.array(lattice) * 1.0
    face_vander = np.prod((lattice_powers / 4.0)[:, None, :] ** lattice_powers[None, :, :], axis=2)
    face_inverse = invert_matrix(face_vander)
    face_moments = np.array(
        [
            [
                math.factorial(first[0] + second[0])
                * math.factorial(first[1] + second[1])
                / math.factorial(sum(first) + sum(second) + 2)
                for second in lattice
            ]
            for first in lattice
        ]
    )
    face_mass = face_inverse.T @ face_moments @ face_inverse
    numbers = {point: number for number, point in enumerate(points)}
    face_points = [
        [(across, along, 0) for across, along in lattice],
        [(across, 0, along) for across, along in lattice],
        [(0, across, along) for across, along in lattice],
        [(across, along, 4 - across - along) for across, along in lattice],
    ]
    face_nodes = np.array(
        [[numbers[point] for point in listing] for listing in face_points], np.int32
    )
    mass_inverse = invert_matrix(mass_matrix)
    lift_tables = []
    for face_number in range(4):
        selector = np.eye(35)[face_nodes[face_number]]
        lift_tables.append(mass_inverse @ selector.T @ face_mass)
    orderings = [(0, 1, 2), (1, 2, 0), (2, 0, 1), (1, 0, 2), (0, 2, 1), (2, 1, 0)]
    lattice_numbers = {point: number for number, point in enumerate(lattice)}
    triples = [(across, along, 4 - across - along) for across, along in lattice]
    turn_nodes = np.array(
        [
            [lattice_numbers[triple[ordering[0]], triple[ordering[1]]] for triple in triples]
            for ordering in orderings
        ],
        np.int32,
    )
    return (
        jnp.asarray(np.stack(derivs), jnp.float32),
        jnp.asarray(np.stack(lift_tables), jnp.float32),
        face_nodes,
        turn_nodes,
    )


def spatial_of(field, metric, derivs):
    reference_grads = jnp.einsum("rab,fbe->rfae", derivs, field, precision=MIX)
    rows = []
    for direction_axis in range(3):
        total = metric[0, direction_axis] * reference_grads[0]
        total = total + metric[1, direction_axis] * reference_grads[1]
        total = total + metric[2, direction_axis] * reference_grads[2]
        rows.append(total)
    return jnp.stack(rows)


def volume_term(adjoint, material, coupling, metric, derivs):
    spatial = spatial_of(adjoint, metric, derivs)
    mixing = jnp.einsum("dpfg,dfae->pgae", coupling, spatial, precision=MIX)
    return jnp.sum(material[:, None] * mixing, axis=0)


def kernel_term(adjoint, forward, coupling, metric, derivs):
    spatial = spatial_of(forward, metric, derivs)
    mixing = jnp.einsum("dpfg,dgae->pfae", coupling, spatial, precision=MIX)
    return jnp.sum(mixing * adjoint[None], axis=1)


def surface_term(jump_trace, face_material, face_normals, face_scale, coupling, lift_tables):
    weighted = face_normals[:, None, None] * jump_trace[None]
    mixing = jnp.einsum("dpfg,dfnxe->pgnxe", coupling, weighted, precision=MIX)
    face_flux = 0.5 * jnp.sum(face_material[:, None] * mixing, axis=0) + 0.5 * jump_trace
    return jnp.einsum(
        "xan,fnxe->fae", lift_tables, face_flux * face_scale[None, None], precision=MIX
    )


def halving_sum(values, axis, count):
    position = lax.axis_index(axis)
    work = values
    bit = count // 2
    while bit >= 1:
        width = work.shape[-1] // 2
        upper = (position & bit) != 0
        low = work[..., :width]
        high = work[..., width:]
        sent = lax.ppermute(
            jnp.where(upper, low, high), axis, [(i, i ^ bit) for i in range(count)]
        )
        work = jnp.where(upper, high, low) + sent
        bit //= 2
    return work


def search_direction(grad_share, step_share, change_share, gram, combine_sums):
    pairs = step_share.shape[0]
    both_share = jnp.concatenate([step_share, change_share], axis=0)
    with_grad = jnp.sum(both_share * grad_share[None], axis=(1, 2, 3))
    summed = combine_sums(jnp.concatenate([with_grad, gram.reshape(-1)]))
    lanes = 0.0 * step_share[0, 0, :8, :]
    summed = summed[:, None, None] + lanes[None]
    step_grad = summed[:pairs]
    change_grad = summed[pairs : 2 * pairs]
    gram = summed[2 * pairs :].reshape((2 * pairs, pairs) + summed.shape[1:])
    step_change = gram[:pairs]
    change_change = gram[pairs:]
    curvature = [step_change[slot, slot] for slot in range(pairs)]
    alphas = [None] * pairs
    for slot in reversed(range(pairs)):
        projected = step_grad[slot]
        for later in range(slot + 1, pairs):
            projected = projected - alphas[later] * step_change[slot, later]
        alphas[slot] = projected / curvature[slot]
    scaling = curvature[pairs - 1] / change_change[pairs - 1, pairs - 1]
    weights = [None] * pairs
    for slot in range(pairs):
        along = change_grad[slot]
        for other in range(pairs):
            along = along - alphas[other] * change_change[slot, other]
        along = scaling * along
        for earlier in range(slot):
            along = along + weights[earlier] * step_change[earlier, slot]
        beta_now = along / curvature[slot]
        weights[slot] = alphas[slot] - beta_now
    coefficients = jnp.stack(
        [weights[slot] for slot in range(pairs)]
        + [-scaling * alphas[slot] for slot in range(pairs)]
        + [scaling]
    )[:, 0, 0]
    rows = jnp.concatenate([both_share, grad_share[None]], axis=0)
    work = jnp.sum(coefficients[:, None, None, None] * rows, axis=0)
    return -work


def shards(
    adjoint_state,
    forward_states,
    material,
    coupling,
    metric,
    face_normals,
    face_scale,
    face_neighbours,
    face_orientation,
    send_faces,
    history_steps,
    history_changes,
):
    derivs, lift_tables, face_nodes, turn_nodes = basis_tables()
    fields = adjoint_state.shape[1]
    elements = adjoint_state.shape[3]
    node_count = material.shape[1]
    params = material.shape[0]
    face_width = face_nodes.shape[1]
    border = send_faces.shape[0] // 2
    slot_count = 4 * elements + 2 * border
    adjoint = adjoint_state[0]
    face_material = material[:, face_nodes.T, :]
    neighbours = face_neighbours.reshape(-1)
    orient = face_orientation.reshape(-1)
    face_total = 4 * elements
    slot_pick = (
        neighbours[None, :] == jnp.arange(slot_count, dtype=jnp.int32)[:, None]
    ).astype(jnp.float32)
    local_pick = slot_pick[:face_total]
    below_pick = slot_pick[face_total : face_total + border]
    above_pick = slot_pick[face_total + border :]
    node_turn = jnp.zeros((face_width, face_width, face_total), jnp.float32)
    for option in range(turn_nodes.shape[0]):
        node_turn = node_turn + (orient == option).astype(jnp.float32)[None, None, :] * jnp.asarray(
            np.eye(face_width, dtype=np.float32)[turn_nodes[option]].T
        )[:, :, None]
    send_pick = (
        send_faces[None, :] == jnp.arange(face_total, dtype=jnp.int32)[:, None]
    ).astype(jnp.float32)
    shot_count = lax.axis_size("shot")
    share_width = elements // shot_count
    share_start = lax.axis_index("shot") * share_width

    def own_share(rows):
        return lax.dynamic_slice_in_dim(rows, share_start, share_width, rows.ndim - 1)

    lane_pick = (
        jnp.arange(elements, dtype=jnp.int32)[:, None]
        == share_start + jnp.arange(share_width, dtype=jnp.int32)[None, :]
    ).astype(jnp.float32)
    both_share = jnp.einsum(
        "ipae,ej->ipaj",
        jnp.concatenate([history_steps, history_changes], axis=0),
        lane_pick,
        precision=MIX,
    )
    pairs = history_steps.shape[0]
    step_share = both_share[:pairs]
    change_share = both_share[pairs:]
    gram = jnp.sum(both_share[:, None] * change_share[None, :], axis=(2, 3, 4))
    step_share, change_share, gram, adjoint = lax.optimization_barrier(
        (step_share, change_share, gram, adjoint)
    )
    gradient = jnp.zeros((params, node_count, elements), jnp.float32)
    steps = forward_states.shape[1]
    forward_spatial = spatial_of(
        forward_states[0].reshape(steps * fields, node_count, elements), metric, derivs
    ).reshape(3, steps, fields, node_count, elements)
    forward_mixing = jnp.einsum(
        "dpfg,dtgae->tpfae", coupling, forward_spatial, precision=MIX
    )
    for step_index in range(steps):
        inner_trace = adjoint[:, face_nodes.T, :]
        flat_trace = inner_trace.reshape(fields, face_width, 4 * elements)
        sent_traces = jnp.einsum("fns,sj->fnj", flat_trace, send_pick, precision=MIX)
        extended = padded(sent_traces, (("mesh", 2),), border)
        gathered = jnp.einsum("fns,sj->fnj", flat_trace, local_pick, precision=MIX)
        gathered = gathered + jnp.einsum(
            "fns,sj->fnj", extended[:, :, :border], below_pick, precision=MIX
        )
        gathered = gathered + jnp.einsum(
            "fns,sj->fnj", extended[:, :, 3 * border :], above_pick, precision=MIX
        )
        turned = jnp.sum(gathered[:, :, None, :] * node_turn[None], axis=1)
        jump_trace = turned.reshape(fields, face_width, 4, elements) - inner_trace
        change = volume_term(adjoint, material, coupling, metric, derivs) + surface_term(
            jump_trace, face_material, face_normals, face_scale, coupling, lift_tables
        )
        adjoint = adjoint + STEP_SIZE * change
        gradient = gradient + STEP_SIZE * jnp.sum(
            forward_mixing[step_index] * adjoint[None], axis=1
        )
    device_count = shot_count * lax.axis_size("mesh")

    def combine_sums(values):
        spread = jnp.broadcast_to(values[None], (device_count,) + values.shape)
        return jnp.sum(lax.all_to_all(spread, ("shot", "mesh"), 0, 0, tiled=False), axis=0)

    grad_share = halving_sum(gradient, "shot", shot_count)
    result = search_direction(grad_share, step_share, change_share, gram, combine_sums)
    return (adjoint[None], result)


def solution(mesh):
    placed = (
        P("shot", None, None, "mesh"),
        P("shot", None, None, None, "mesh"),
        P(None, None, "mesh"),
        P(),
        P(None, None, "mesh"),
        P(None, None, "mesh"),
        P(None, "mesh"),
        P(None, "mesh"),
        P(None, "mesh"),
        P("mesh"),
        P(None, None, None, "mesh"),
        P(None, None, None, "mesh"),
    )
    return jax.shard_map(
        shards,
        mesh=mesh,
        in_specs=placed,
        out_specs=(P("shot", None, None, "mesh"), P(None, None, ("mesh", "shot"))),
        check_vma=False,
    )
```

```python
import math

import jax
import jax.numpy as jnp
import numpy as np
from jax import lax
from jax.sharding import PartitionSpec as P

HIGH = lax.Precision.HIGHEST
MIX = lax.Precision.HIGH
STEP_SIZE = 0.02


def padded(x, sides, width):
    for axis, dim in sides:
        devices, length = (lax.axis_size(axis), x.shape[dim])
        up = [(i, (i + 1) % devices) for i in range(devices - 1)]
        down = [(j, i) for i, j in up]
        last = lax.slice_in_dim(x, length - width, length, axis=dim)
        first = lax.slice_in_dim(x, 0, width, axis=dim)
        before = lax.ppermute(last, axis, up)
        after = lax.ppermute(first, axis, down)
        x = jnp.concatenate([before, x, after], axis=dim)
    return x


def invert_matrix(matrix):
    order_count = matrix.shape[0]
    working = np.concatenate([matrix * 1.0, np.eye(order_count)], axis=1)
    for column in range(order_count):
        pivot_row = column + int(np.argmax(np.abs(working[column:, column])))
        working[[column, pivot_row]] = working[[pivot_row, column]]
        working[column] = working[column] / working[column, column]
        for target in range(order_count):
            if target != column:
                working[target] = working[target] - working[target, column] * working[column]
    return working[:, order_count:]


def basis_tables():
    points = [
        (across, along, upward)
        for upward in range(5)
        for along in range(5 - upward)
        for across in range(5 - upward - along)
    ]
    exponents = np.array(points) * 1.0
    coords = exponents / 4.0
    vander = np.prod(coords[:, None, :] ** exponents[None, :, :], axis=2)
    inverse = invert_matrix(vander)
    derivs = []
    for direction_axis in range(3):
        lowered = np.maximum(exponents - np.eye(3)[direction_axis], 0.0)
        slopes = exponents[None, :, direction_axis] * np.prod(
            coords[:, None, :] ** lowered[None, :, :], axis=2
        )
        derivs.append(slopes @ inverse)
    moments = np.array(
        [
            [
                math.factorial(first[0] + second[0])
                * math.factorial(first[1] + second[1])
                * math.factorial(first[2] + second[2])
                / math.factorial(sum(first) + sum(second) + 3)
                for second in points
            ]
            for first in points
        ]
    )
    mass_matrix = inverse.T @ moments @ inverse
    lattice = [(across, along) for along in range(5) for across in range(5 - along)]
    lattice_powers = np.array(lattice) * 1.0
    face_vander = np.prod((lattice_powers / 4.0)[:, None, :] ** lattice_powers[None, :, :], axis=2)
    face_inverse = invert_matrix(face_vander)
    face_moments = np.array(
        [
            [
                math.factorial(first[0] + second[0])
                * math.factorial(first[1] + second[1])
                / math.factorial(sum(first) + sum(second) + 2)
                for second in lattice
            ]
            for first in lattice
        ]
    )
    face_mass = face_inverse.T @ face_moments @ face_inverse
    numbers = {point: number for number, point in enumerate(points)}
    face_points = [
        [(across, along, 0) for across, along in lattice],
        [(across, 0, along) for across, along in lattice],
        [(0, across, along) for across, along in lattice],
        [(across, along, 4 - across - along) for across, along in lattice],
    ]
    face_nodes = np.array(
        [[numbers[point] for point in listing] for listing in face_points], np.int32
    )
    mass_inverse = invert_matrix(mass_matrix)
    lift_tables = []
    for face_number in range(4):
        selector = np.eye(35)[face_nodes[face_number]]
        lift_tables.append(mass_inverse @ selector.T @ face_mass)
    orderings = [(0, 1, 2), (1, 2, 0), (2, 0, 1), (1, 0, 2), (0, 2, 1), (2, 1, 0)]
    lattice_numbers = {point: number for number, point in enumerate(lattice)}
    triples = [(across, along, 4 - across - along) for across, along in lattice]
    turn_nodes = np.array(
        [
            [lattice_numbers[triple[ordering[0]], triple[ordering[1]]] for triple in triples]
            for ordering in orderings
        ],
        np.int32,
    )
    return (
        jnp.asarray(np.stack(derivs), jnp.float32),
        jnp.asarray(np.stack(lift_tables), jnp.float32),
        face_nodes,
        turn_nodes,
    )


def spatial_of(field, metric, derivs):
    reference_grads = jnp.einsum("rab,fbe->rfae", derivs, field, precision=MIX)
    rows = []
    for direction_axis in range(3):
        total = metric[0, direction_axis] * reference_grads[0]
        total = total + metric[1, direction_axis] * reference_grads[1]
        total = total + metric[2, direction_axis] * reference_grads[2]
        rows.append(total)
    return jnp.stack(rows)


def volume_term(adjoint, material, coupling, metric, derivs):
    spatial = spatial_of(adjoint, metric, derivs)
    mixing = jnp.einsum("dpfg,dfae->pgae", coupling, spatial, precision=MIX)
    return jnp.sum(material[:, None] * mixing, axis=0)


def kernel_term(adjoint, forward, coupling, metric, derivs):
    spatial = spatial_of(forward, metric, derivs)
    mixing = jnp.einsum("dpfg,dgae->pfae", coupling, spatial, precision=MIX)
    return jnp.sum(mixing * adjoint[None], axis=1)


def surface_term(jump_trace, face_material, face_normals, face_scale, coupling, lift_tables):
    weighted = face_normals[:, None, None] * jump_trace[None]
    mixing = jnp.einsum("dpfg,dfnxe->pgnxe", coupling, weighted, precision=MIX)
    face_flux = 0.5 * jnp.sum(face_material[:, None] * mixing, axis=0) + 0.5 * jump_trace
    return jnp.einsum(
        "xan,fnxe->fae", lift_tables, face_flux * face_scale[None, None], precision=MIX
    )


def halving_sum(values, axis, count):
    position = lax.axis_index(axis)
    work = values
    bit = count // 2
    while bit >= 1:
        width = work.shape[-1] // 2
        upper = (position & bit) != 0
        low = work[..., :width]
        high = work[..., width:]
        sent = lax.ppermute(
            jnp.where(upper, low, high), axis, [(i, i ^ bit) for i in range(count)]
        )
        work = jnp.where(upper, high, low) + sent
        bit //= 2
    return work


def search_direction(grad_share, step_share, change_share, gram, combine_sums):
    pairs = step_share.shape[0]
    both_share = jnp.concatenate([step_share, change_share], axis=0)
    with_grad = jnp.sum(both_share * grad_share[None], axis=(1, 2, 3))
    summed = combine_sums(jnp.concatenate([with_grad, gram.reshape(-1)]))
    lanes = 0.0 * step_share[0, 0, :8, :]
    summed = summed[:, None, None] + lanes[None]
    step_grad = summed[:pairs]
    change_grad = summed[pairs : 2 * pairs]
    gram = summed[2 * pairs :].reshape((2 * pairs, pairs) + summed.shape[1:])
    step_change = gram[:pairs]
    change_change = gram[pairs:]
    curvature = [step_change[slot, slot] for slot in range(pairs)]
    alphas = [None] * pairs
    for slot in reversed(range(pairs)):
        projected = step_grad[slot]
        for later in range(slot + 1, pairs):
            projected = projected - alphas[later] * step_change[slot, later]
        alphas[slot] = projected / curvature[slot]
    scaling = curvature[pairs - 1] / change_change[pairs - 1, pairs - 1]
    weights = [None] * pairs
    for slot in range(pairs):
        along = change_grad[slot]
        for other in range(pairs):
            along = along - alphas[other] * change_change[slot, other]
        along = scaling * along
        for earlier in range(slot):
            along = along + weights[earlier] * step_change[earlier, slot]
        beta_now = along / curvature[slot]
        weights[slot] = alphas[slot] - beta_now
    coefficients = jnp.stack(
        [weights[slot] for slot in range(pairs)]
        + [-scaling * alphas[slot] for slot in range(pairs)]
        + [scaling]
    )[:, 0, 0]
    rows = jnp.concatenate([both_share, grad_share[None]], axis=0)
    work = jnp.sum(coefficients[:, None, None, None] * rows, axis=0)
    return -work


def shards(
    adjoint_state,
    forward_states,
    material,
    coupling,
    metric,
    face_normals,
    face_scale,
    face_neighbours,
    face_orientation,
    send_faces,
    history_steps,
    history_changes,
):
    derivs, lift_tables, face_nodes, turn_nodes = basis_tables()
    fields = adjoint_state.shape[1]
    elements = adjoint_state.shape[3]
    node_count = material.shape[1]
    params = material.shape[0]
    face_width = face_nodes.shape[1]
    border = send_faces.shape[0] // 2
    slot_count = 4 * elements + 2 * border
    adjoint = adjoint_state[0]
    face_material = material[:, face_nodes.T, :]
    neighbours = face_neighbours.reshape(-1)
    orient = face_orientation.reshape(-1)
    face_total = 4 * elements
    slot_pick = (
        neighbours[None, :] == jnp.arange(slot_count, dtype=jnp.int32)[:, None]
    ).astype(jnp.float32)
    local_pick = slot_pick[:face_total]
    below_pick = slot_pick[face_total : face_total + border]
    above_pick = slot_pick[face_total + border :]
    node_turn = jnp.zeros((face_width, face_width, face_total), jnp.float32)
    for option in range(turn_nodes.shape[0]):
        node_turn = node_turn + (orient == option).astype(jnp.float32)[None, None, :] * jnp.asarray(
            np.eye(face_width, dtype=np.float32)[turn_nodes[option]].T
        )[:, :, None]
    send_pick = (
        send_faces[None, :] == jnp.arange(face_total, dtype=jnp.int32)[:, None]
    ).astype(jnp.float32)
    shot_count = lax.axis_size("shot")
    share_width = elements // shot_count
    share_start = lax.axis_index("shot") * share_width

    def own_share(rows):
        return lax.dynamic_slice_in_dim(rows, share_start, share_width, rows.ndim - 1)

    lane_pick = (
        jnp.arange(elements, dtype=jnp.int32)[:, None]
        == share_start + jnp.arange(share_width, dtype=jnp.int32)[None, :]
    ).astype(jnp.float32)
    both_share = jnp.einsum(
        "ipae,ej->ipaj",
        jnp.concatenate([history_steps, history_changes], axis=0),
        lane_pick,
        precision=MIX,
    )
    pairs = history_steps.shape[0]
    step_share = both_share[:pairs]
    change_share = both_share[pairs:]
    gram = jnp.sum(both_share[:, None] * change_share[None, :], axis=(2, 3, 4))
    gradient = jnp.zeros((params, node_count, elements), jnp.float32)
    for step_index in range(forward_states.shape[1]):
        inner_trace = adjoint[:, face_nodes.T, :]
        flat_trace = inner_trace.reshape(fields, face_width, 4 * elements)
        sent_traces = jnp.einsum("fns,sj->fnj", flat_trace, send_pick, precision=MIX)
        extended = padded(sent_traces, (("mesh", 2),), border)
        if step_index == 0:
            step_share, change_share, gram, extended = lax.optimization_barrier(
                (step_share, change_share, gram, extended)
            )
        gathered = jnp.einsum("fns,sj->fnj", flat_trace, local_pick, precision=MIX)
        gathered = gathered + jnp.einsum(
            "fns,sj->fnj", extended[:, :, :border], below_pick, precision=MIX
        )
        gathered = gathered + jnp.einsum(
            "fns,sj->fnj", extended[:, :, 3 * border :], above_pick, precision=MIX
        )
        turned = jnp.sum(gathered[:, :, None, :] * node_turn[None], axis=1)
        jump_trace = turned.reshape(fields, face_width, 4, elements) - inner_trace
        change = volume_term(adjoint, material, coupling, metric, derivs) + surface_term(
            jump_trace, face_material, face_normals, face_scale, coupling, lift_tables
        )
        adjoint = adjoint + STEP_SIZE * change
        gradient = gradient + STEP_SIZE * kernel_term(
            adjoint, forward_states[0, step_index], coupling, metric, derivs
        )
    device_count = shot_count * lax.axis_size("mesh")

    def combine_sums(values):
        spread = jnp.broadcast_to(values[None], (device_count,) + values.shape)
        return jnp.sum(lax.all_to_all(spread, ("shot", "mesh"), 0, 0, tiled=False), axis=0)

    grad_share = halving_sum(gradient, "shot", shot_count)
    result = search_direction(grad_share, step_share, change_share, gram, combine_sums)
    return (adjoint[None], result)


def solution(mesh):
    placed = (
        P("shot", None, None, "mesh"),
        P("shot", None, None, None, "mesh"),
        P(None, None, "mesh"),
        P(),
        P(None, None, "mesh"),
        P(None, None, "mesh"),
        P(None, "mesh"),
        P(None, "mesh"),
        P(None, "mesh"),
        P("mesh"),
        P(None, None, None, "mesh"),
        P(None, None, None, "mesh"),
    )
    return jax.shard_map(
        shards,
        mesh=mesh,
        in_specs=placed,
        out_specs=(P("shot", None, None, "mesh"), P(None, None, ("mesh", "shot"))),
        check_vma=False,
    )
```

```python
import math

import jax
import jax.numpy as jnp
import numpy as np
from jax import lax
from jax.sharding import PartitionSpec as P

HIGH = lax.Precision.HIGHEST
MIX = lax.Precision.HIGH
STEP_SIZE = 0.02


def padded(x, sides, width):
    for axis, dim in sides:
        devices, length = (lax.axis_size(axis), x.shape[dim])
        up = [(i, (i + 1) % devices) for i in range(devices - 1)]
        down = [(j, i) for i, j in up]
        last = lax.slice_in_dim(x, length - width, length, axis=dim)
        first = lax.slice_in_dim(x, 0, width, axis=dim)
        before = lax.ppermute(last, axis, up)
        after = lax.ppermute(first, axis, down)
        x = jnp.concatenate([before, x, after], axis=dim)
    return x


def invert_matrix(matrix):
    order_count = matrix.shape[0]
    working = np.concatenate([matrix * 1.0, np.eye(order_count)], axis=1)
    for column in range(order_count):
        pivot_row = column + int(np.argmax(np.abs(working[column:, column])))
        working[[column, pivot_row]] = working[[pivot_row, column]]
        working[column] = working[column] / working[column, column]
        for target in range(order_count):
            if target != column:
                working[target] = working[target] - working[target, column] * working[column]
    return working[:, order_count:]


def basis_tables():
    points = [
        (across, along, upward)
        for upward in range(5)
        for along in range(5 - upward)
        for across in range(5 - upward - along)
    ]
    exponents = np.array(points) * 1.0
    coords = exponents / 4.0
    vander = np.prod(coords[:, None, :] ** exponents[None, :, :], axis=2)
    inverse = invert_matrix(vander)
    derivs = []
    for direction_axis in range(3):
        lowered = np.maximum(exponents - np.eye(3)[direction_axis], 0.0)
        slopes = exponents[None, :, direction_axis] * np.prod(
            coords[:, None, :] ** lowered[None, :, :], axis=2
        )
        derivs.append(slopes @ inverse)
    moments = np.array(
        [
            [
                math.factorial(first[0] + second[0])
                * math.factorial(first[1] + second[1])
                * math.factorial(first[2] + second[2])
                / math.factorial(sum(first) + sum(second) + 3)
                for second in points
            ]
            for first in points
        ]
    )
    mass_matrix = inverse.T @ moments @ inverse
    lattice = [(across, along) for along in range(5) for across in range(5 - along)]
    lattice_powers = np.array(lattice) * 1.0
    face_vander = np.prod((lattice_powers / 4.0)[:, None, :] ** lattice_powers[None, :, :], axis=2)
    face_inverse = invert_matrix(face_vander)
    face_moments = np.array(
        [
            [
                math.factorial(first[0] + second[0])
                * math.factorial(first[1] + second[1])
                / math.factorial(sum(first) + sum(second) + 2)
                for second in lattice
            ]
            for first in lattice
        ]
    )
    face_mass = face_inverse.T @ face_moments @ face_inverse
    numbers = {point: number for number, point in enumerate(points)}
    face_points = [
        [(across, along, 0) for across, along in lattice],
        [(across, 0, along) for across, along in lattice],
        [(0, across, along) for across, along in lattice],
        [(across, along, 4 - across - along) for across, along in lattice],
    ]
    face_nodes = np.array(
        [[numbers[point] for point in listing] for listing in face_points], np.int32
    )
    mass_inverse = invert_matrix(mass_matrix)
    lift_tables = []
    for face_number in range(4):
        selector = np.eye(35)[face_nodes[face_number]]
        lift_tables.append(mass_inverse @ selector.T @ face_mass)
    orderings = [(0, 1, 2), (1, 2, 0), (2, 0, 1), (1, 0, 2), (0, 2, 1), (2, 1, 0)]
    lattice_numbers = {point: number for number, point in enumerate(lattice)}
    triples = [(across, along, 4 - across - along) for across, along in lattice]
    turn_nodes = np.array(
        [
            [lattice_numbers[triple[ordering[0]], triple[ordering[1]]] for triple in triples]
            for ordering in orderings
        ],
        np.int32,
    )
    return (
        jnp.asarray(np.stack(derivs), jnp.float32),
        jnp.asarray(np.stack(lift_tables), jnp.float32),
        face_nodes,
        turn_nodes,
    )


def spatial_of(field, metric, derivs):
    reference_grads = jnp.einsum("rab,fbe->rfae", derivs, field, precision=MIX)
    rows = []
    for direction_axis in range(3):
        total = metric[0, direction_axis] * reference_grads[0]
        total = total + metric[1, direction_axis] * reference_grads[1]
        total = total + metric[2, direction_axis] * reference_grads[2]
        rows.append(total)
    return jnp.stack(rows)


def volume_term(adjoint, material, coupling, metric, derivs):
    spatial = spatial_of(adjoint, metric, derivs)
    mixing = jnp.einsum("dpfg,dfae->pgae", coupling, spatial, precision=MIX)
    return jnp.sum(material[:, None] * mixing, axis=0)


def kernel_term(adjoint, forward, coupling, metric, derivs):
    spatial = spatial_of(forward, metric, derivs)
    mixing = jnp.einsum("dpfg,dgae->pfae", coupling, spatial, precision=MIX)
    return jnp.sum(mixing * adjoint[None], axis=1)


def surface_term(jump_trace, face_material, face_normals, face_scale, coupling, lift_tables):
    weighted = face_normals[:, None, None] * jump_trace[None]
    mixing = jnp.einsum("dpfg,dfnxe->pgnxe", coupling, weighted, precision=MIX)
    face_flux = 0.5 * jnp.sum(face_material[:, None] * mixing, axis=0) + 0.5 * jump_trace
    return jnp.einsum(
        "xan,fnxe->fae", lift_tables, face_flux * face_scale[None, None], precision=MIX
    )


def halving_sum(values, axis, count):
    position = lax.axis_index(axis)
    bits = count.bit_length() - 1
    order = [int(format(chunk, "0%db" % bits)[::-1] or "0", 2) for chunk in range(count)]
    width = values.shape[-1] // count
    work = values.reshape(values.shape[:-1] + (count, width))[..., order, :]
    work = work.reshape(values.shape)
    bit = 1
    while bit < count:
        width = work.shape[-1] // 2
        upper = (position & bit) != 0
        low = work[..., :width]
        high = work[..., width:]
        sent = lax.ppermute(
            jnp.where(upper, low, high), axis, [(i, i ^ bit) for i in range(count)]
        )
        work = jnp.where(upper, high, low) + sent
        bit *= 2
    return work


def search_direction(grad_share, step_share, change_share, gram, combine_sums):
    pairs = step_share.shape[0]
    both_share = jnp.concatenate([step_share, change_share], axis=0)
    with_grad = jnp.sum(both_share * grad_share[None], axis=(1, 2, 3))
    summed = combine_sums(jnp.concatenate([with_grad, gram.reshape(-1)]))
    lanes = 0.0 * step_share[0, 0, :8, :]
    summed = summed[:, None, None] + lanes[None]
    step_grad = summed[:pairs]
    change_grad = summed[pairs : 2 * pairs]
    gram = summed[2 * pairs :].reshape((2 * pairs, pairs) + summed.shape[1:])
    step_change = gram[:pairs]
    change_change = gram[pairs:]
    curvature = [step_change[slot, slot] for slot in range(pairs)]
    alphas = [None] * pairs
    for slot in reversed(range(pairs)):
        projected = step_grad[slot]
        for later in range(slot + 1, pairs):
            projected = projected - alphas[later] * step_change[slot, later]
        alphas[slot] = projected / curvature[slot]
    scaling = curvature[pairs - 1] / change_change[pairs - 1, pairs - 1]
    weights = [None] * pairs
    for slot in range(pairs):
        along = change_grad[slot]
        for other in range(pairs):
            along = along - alphas[other] * change_change[slot, other]
        along = scaling * along
        for earlier in range(slot):
            along = along + weights[earlier] * step_change[earlier, slot]
        beta_now = along / curvature[slot]
        weights[slot] = alphas[slot] - beta_now
    coefficients = jnp.stack(
        [weights[slot] for slot in range(pairs)]
        + [-scaling * alphas[slot] for slot in range(pairs)]
        + [scaling]
    )[:, 0, 0]
    rows = jnp.concatenate([both_share, grad_share[None]], axis=0)
    work = jnp.sum(coefficients[:, None, None, None] * rows, axis=0)
    return -work


def shards(
    adjoint_state,
    forward_states,
    material,
    coupling,
    metric,
    face_normals,
    face_scale,
    face_neighbours,
    face_orientation,
    send_faces,
    history_steps,
    history_changes,
):
    derivs, lift_tables, face_nodes, turn_nodes = basis_tables()
    fields = adjoint_state.shape[1]
    elements = adjoint_state.shape[3]
    node_count = material.shape[1]
    params = material.shape[0]
    face_width = face_nodes.shape[1]
    border = send_faces.shape[0] // 2
    slot_count = 4 * elements + 2 * border
    adjoint = adjoint_state[0]
    face_material = material[:, face_nodes.T, :]
    neighbours = face_neighbours.reshape(-1)
    orient = face_orientation.reshape(-1)
    face_total = 4 * elements
    slot_pick = (
        neighbours[None, :] == jnp.arange(slot_count, dtype=jnp.int32)[:, None]
    ).astype(jnp.float32)
    local_pick = slot_pick[:face_total]
    below_pick = slot_pick[face_total : face_total + border]
    above_pick = slot_pick[face_total + border :]
    node_turn = jnp.zeros((face_width, face_width, face_total), jnp.float32)
    for option in range(turn_nodes.shape[0]):
        node_turn = node_turn + (orient == option).astype(jnp.float32)[None, None, :] * jnp.asarray(
            np.eye(face_width, dtype=np.float32)[turn_nodes[option]].T
        )[:, :, None]
    send_pick = (
        send_faces[None, :] == jnp.arange(face_total, dtype=jnp.int32)[:, None]
    ).astype(jnp.float32)
    shot_count = lax.axis_size("shot")
    share_width = elements // shot_count
    share_start = lax.axis_index("shot") * share_width

    def own_share(rows):
        return lax.dynamic_slice_in_dim(rows, share_start, share_width, rows.ndim - 1)

    lane_pick = (
        jnp.arange(elements, dtype=jnp.int32)[:, None]
        == share_start + jnp.arange(share_width, dtype=jnp.int32)[None, :]
    ).astype(jnp.float32)
    both_share = jnp.einsum(
        "ipae,ej->ipaj",
        jnp.concatenate([history_steps, history_changes], axis=0),
        lane_pick,
        precision=MIX,
    )
    pairs = history_steps.shape[0]
    step_share = both_share[:pairs]
    change_share = both_share[pairs:]
    gram = jnp.sum(both_share[:, None] * change_share[None, :], axis=(2, 3, 4))
    gradient = jnp.zeros((params, node_count, elements), jnp.float32)
    for step_index in range(forward_states.shape[1]):
        inner_trace = adjoint[:, face_nodes.T, :]
        flat_trace = inner_trace.reshape(fields, face_width, 4 * elements)
        sent_traces = jnp.einsum("fns,sj->fnj", flat_trace, send_pick, precision=MIX)
        extended = padded(sent_traces, (("mesh", 2),), border)
        if step_index == 0:
            step_share, change_share, gram, extended = lax.optimization_barrier(
                (step_share, change_share, gram, extended)
            )
        gathered = jnp.einsum("fns,sj->fnj", flat_trace, local_pick, precision=MIX)
        gathered = gathered + jnp.einsum(
            "fns,sj->fnj", extended[:, :, :border], below_pick, precision=MIX
        )
        gathered = gathered + jnp.einsum(
            "fns,sj->fnj", extended[:, :, 3 * border :], above_pick, precision=MIX
        )
        turned = jnp.sum(gathered[:, :, None, :] * node_turn[None], axis=1)
        jump_trace = turned.reshape(fields, face_width, 4, elements) - inner_trace
        change = volume_term(adjoint, material, coupling, metric, derivs) + surface_term(
            jump_trace, face_material, face_normals, face_scale, coupling, lift_tables
        )
        adjoint = adjoint + STEP_SIZE * change
        gradient = gradient + STEP_SIZE * kernel_term(
            adjoint, forward_states[0, step_index], coupling, metric, derivs
        )
    device_count = shot_count * lax.axis_size("mesh")

    def combine_sums(values):
        spread = jnp.broadcast_to(values[None], (device_count,) + values.shape)
        return jnp.sum(lax.all_to_all(spread, ("shot", "mesh"), 0, 0, tiled=False), axis=0)

    grad_share = halving_sum(gradient, "shot", shot_count)
    result = search_direction(grad_share, step_share, change_share, gram, combine_sums)
    return (adjoint[None], result)


def solution(mesh):
    placed = (
        P("shot", None, None, "mesh"),
        P("shot", None, None, None, "mesh"),
        P(None, None, "mesh"),
        P(),
        P(None, None, "mesh"),
        P(None, None, "mesh"),
        P(None, "mesh"),
        P(None, "mesh"),
        P(None, "mesh"),
        P("mesh"),
        P(None, None, None, "mesh"),
        P(None, None, None, "mesh"),
    )
    return jax.shard_map(
        shards,
        mesh=mesh,
        in_specs=placed,
        out_specs=(P("shot", None, None, "mesh"), P(None, None, ("mesh", "shot"))),
        check_vma=False,
    )
```

```python
import math

import jax
import jax.numpy as jnp
import numpy as np
from jax import lax
from jax.sharding import PartitionSpec as P

HIGH = lax.Precision.HIGHEST
MIX = lax.Precision.HIGH
STEP_SIZE = 0.02


def padded(x, sides, width):
    for axis, dim in sides:
        devices, length = (lax.axis_size(axis), x.shape[dim])
        up = [(i, (i + 1) % devices) for i in range(devices - 1)]
        down = [(j, i) for i, j in up]
        last = lax.slice_in_dim(x, length - width, length, axis=dim)
        first = lax.slice_in_dim(x, 0, width, axis=dim)
        before = lax.ppermute(last, axis, up)
        after = lax.ppermute(first, axis, down)
        x = jnp.concatenate([before, x, after], axis=dim)
    return x


def invert_matrix(matrix):
    order_count = matrix.shape[0]
    working = np.concatenate([matrix * 1.0, np.eye(order_count)], axis=1)
    for column in range(order_count):
        pivot_row = column + int(np.argmax(np.abs(working[column:, column])))
        working[[column, pivot_row]] = working[[pivot_row, column]]
        working[column] = working[column] / working[column, column]
        for target in range(order_count):
            if target != column:
                working[target] = working[target] - working[target, column] * working[column]
    return working[:, order_count:]


def basis_tables():
    points = [
        (across, along, upward)
        for upward in range(5)
        for along in range(5 - upward)
        for across in range(5 - upward - along)
    ]
    exponents = np.array(points) * 1.0
    coords = exponents / 4.0
    vander = np.prod(coords[:, None, :] ** exponents[None, :, :], axis=2)
    inverse = invert_matrix(vander)
    derivs = []
    for direction_axis in range(3):
        lowered = np.maximum(exponents - np.eye(3)[direction_axis], 0.0)
        slopes = exponents[None, :, direction_axis] * np.prod(
            coords[:, None, :] ** lowered[None, :, :], axis=2
        )
        derivs.append(slopes @ inverse)
    moments = np.array(
        [
            [
                math.factorial(first[0] + second[0])
                * math.factorial(first[1] + second[1])
                * math.factorial(first[2] + second[2])
                / math.factorial(sum(first) + sum(second) + 3)
                for second in points
            ]
            for first in points
        ]
    )
    mass_matrix = inverse.T @ moments @ inverse
    lattice = [(across, along) for along in range(5) for across in range(5 - along)]
    lattice_powers = np.array(lattice) * 1.0
    face_vander = np.prod((lattice_powers / 4.0)[:, None, :] ** lattice_powers[None, :, :], axis=2)
    face_inverse = invert_matrix(face_vander)
    face_moments = np.array(
        [
            [
                math.factorial(first[0] + second[0])
                * math.factorial(first[1] + second[1])
                / math.factorial(sum(first) + sum(second) + 2)
                for second in lattice
            ]
            for first in lattice
        ]
    )
    face_mass = face_inverse.T @ face_moments @ face_inverse
    numbers = {point: number for number, point in enumerate(points)}
    face_points = [
        [(across, along, 0) for across, along in lattice],
        [(across, 0, along) for across, along in lattice],
        [(0, across, along) for across, along in lattice],
        [(across, along, 4 - across - along) for across, along in lattice],
    ]
    face_nodes = np.array(
        [[numbers[point] for point in listing] for listing in face_points], np.int32
    )
    mass_inverse = invert_matrix(mass_matrix)
    lift_tables = []
    for face_number in range(4):
        selector = np.eye(35)[face_nodes[face_number]]
        lift_tables.append(mass_inverse @ selector.T @ face_mass)
    orderings = [(0, 1, 2), (1, 2, 0), (2, 0, 1), (1, 0, 2), (0, 2, 1), (2, 1, 0)]
    lattice_numbers = {point: number for number, point in enumerate(lattice)}
    triples = [(across, along, 4 - across - along) for across, along in lattice]
    turn_nodes = np.array(
        [
            [lattice_numbers[triple[ordering[0]], triple[ordering[1]]] for triple in triples]
            for ordering in orderings
        ],
        np.int32,
    )
    return (
        jnp.asarray(np.stack(derivs), jnp.float32),
        jnp.asarray(np.stack(lift_tables), jnp.float32),
        face_nodes,
        turn_nodes,
    )


def spatial_of(field, metric, derivs):
    reference_grads = jnp.einsum("rab,fbe->rfae", derivs, field, precision=MIX)
    weighted = metric[:, :, None, None, :] * reference_grads[:, None]
    return weighted[0] + weighted[1] + weighted[2]


def volume_term(adjoint, material, coupling, metric, derivs):
    spatial = spatial_of(adjoint, metric, derivs)
    mixing = jnp.einsum("dpfg,dfae->pgae", coupling, spatial, precision=MIX)
    return jnp.sum(material[:, None] * mixing, axis=0)


def kernel_term(adjoint, forward, coupling, metric, derivs):
    spatial = spatial_of(forward, metric, derivs)
    mixing = jnp.einsum("dpfg,dgae->pfae", coupling, spatial, precision=MIX)
    return jnp.sum(mixing * adjoint[None], axis=1)


def surface_term(jump_trace, face_material, face_normals, face_scale, coupling, lift_tables):
    weighted = face_normals[:, None, None] * jump_trace[None]
    mixing = jnp.einsum("dpfg,dfnxe->pgnxe", coupling, weighted, precision=MIX)
    face_flux = 0.5 * jnp.sum(face_material[:, None] * mixing, axis=0) + 0.5 * jump_trace
    return jnp.einsum(
        "xan,fnxe->fae", lift_tables, face_flux * face_scale[None, None], precision=MIX
    )


def halving_sum(values, axis, count):
    position = lax.axis_index(axis)
    work = values
    bit = count // 2
    while bit >= 1:
        width = work.shape[-1] // 2
        upper = (position & bit) != 0
        low = work[..., :width]
        high = work[..., width:]
        sent = lax.ppermute(
            jnp.where(upper, low, high), axis, [(i, i ^ bit) for i in range(count)]
        )
        work = jnp.where(upper, high, low) + sent
        bit //= 2
    return work


def search_direction(grad_share, step_share, change_share, gram, combine_sums):
    pairs = step_share.shape[0]
    both_share = jnp.concatenate([step_share, change_share], axis=0)
    with_grad = jnp.sum(both_share * grad_share[None], axis=(1, 2, 3))
    summed = combine_sums(jnp.concatenate([with_grad, gram.reshape(-1)]))
    lanes = 0.0 * step_share[0, 0, :8, :]
    summed = summed[:, None, None] + lanes[None]
    step_grad = summed[:pairs]
    change_grad = summed[pairs : 2 * pairs]
    gram = summed[2 * pairs :].reshape((2 * pairs, pairs) + summed.shape[1:])
    step_change = gram[:pairs]
    change_change = gram[pairs:]
    curvature = [step_change[slot, slot] for slot in range(pairs)]
    alphas = [None] * pairs
    for slot in reversed(range(pairs)):
        projected = step_grad[slot]
        for later in range(slot + 1, pairs):
            projected = projected - alphas[later] * step_change[slot, later]
        alphas[slot] = projected / curvature[slot]
    scaling = curvature[pairs - 1] / change_change[pairs - 1, pairs - 1]
    weights = [None] * pairs
    for slot in range(pairs):
        along = change_grad[slot]
        for other in range(pairs):
            along = along - alphas[other] * change_change[slot, other]
        along = scaling * along
        for earlier in range(slot):
            along = along + weights[earlier] * step_change[earlier, slot]
        beta_now = along / curvature[slot]
        weights[slot] = alphas[slot] - beta_now
    coefficients = jnp.stack(
        [weights[slot] for slot in range(pairs)]
        + [-scaling * alphas[slot] for slot in range(pairs)]
        + [scaling]
    )[:, 0, 0]
    rows = jnp.concatenate([both_share, grad_share[None]], axis=0)
    work = jnp.sum(coefficients[:, None, None, None] * rows, axis=0)
    return -work


def shards(
    adjoint_state,
    forward_states,
    material,
    coupling,
    metric,
    face_normals,
    face_scale,
    face_neighbours,
    face_orientation,
    send_faces,
    history_steps,
    history_changes,
):
    derivs, lift_tables, face_nodes, turn_nodes = basis_tables()
    fields = adjoint_state.shape[1]
    elements = adjoint_state.shape[3]
    node_count = material.shape[1]
    params = material.shape[0]
    face_width = face_nodes.shape[1]
    border = send_faces.shape[0] // 2
    slot_count = 4 * elements + 2 * border
    adjoint = adjoint_state[0]
    face_material = material[:, face_nodes.T, :]
    neighbours = face_neighbours.reshape(-1)
    orient = face_orientation.reshape(-1)
    face_total = 4 * elements
    slot_pick = (
        neighbours[None, :] == jnp.arange(slot_count, dtype=jnp.int32)[:, None]
    ).astype(jnp.float32)
    local_pick = slot_pick[:face_total]
    below_pick = slot_pick[face_total : face_total + border]
    above_pick = slot_pick[face_total + border :]
    node_turn = jnp.zeros((face_width, face_width, face_total), jnp.float32)
    for option in range(turn_nodes.shape[0]):
        node_turn = node_turn + (orient == option).astype(jnp.float32)[None, None, :] * jnp.asarray(
            np.eye(face_width, dtype=np.float32)[turn_nodes[option]].T
        )[:, :, None]
    send_pick = (
        send_faces[None, :] == jnp.arange(face_total, dtype=jnp.int32)[:, None]
    ).astype(jnp.float32)
    shot_count = lax.axis_size("shot")
    share_width = elements // shot_count
    share_start = lax.axis_index("shot") * share_width

    def own_share(rows):
        return lax.dynamic_slice_in_dim(rows, share_start, share_width, rows.ndim - 1)

    lane_pick = (
        jnp.arange(elements, dtype=jnp.int32)[:, None]
        == share_start + jnp.arange(share_width, dtype=jnp.int32)[None, :]
    ).astype(jnp.float32)
    both_share = jnp.einsum(
        "ipae,ej->ipaj",
        jnp.concatenate([history_steps, history_changes], axis=0),
        lane_pick,
        precision=MIX,
    )
    pairs = history_steps.shape[0]
    step_share = both_share[:pairs]
    change_share = both_share[pairs:]
    gram = jnp.sum(both_share[:, None] * change_share[None, :], axis=(2, 3, 4))
    gradient = jnp.zeros((params, node_count, elements), jnp.float32)
    for step_index in range(forward_states.shape[1]):
        inner_trace = adjoint[:, face_nodes.T, :]
        flat_trace = inner_trace.reshape(fields, face_width, 4 * elements)
        sent_traces = jnp.einsum("fns,sj->fnj", flat_trace, send_pick, precision=MIX)
        extended = padded(sent_traces, (("mesh", 2),), border)
        if step_index == 0:
            step_share, change_share, gram, extended = lax.optimization_barrier(
                (step_share, change_share, gram, extended)
            )
        gathered = jnp.einsum("fns,sj->fnj", flat_trace, local_pick, precision=MIX)
        gathered = gathered + jnp.einsum(
            "fns,sj->fnj", extended[:, :, :border], below_pick, precision=MIX
        )
        gathered = gathered + jnp.einsum(
            "fns,sj->fnj", extended[:, :, 3 * border :], above_pick, precision=MIX
        )
        turned = jnp.sum(gathered[:, :, None, :] * node_turn[None], axis=1)
        jump_trace = turned.reshape(fields, face_width, 4, elements) - inner_trace
        change = volume_term(adjoint, material, coupling, metric, derivs) + surface_term(
            jump_trace, face_material, face_normals, face_scale, coupling, lift_tables
        )
        adjoint = adjoint + STEP_SIZE * change
        gradient = gradient + STEP_SIZE * kernel_term(
            adjoint, forward_states[0, step_index], coupling, metric, derivs
        )
    device_count = shot_count * lax.axis_size("mesh")

    def combine_sums(values):
        spread = jnp.broadcast_to(values[None], (device_count,) + values.shape)
        return jnp.sum(lax.all_to_all(spread, ("shot", "mesh"), 0, 0, tiled=False), axis=0)

    grad_share = halving_sum(gradient, "shot", shot_count)
    result = search_direction(grad_share, step_share, change_share, gram, combine_sums)
    return (adjoint[None], result)


def solution(mesh):
    placed = (
        P("shot", None, None, "mesh"),
        P("shot", None, None, None, "mesh"),
        P(None, None, "mesh"),
        P(),
        P(None, None, "mesh"),
        P(None, None, "mesh"),
        P(None, "mesh"),
        P(None, "mesh"),
        P(None, "mesh"),
        P("mesh"),
        P(None, None, None, "mesh"),
        P(None, None, None, "mesh"),
    )
    return jax.shard_map(
        shards,
        mesh=mesh,
        in_specs=placed,
        out_specs=(P("shot", None, None, "mesh"), P(None, None, ("mesh", "shot"))),
        check_vma=False,
    )
```

```python
import math

import jax
import jax.numpy as jnp
import numpy as np
from jax import lax
from jax.sharding import PartitionSpec as P

HIGH = lax.Precision.HIGHEST
MIX = lax.Precision.HIGH
STEP_SIZE = 0.02


def padded(x, sides, width):
    for axis, dim in sides:
        devices, length = (lax.axis_size(axis), x.shape[dim])
        up = [(i, (i + 1) % devices) for i in range(devices - 1)]
        down = [(j, i) for i, j in up]
        last = lax.slice_in_dim(x, length - width, length, axis=dim)
        first = lax.slice_in_dim(x, 0, width, axis=dim)
        before = lax.ppermute(last, axis, up)
        after = lax.ppermute(first, axis, down)
        x = jnp.concatenate([before, x, after], axis=dim)
    return x


def invert_matrix(matrix):
    order_count = matrix.shape[0]
    working = np.concatenate([matrix * 1.0, np.eye(order_count)], axis=1)
    for column in range(order_count):
        pivot_row = column + int(np.argmax(np.abs(working[column:, column])))
        working[[column, pivot_row]] = working[[pivot_row, column]]
        working[column] = working[column] / working[column, column]
        for target in range(order_count):
            if target != column:
                working[target] = working[target] - working[target, column] * working[column]
    return working[:, order_count:]


def basis_tables():
    points = [
        (across, along, upward)
        for upward in range(5)
        for along in range(5 - upward)
        for across in range(5 - upward - along)
    ]
    exponents = np.array(points) * 1.0
    coords = exponents / 4.0
    vander = np.prod(coords[:, None, :] ** exponents[None, :, :], axis=2)
    inverse = invert_matrix(vander)
    derivs = []
    for direction_axis in range(3):
        lowered = np.maximum(exponents - np.eye(3)[direction_axis], 0.0)
        slopes = exponents[None, :, direction_axis] * np.prod(
            coords[:, None, :] ** lowered[None, :, :], axis=2
        )
        derivs.append(slopes @ inverse)
    moments = np.array(
        [
            [
                math.factorial(first[0] + second[0])
                * math.factorial(first[1] + second[1])
                * math.factorial(first[2] + second[2])
                / math.factorial(sum(first) + sum(second) + 3)
                for second in points
            ]
            for first in points
        ]
    )
    mass_matrix = inverse.T @ moments @ inverse
    lattice = [(across, along) for along in range(5) for across in range(5 - along)]
    lattice_powers = np.array(lattice) * 1.0
    face_vander = np.prod((lattice_powers / 4.0)[:, None, :] ** lattice_powers[None, :, :], axis=2)
    face_inverse = invert_matrix(face_vander)
    face_moments = np.array(
        [
            [
                math.factorial(first[0] + second[0])
                * math.factorial(first[1] + second[1])
                / math.factorial(sum(first) + sum(second) + 2)
                for second in lattice
            ]
            for first in lattice
        ]
    )
    face_mass = face_inverse.T @ face_moments @ face_inverse
    numbers = {point: number for number, point in enumerate(points)}
    face_points = [
        [(across, along, 0) for across, along in lattice],
        [(across, 0, along) for across, along in lattice],
        [(0, across, along) for across, along in lattice],
        [(across, along, 4 - across - along) for across, along in lattice],
    ]
    face_nodes = np.array(
        [[numbers[point] for point in listing] for listing in face_points], np.int32
    )
    mass_inverse = invert_matrix(mass_matrix)
    lift_tables = []
    for face_number in range(4):
        selector = np.eye(35)[face_nodes[face_number]]
        lift_tables.append(mass_inverse @ selector.T @ face_mass)
    orderings = [(0, 1, 2), (1, 2, 0), (2, 0, 1), (1, 0, 2), (0, 2, 1), (2, 1, 0)]
    lattice_numbers = {point: number for number, point in enumerate(lattice)}
    triples = [(across, along, 4 - across - along) for across, along in lattice]
    turn_nodes = np.array(
        [
            [lattice_numbers[triple[ordering[0]], triple[ordering[1]]] for triple in triples]
            for ordering in orderings
        ],
        np.int32,
    )
    return (
        jnp.asarray(np.stack(derivs), jnp.float32),
        jnp.asarray(np.stack(lift_tables), jnp.float32),
        face_nodes,
        turn_nodes,
    )


def spatial_of(field, metric, derivs):
    reference_grads = jnp.einsum("rab,fbe->rfae", derivs, field, precision=MIX)
    rows = []
    for direction_axis in range(3):
        total = metric[0, direction_axis] * reference_grads[0]
        total = total + metric[1, direction_axis] * reference_grads[1]
        total = total + metric[2, direction_axis] * reference_grads[2]
        rows.append(total)
    return jnp.stack(rows)


def volume_term(adjoint, material, coupling, metric, derivs):
    spatial = spatial_of(adjoint, metric, derivs)
    mixing = jnp.einsum("dpfg,dfae->pgae", coupling, spatial, precision=MIX)
    return jnp.sum(material[:, None] * mixing, axis=0)


def kernel_term(adjoint, forward, coupling, metric, derivs):
    spatial = spatial_of(forward, metric, derivs)
    mixing = jnp.einsum("dpfg,dgae->pfae", coupling, spatial, precision=MIX)
    return jnp.sum(mixing * adjoint[None], axis=1)


def surface_term(jump_trace, face_material, face_normals, face_scale, coupling, lift_tables):
    weighted = face_normals[:, None, None] * jump_trace[None]
    mixing = jnp.einsum("dpfg,dfnxe->pgnxe", coupling, weighted, precision=MIX)
    face_flux = 0.5 * jnp.sum(face_material[:, None] * mixing, axis=0) + 0.5 * jump_trace
    return jnp.einsum(
        "xan,fnxe->fae", lift_tables, face_flux * face_scale[None, None], precision=MIX
    )


def halving_round(work, axis, count, bit):
    position = lax.axis_index(axis)
    width = work.shape[-1] // 2
    upper = (position & bit) != 0
    low = work[..., :width]
    high = work[..., width:]
    sent = lax.ppermute(jnp.where(upper, low, high), axis, [(i, i ^ bit) for i in range(count)])
    return jnp.where(upper, high, low) + sent


def search_direction(grad_share, with_grad, step_share, change_share, gram, combine_sums):
    pairs = step_share.shape[0]
    both_share = jnp.concatenate([step_share, change_share], axis=0)
    summed = combine_sums(jnp.concatenate([with_grad, gram.reshape(-1)]))
    lanes = 0.0 * step_share[0, 0, :8, :]
    summed = summed[:, None, None] + lanes[None]
    step_grad = summed[:pairs]
    change_grad = summed[pairs : 2 * pairs]
    gram = summed[2 * pairs :].reshape((2 * pairs, pairs) + summed.shape[1:])
    step_change = gram[:pairs]
    change_change = gram[pairs:]
    curvature = [step_change[slot, slot] for slot in range(pairs)]
    alphas = [None] * pairs
    for slot in reversed(range(pairs)):
        projected = step_grad[slot]
        for later in range(slot + 1, pairs):
            projected = projected - alphas[later] * step_change[slot, later]
        alphas[slot] = projected / curvature[slot]
    scaling = curvature[pairs - 1] / change_change[pairs - 1, pairs - 1]
    weights = [None] * pairs
    for slot in range(pairs):
        along = change_grad[slot]
        for other in range(pairs):
            along = along - alphas[other] * change_change[slot, other]
        along = scaling * along
        for earlier in range(slot):
            along = along + weights[earlier] * step_change[earlier, slot]
        beta_now = along / curvature[slot]
        weights[slot] = alphas[slot] - beta_now
    coefficients = jnp.stack(
        [weights[slot] for slot in range(pairs)]
        + [-scaling * alphas[slot] for slot in range(pairs)]
        + [scaling]
    )[:, 0, 0]
    rows = jnp.concatenate([both_share, grad_share[None]], axis=0)
    work = jnp.sum(coefficients[:, None, None, None] * rows, axis=0)
    return -work


def shards(
    adjoint_state,
    forward_states,
    material,
    coupling,
    metric,
    face_normals,
    face_scale,
    face_neighbours,
    face_orientation,
    send_faces,
    history_steps,
    history_changes,
):
    derivs, lift_tables, face_nodes, turn_nodes = basis_tables()
    fields = adjoint_state.shape[1]
    elements = adjoint_state.shape[3]
    node_count = material.shape[1]
    params = material.shape[0]
    face_width = face_nodes.shape[1]
    border = send_faces.shape[0] // 2
    slot_count = 4 * elements + 2 * border
    adjoint = adjoint_state[0]
    face_material = material[:, face_nodes.T, :]
    neighbours = face_neighbours.reshape(-1)
    orient = face_orientation.reshape(-1)
    face_total = 4 * elements
    slot_pick = (
        neighbours[None, :] == jnp.arange(slot_count, dtype=jnp.int32)[:, None]
    ).astype(jnp.float32)
    local_pick = slot_pick[:face_total]
    below_pick = slot_pick[face_total : face_total + border]
    above_pick = slot_pick[face_total + border :]
    node_turn = jnp.zeros((face_width, face_width, face_total), jnp.float32)
    for option in range(turn_nodes.shape[0]):
        node_turn = node_turn + (orient == option).astype(jnp.float32)[None, None, :] * jnp.asarray(
            np.eye(face_width, dtype=np.float32)[turn_nodes[option]].T
        )[:, :, None]
    send_pick = (
        send_faces[None, :] == jnp.arange(face_total, dtype=jnp.int32)[:, None]
    ).astype(jnp.float32)
    shot_count = lax.axis_size("shot")
    share_width = elements // shot_count
    share_start = lax.axis_index("shot") * share_width

    def own_share(rows):
        return lax.dynamic_slice_in_dim(rows, share_start, share_width, rows.ndim - 1)

    lane_pick = (
        jnp.arange(elements, dtype=jnp.int32)[:, None]
        == share_start + jnp.arange(share_width, dtype=jnp.int32)[None, :]
    ).astype(jnp.float32)
    both_share = jnp.einsum(
        "ipae,ej->ipaj",
        jnp.concatenate([history_steps, history_changes], axis=0),
        lane_pick,
        precision=MIX,
    )
    pairs = history_steps.shape[0]
    step_share = both_share[:pairs]
    change_share = both_share[pairs:]
    gram = jnp.sum(both_share[:, None] * change_share[None, :], axis=(2, 3, 4))
    half_width = elements // 2
    half_bit = shot_count // 2
    half_start = ((lax.axis_index("shot") & half_bit) != 0).astype(jnp.int32) * half_width
    half_pick = (
        jnp.arange(elements, dtype=jnp.int32)[:, None]
        == half_start + jnp.arange(half_width, dtype=jnp.int32)[None, :]
    ).astype(jnp.float32)
    both_half = jnp.einsum(
        "ipae,ej->ipaj",
        jnp.concatenate([history_steps, history_changes], axis=0),
        half_pick,
        precision=MIX,
    )
    gradient = jnp.zeros((params, node_count, elements), jnp.float32)
    for step_index in range(forward_states.shape[1]):
        inner_trace = adjoint[:, face_nodes.T, :]
        flat_trace = inner_trace.reshape(fields, face_width, 4 * elements)
        sent_traces = jnp.einsum("fns,sj->fnj", flat_trace, send_pick, precision=MIX)
        extended = padded(sent_traces, (("mesh", 2),), border)
        if step_index == 0:
            step_share, change_share, gram, both_half, extended = lax.optimization_barrier(
                (step_share, change_share, gram, both_half, extended)
            )
        gathered = jnp.einsum("fns,sj->fnj", flat_trace, local_pick, precision=MIX)
        gathered = gathered + jnp.einsum(
            "fns,sj->fnj", extended[:, :, :border], below_pick, precision=MIX
        )
        gathered = gathered + jnp.einsum(
            "fns,sj->fnj", extended[:, :, 3 * border :], above_pick, precision=MIX
        )
        turned = jnp.sum(gathered[:, :, None, :] * node_turn[None], axis=1)
        jump_trace = turned.reshape(fields, face_width, 4, elements) - inner_trace
        change = volume_term(adjoint, material, coupling, metric, derivs) + surface_term(
            jump_trace, face_material, face_normals, face_scale, coupling, lift_tables
        )
        adjoint = adjoint + STEP_SIZE * change
        gradient = gradient + STEP_SIZE * kernel_term(
            adjoint, forward_states[0, step_index], coupling, metric, derivs
        )
    device_count = shot_count * lax.axis_size("mesh")

    def combine_sums(values):
        spread = jnp.broadcast_to(values[None], (device_count,) + values.shape)
        return jnp.sum(lax.all_to_all(spread, ("shot", "mesh"), 0, 0, tiled=False), axis=0)

    grad_half = halving_round(gradient, "shot", shot_count, half_bit)
    with_grad = jnp.sum(both_half * grad_half[None], axis=(1, 2, 3))
    grad_share = grad_half
    bit = half_bit // 2
    while bit >= 1:
        grad_share = halving_round(grad_share, "shot", shot_count, bit)
        bit //= 2
    result = search_direction(grad_share, with_grad, step_share, change_share, gram, combine_sums)
    return (adjoint[None], result)


def solution(mesh):
    placed = (
        P("shot", None, None, "mesh"),
        P("shot", None, None, None, "mesh"),
        P(None, None, "mesh"),
        P(),
        P(None, None, "mesh"),
        P(None, None, "mesh"),
        P(None, "mesh"),
        P(None, "mesh"),
        P(None, "mesh"),
        P("mesh"),
        P(None, None, None, "mesh"),
        P(None, None, None, "mesh"),
    )
    return jax.shard_map(
        shards,
        mesh=mesh,
        in_specs=placed,
        out_specs=(P("shot", None, None, "mesh"), P(None, None, ("mesh", "shot"))),
        check_vma=False,
    )
```
